32 devices in a mesh: groups: 2 (over x), heads: 8 (over z, y), tp: 2 (over core).
Axes of the slice: x: 2, y: 2, z: 4, core: 2. Of those that a mesh axis runs over, the one named last changes fastest.
Arguments:
- query_span: bfloat16 [32, 128, 16, 256], P(('groups', 'heads'), None, 'tp'), parts along dimension 0, may hold values from -6 to 6
- key_span: bfloat16 [32, 128, 16, 256], P(('groups', 'heads'), None, 'tp'), parts along dimension 0, may hold values from -6 to 6
- value_span: bfloat16 [32, 128, 16, 512], P(('groups', 'heads'), None, 'tp'), parts along dimension 0, may hold values from -6 to 6
- prior_state: bfloat16 [32, 16, 256, 512], P(('groups', 'heads'), 'tp'), parts along dimension 0, may hold values from -0.59765625 to 0.59765625
- decay_rates: float32 [16], replicated, may hold values from 0.001 to 0.05
- prompt_lengths: int32 [32], P('groups'), parts along dimension 0, may hold values from 1024 to 4095
- decode_inputs: bfloat16 [4, 32, 4096], P(None, 'groups'), parts along dimension 1, may hold values from -6 to 6
- w_query: bfloat16 [4096, 2, 8, 256], P(None, 'tp', 'heads'), may hold values from -0.09375 to 0.09375
- w_key: bfloat16 [4096, 2, 8, 256], P(None, 'tp', 'heads'), may hold values from -0.09375 to 0.09375
- w_value: bfloat16 [4096, 2, 8, 8, 64], P(None, 'tp', None, 'heads'), may hold values from -0.09375 to 0.09375
- w_gate: bfloat16 [4096, 2, 8, 8, 64], P(None, 'tp', None, 'heads'), may hold values from -0.09375 to 0.09375
- w_out: bfloat16 [2, 8, 8, 64, 4096], P('tp', None, 'heads'), may hold values from -0.09375 to 0.09375
Outputs:
- prefill_out: bfloat16 [32, 128, 16, 512], P(('groups', 'heads'), None, 'tp'), parts along dimension 0
- decode_out: bfloat16 [4, 32, 4096], P(None, 'groups', ('heads', 'tp')), parts along dimension 1
The draws below stay inside these ranges and needn't reach their ends.
There are 2 independent parts, one for each index of `groups`. The reference program is written for one: setup_inputs(seed, part) draws one part's arguments, and reference() takes and returns one part's arrays. A program takes and returns all parts, laid end to end along the dimension named above; an argument that names none is the same for every part. Nothing has to cross between parts.
All inputs are finite; a program needn't handle non-finite values.
Results may differ from the reference program's by a relative error of at most 0.0083.
Values may be sent and summed in bfloat16 or wider, within the bound.
No kernel may reach another device: no remote copies, remote signals or barrier semaphores. Data moves between devices by JAX's collectives and lax.ppermute only.
A program may use at most 128 MiB of HBM per device.

```python
import math
import jax
import jax.numpy as jnp
from jax import lax

D = 4096
H = 16
K = 256
V = 512
C = 128
STEPS = 4
B = 16
HP = 8
KP = 256
VS = 64
N_HEADS = 8
N_TP = 2


def place_ends(array, rng, low, high):
    dims = array.shape
    index_at = [jax.random.randint(jax.random.fold_in(rng, axis), (), 0, dims[axis]) for axis in range(len(dims))]
    array = array.at[tuple(index_at)].set(low)
    longest = dims.index(max(dims))
    index_at[longest] = (index_at[longest] + 1) % dims[longest]
    return array.at[tuple(index_at)].set(high)


def spiked(drawn, key, source, target, blocks, factor):
    def block_of(position):
        return (jnp.arange(drawn.shape[position]) // (drawn.shape[position] // blocks)).reshape((-1,) + (1,) * (drawn.ndim - 1 - position))

    near = jax.random.permutation(key, blocks)[block_of(target)]
    far = (block_of(target) + blocks // 2) % blocks
    return jnp.where((block_of(source) == near) | (block_of(source) == far), factor * drawn, drawn)


def block_levels(own_key, shape, pieces, smallest, top_value):
    gain, own = 1.0, jax.random.fold_in(own_key, 6)
    for dim, blocks in pieces:
        steps = jnp.exp(jax.random.uniform(jax.random.fold_in(own, dim), (blocks,), jnp.float32, smallest / len(pieces), top_value / len(pieces)))
        gain = gain * jnp.repeat(steps, shape[dim] // blocks).reshape([-1 if axis == dim else 1 for axis in range(len(shape))])
    return gain


def centred(rng, extent, scale, bound, split=(), held_as=jnp.bfloat16):
    entries = scale * jax.random.normal(rng, extent, jnp.float32)
    if split:
        entries = entries * block_levels(rng, extent, split, -0.22, 0.18)
    return jnp.clip(entries, -bound, bound).astype(held_as)


def bell_draw_with(stream_key, shape, width, bound, pieces, heavy, kind=jnp.bfloat16):
    result = width * jax.random.normal(stream_key, shape, jnp.float32)
    if pieces:
        result = result * block_levels(stream_key, shape, pieces, -0.22, 0.18)
    return jnp.clip(spiked(result, jax.random.fold_in(stream_key, 3), *heavy), -bound, bound).astype(kind)


def setup_inputs(seed: int = 0, part: int = 0) -> dict:
    seeds = jax.random.split(jax.random.key(seed), 13)
    part_splits = jax.random.split(jax.random.fold_in(seeds[12], part), 13)
    query_span = centred(part_splits[0], (B, C, H, K), 1.0, 6.0, ((0, 8), (2, 2)))
    key_span = centred(part_splits[1], (B, C, H, K), 1.0, 6.0, ((0, 8), (2, 2)))
    value_span = centred(part_splits[2], (B, C, H, V), 1.0, 6.0, ((0, 8), (2, 2)))
    prior_state = centred(part_splits[3], (B, H, K, V), 0.1, 0.59765625, ((0, 8), (1, 2)))
    decay_rates = jnp.clip(jnp.exp(jax.random.uniform(seeds[4], (H,), jnp.float32, math.log(0.001), math.log(0.05))), 0.001, 0.05)
    prompt_lengths = place_ends(jax.random.randint(part_splits[5], (B,), 8 * C, 32 * C), jax.random.fold_in(part_splits[5], 1), 8 * C, (32 * C) - 1).astype(jnp.int32)
    decode_inputs = centred(part_splits[6], (STEPS, B, D), 1.0, 6.0)
    w_query = centred(seeds[7], (D, N_TP, N_HEADS, KP), D ** -0.5, 0.09375, ((1, 2), (2, 8)))
    w_key = centred(seeds[8], (D, N_TP, N_HEADS, KP), D ** -0.5, 0.09375, ((1, 2), (2, 8)))
    w_value = centred(seeds[9], (D, N_TP, HP, N_HEADS, VS), D ** -0.5, 0.09375, ((1, 2), (3, 8)))
    w_gate = centred(seeds[10], (D, N_TP, HP, N_HEADS, VS), D ** -0.5, 0.09375, ((1, 2), (3, 8)))
    w_out = bell_draw_with(seeds[11], (N_TP, HP, N_HEADS, VS, D), (H * V) ** -0.5, 0.09375, ((0, 2), (2, 8)), (2, 4, 8, 2.0))
    return {"query_span": query_span, "key_span": key_span, "value_span": value_span, "prior_state": prior_state, "decay_rates": decay_rates, "prompt_lengths": prompt_lengths, "decode_inputs": decode_inputs, "w_query": w_query, "w_key": w_key, "w_value": w_value, "w_gate": w_gate, "w_out": w_out}


EPSILON = 1e-05

def rotate(values, positions):
    halfway = values.shape[-1] // 2
    frequency = 10000.0 ** (-jnp.arange(halfway).astype(jnp.float32) / halfway)
    angles = positions[..., None] * frequency
    cosine = jnp.cos(angles)
    sine_part = jnp.sin(angles)
    paired = values.reshape(values.shape[:-1] + (halfway, 2))
    even_part = paired[..., 0]
    odd_part = paired[..., 1]
    turned = jnp.stack([even_part * cosine - odd_part * sine_part, odd_part * cosine + even_part * sine_part], -1)
    return turned.reshape(values.shape)

def group_norm(output):
    mean_value = lax.optimization_barrier(jnp.mean(output, -1, keepdims=True))
    mean_square = lax.optimization_barrier(jnp.mean(output * output, -1, keepdims=True))
    return (output - mean_value) * lax.rsqrt(mean_square - mean_value * mean_value + EPSILON)

def reference(query_span, key_span, value_span, prior_state, decay_rates, prompt_lengths, decode_inputs, w_query, w_key, w_value, w_gate, w_out):
    prior_wide = prior_state.astype(jnp.float32)
    span_start = C * ((prompt_lengths - 1) // C)
    live_count = prompt_lengths - span_start
    offsets = jnp.arange(C).astype(jnp.int32)
    positions = (span_start[:, None] + offsets[None, :]).astype(jnp.float32)
    queries = rotate(query_span.astype(jnp.float32), positions[:, :, None]).astype(jnp.bfloat16)
    keys = (rotate(key_span.astype(jnp.float32), positions[:, :, None]) * K ** (-0.5)).astype(jnp.bfloat16)
    valid_rows = offsets[None, :] < live_count[:, None]
    distance = (offsets[:, None] - offsets[None, :]).astype(jnp.float32)
    decay_table = jnp.where(distance[None] >= 0, jnp.exp(-decay_rates[:, None, None] * jnp.maximum(distance, 0.0)[None]), 0.0)
    scores = jnp.einsum('bihk,bjhk->bhij', queries.astype(jnp.float32), keys.astype(jnp.float32))
    weights = jnp.where(valid_rows[:, None, None, :], scores * decay_table[None], 0.0).astype(jnp.bfloat16)
    inner_sum = jnp.einsum('bhij,bjhv->bihv', weights.astype(jnp.float32), value_span.astype(jnp.float32))
    carried = jnp.einsum('bihk,bhkv->bihv', queries.astype(jnp.float32), prior_wide)
    lead_decay = jnp.exp(-decay_rates[None, :] * (offsets[:, None] + 1).astype(jnp.float32))
    mixed = inner_sum + lead_decay[None, :, :, None] * carried
    prefill_out = jnp.where(valid_rows[:, :, None, None], group_norm(mixed), 0.0).astype(jnp.bfloat16)
    remaining = (live_count[:, None] - 1 - offsets[None, :]).astype(jnp.float32)
    key_weight = jnp.where(valid_rows[:, :, None], jnp.exp(-decay_rates[None, None, :] * jnp.maximum(remaining, 0.0)[:, :, None]), 0.0)
    weighted = (keys.astype(jnp.float32) * key_weight[..., None]).astype(jnp.bfloat16)
    update = jnp.einsum('bjhk,bjhv->bhkv', weighted.astype(jnp.float32), value_span.astype(jnp.float32))
    kept_share = jnp.exp(-decay_rates[None, :] * live_count[:, None].astype(jnp.float32))
    state_short = (kept_share[:, :, None, None] * prior_wide + update).astype(jnp.bfloat16)
    state_now = lax.optimization_barrier(state_short).astype(jnp.float32)
    flat_inputs = decode_inputs.reshape(STEPS * B, D)
    query_dec = jnp.dot(flat_inputs, w_query.reshape(D, H * K), preferred_element_type=jnp.float32).astype(jnp.bfloat16).reshape(STEPS, B, H, K)
    key_dec = jnp.dot(flat_inputs, w_key.reshape(D, H * K), preferred_element_type=jnp.float32).astype(jnp.bfloat16).reshape(STEPS, B, H, K)
    value_dec = jnp.dot(flat_inputs, w_value.reshape(D, H * V), preferred_element_type=jnp.float32).astype(jnp.bfloat16).reshape(STEPS, B, H, V)
    gate_values = jnp.dot(flat_inputs, w_gate.reshape(D, H * V), preferred_element_type=jnp.float32).reshape(STEPS, B, H, V)
    dec_positions = (prompt_lengths[None, :] + jnp.arange(STEPS).astype(jnp.int32)[:, None]).astype(jnp.float32)
    query_rot = rotate(query_dec.astype(jnp.float32), dec_positions[:, :, None]).astype(jnp.bfloat16)
    key_rot = (rotate(key_dec.astype(jnp.float32), dec_positions[:, :, None]) * K ** (-0.5)).astype(jnp.bfloat16)
    retain = jnp.exp(-decay_rates)[None, :, None, None]
    outputs = []
    for step_index in range(STEPS):
        state_now = retain * state_now + key_rot[step_index].astype(jnp.float32)[:, :, :, None] * value_dec[step_index].astype(jnp.float32)[:, :, None, :]
        outputs.append(jnp.einsum('bhk,bhkv->bhv', query_rot[step_index].astype(jnp.float32), state_now, precision=lax.Precision.HIGHEST))
    readout = jnp.stack(outputs)
    activated = (jax.nn.silu(gate_values) * group_norm(readout)).astype(jnp.bfloat16).reshape(STEPS * B, H * V)
    decode_out = jnp.dot(activated, w_out.reshape(H * V, D), preferred_element_type=jnp.float32).astype(jnp.bfloat16).reshape(STEPS, B, D)
    return (prefill_out, decode_out)
```

```python
import jax
import jax.numpy as jnp
from jax import lax
from jax.sharding import PartitionSpec as P

EPSILON = 1e-05


def rotate(values, positions):
    halfway = values.shape[-1] // 2
    frequency = 10000.0 ** (-jnp.arange(halfway).astype(jnp.float32) / halfway)
    angles = positions[..., None] * frequency
    cosine = jnp.cos(angles)
    sine_part = jnp.sin(angles)
    paired = values.reshape(values.shape[:-1] + (halfway, 2))
    even_part = paired[..., 0]
    odd_part = paired[..., 1]
    turned = jnp.stack(
        [even_part * cosine - odd_part * sine_part, odd_part * cosine + even_part * sine_part], -1
    )
    return turned.reshape(values.shape)


def norm_with(output, mean_value, mean_square):
    return (output - mean_value) * lax.rsqrt(mean_square - mean_value * mean_value + EPSILON)


def per_device(
    query_span,
    key_span,
    value_span,
    prior_state,
    decay_rates,
    prompt_lengths,
    decode_inputs,
    w_query,
    w_key,
    w_value,
    w_gate,
    w_out,
):
    prompts_here, span_len, heads_here, key_width = query_span.shape
    value_width = value_span.shape[3]
    model_width = decode_inputs.shape[2]
    step_total = decode_inputs.shape[0]
    head_slots = lax.axis_size("heads")
    total_prompts = prompts_here * head_slots
    key_piece = w_query.shape[3]
    value_slice = w_value.shape[4]
    tp_index = lax.axis_index("tp")
    slot_index = lax.axis_index("heads")
    local_rates = lax.dynamic_slice_in_dim(decay_rates, tp_index * heads_here, heads_here)
    local_lengths = lax.dynamic_slice_in_dim(
        prompt_lengths, slot_index * prompts_here, prompts_here
    )
    span_start = span_len * ((local_lengths - 1) // span_len)
    live_count = local_lengths - span_start
    offsets = jnp.arange(span_len)
    positions = (span_start[:, None] + offsets[None, :]).astype(jnp.float32)
    queries = rotate(query_span.astype(jnp.float32), positions[:, :, None]).astype(jnp.bfloat16)
    keys = (
        rotate(key_span.astype(jnp.float32), positions[:, :, None]) * key_width ** (-0.5)
    ).astype(jnp.bfloat16)
    valid_rows = offsets[None, :] < live_count[:, None]
    distance = (offsets[:, None] - offsets[None, :]).astype(jnp.float32)
    decay_table = jnp.where(
        distance[None] >= 0,
        jnp.exp(-local_rates[:, None, None] * jnp.maximum(distance, 0.0)[None]),
        0.0,
    )
    scores = jnp.einsum("bihk,bjhk->bhij", queries, keys, preferred_element_type=jnp.float32)
    weights = jnp.where(valid_rows[:, None, None, :], scores * decay_table[None], 0.0).astype(
        jnp.bfloat16
    )
    inner_sum = jnp.einsum(
        "bhij,bjhv->bihv", weights, value_span, preferred_element_type=jnp.float32
    )
    carried = jnp.einsum(
        "bihk,bhkv->bihv", queries, prior_state, preferred_element_type=jnp.float32
    )
    lead_decay = jnp.exp(-local_rates[None, :] * (offsets[:, None] + 1).astype(jnp.float32))
    mixed = inner_sum + lead_decay[None, :, :, None] * carried
    mean_value = jnp.mean(mixed, -1, keepdims=True)
    mean_square = jnp.mean(mixed * mixed, -1, keepdims=True)
    prefill_out = jnp.where(
        valid_rows[:, :, None, None], norm_with(mixed, mean_value, mean_square), 0.0
    ).astype(jnp.bfloat16)
    remaining = (live_count[:, None] - 1 - offsets[None, :]).astype(jnp.float32)
    key_weight = jnp.where(
        valid_rows[:, :, None],
        jnp.exp(-local_rates[None, None, :] * jnp.maximum(remaining, 0.0)[:, :, None]),
        0.0,
    )
    weighted = (keys.astype(jnp.float32) * key_weight[..., None]).astype(jnp.bfloat16)
    update = jnp.einsum("bjhk,bjhv->bhkv", weighted, value_span, preferred_element_type=jnp.float32)
    kept_share = jnp.exp(-local_rates[None, :] * live_count[:, None].astype(jnp.float32))
    state_new = (kept_share[:, :, None, None] * prior_state.astype(jnp.float32) + update).astype(
        jnp.bfloat16
    )
    slots = head_slots
    flat_inputs = decode_inputs.reshape(step_total * total_prompts, model_width)
    query_part = jnp.dot(
        flat_inputs, w_query.reshape(model_width, key_piece), preferred_element_type=jnp.float32
    ).astype(jnp.bfloat16)
    key_part = jnp.dot(
        flat_inputs, w_key.reshape(model_width, key_piece), preferred_element_type=jnp.float32
    ).astype(jnp.bfloat16)
    value_dec = jnp.dot(
        flat_inputs,
        w_value.reshape(model_width, heads_here * value_slice),
        preferred_element_type=jnp.float32,
    ).astype(jnp.bfloat16)
    gate_values = jnp.dot(
        flat_inputs,
        w_gate.reshape(model_width, heads_here * value_slice),
        preferred_element_type=jnp.float32,
    )
    packed = jnp.concatenate([query_part, key_part, value_dec], -1)
    packed = packed.reshape(step_total, slots, prompts_here, -1).transpose(1, 0, 2, 3)
    arrived = lax.all_to_all(packed, "heads", 0, 0, tiled=True)
    query_own = (
        arrived[..., :key_piece]
        .transpose(1, 2, 0, 3)
        .reshape(step_total, prompts_here, heads_here, key_width)
    )
    key_own = (
        arrived[..., key_piece : 2 * key_piece]
        .transpose(1, 2, 0, 3)
        .reshape(step_total, prompts_here, heads_here, key_width)
    )
    value_own = (
        arrived[..., 2 * key_piece :]
        .reshape(slots, step_total, prompts_here, heads_here, value_slice)
        .transpose(1, 2, 3, 0, 4)
        .reshape(step_total, prompts_here, heads_here, value_width)
    )
    steps = jnp.arange(step_total)
    dec_positions = (local_lengths[None, :] + steps[:, None]).astype(jnp.float32)
    query_rot = rotate(query_own.astype(jnp.float32), dec_positions[:, :, None]).astype(
        jnp.bfloat16
    )
    key_rot = (
        rotate(key_own.astype(jnp.float32), dec_positions[:, :, None]) * key_width ** (-0.5)
    ).astype(jnp.bfloat16)
    from_state = jnp.einsum(
        "tbhk,bhkv->tbhv", query_rot, state_new, preferred_element_type=jnp.float32
    )
    step_gap = (steps[:, None] - steps[None, :]).astype(jnp.float32)
    step_decay = jnp.where(
        step_gap[None] >= 0,
        jnp.exp(-local_rates[:, None, None] * jnp.maximum(step_gap, 0.0)[None]),
        0.0,
    )
    step_scores = jnp.einsum(
        "tbhk,ubhk->bhtu", query_rot, key_rot, preferred_element_type=jnp.float32
    )
    from_steps = jnp.einsum(
        "bhtu,ubhv->tbhv",
        step_scores * step_decay[None],
        value_own.astype(jnp.float32),
        precision=lax.Precision.HIGHEST,
    )
    state_decay = jnp.exp(-local_rates[None, :] * (steps[:, None] + 1).astype(jnp.float32))
    readout = state_decay[:, None, :, None] * from_state + from_steps
    read_mean = jnp.mean(readout, -1, keepdims=True)
    read_square = jnp.mean(readout * readout, -1, keepdims=True)
    normed = norm_with(readout, read_mean, read_square)
    normed = normed.reshape(step_total, prompts_here, heads_here, slots, value_slice)
    normed = normed.transpose(3, 0, 1, 2, 4)
    normed = lax.all_to_all(normed, "heads", 0, 0, tiled=True)
    normed = normed.transpose(1, 0, 2, 3, 4).reshape(
        step_total, total_prompts, heads_here, value_slice
    )
    gates_steps = gate_values.reshape(step_total, total_prompts, heads_here, value_slice)
    activated = (
        (jax.nn.silu(gates_steps) * normed)
        .astype(jnp.bfloat16)
        .reshape(-1, heads_here * value_slice)
    )
    partial_out = jnp.dot(
        activated,
        w_out.reshape(heads_here * value_slice, model_width),
        preferred_element_type=jnp.float32,
    )
    partial_out = partial_out.reshape(step_total, total_prompts, model_width)
    summed = lax.psum_scatter(partial_out, ("heads", "tp"), scatter_dimension=2, tiled=True)
    decode_out = summed.astype(jnp.bfloat16)
    return (prefill_out, decode_out)


def solution(mesh):
    placed = (
        P(("groups", "heads"), None, "tp", None),
        P(("groups", "heads"), None, "tp", None),
        P(("groups", "heads"), None, "tp", None),
        P(("groups", "heads"), "tp", None, None),
        P(),
        P("groups"),
        P(None, "groups", None),
        P(None, "tp", "heads", None),
        P(None, "tp", "heads", None),
        P(None, "tp", None, "heads", None),
        P(None, "tp", None, "heads", None),
        P("tp", None, "heads", None, None),
    )
    return jax.shard_map(
        per_device,
        mesh=mesh,
        in_specs=placed,
        out_specs=(P(("groups", "heads"), None, "tp", None), P(None, "groups", ("heads", "tp"))),
        check_vma=False,
    )
```

```python
import jax
import jax.numpy as jnp
from jax import lax
from jax.sharding import PartitionSpec as P

EPSILON = 1e-05


def rotate(values, positions):
    halfway = values.shape[-1] // 2
    frequency = 10000.0 ** (-jnp.arange(halfway).astype(jnp.float32) / halfway)
    angles = positions[..., None] * frequency
    cosine = jnp.cos(angles)
    sine_part = jnp.sin(angles)
    paired = values.reshape(values.shape[:-1] + (halfway, 2))
    even_part = paired[..., 0]
    odd_part = paired[..., 1]
    turned = jnp.stack(
        [even_part * cosine - odd_part * sine_part, odd_part * cosine + even_part * sine_part], -1
    )
    return turned.reshape(values.shape)


def norm_with(output, mean_value, mean_square):
    return (output - mean_value) * lax.rsqrt(mean_square - mean_value * mean_value + EPSILON)


def per_device(
    query_span,
    key_span,
    value_span,
    prior_state,
    decay_rates,
    prompt_lengths,
    decode_inputs,
    w_query,
    w_key,
    w_value,
    w_gate,
    w_out,
):
    prompts_here, span_len, heads_here, key_width = query_span.shape
    value_width = value_span.shape[3]
    model_width = decode_inputs.shape[2]
    step_total = decode_inputs.shape[0]
    head_slots = lax.axis_size("heads")
    total_prompts = prompts_here * head_slots
    key_piece = w_query.shape[3]
    value_slice = w_value.shape[4]
    tp_index = lax.axis_index("tp")
    slot_index = lax.axis_index("heads")
    local_rates = lax.dynamic_slice_in_dim(decay_rates, tp_index * heads_here, heads_here)
    local_lengths = lax.dynamic_slice_in_dim(
        prompt_lengths, slot_index * prompts_here, prompts_here
    )
    span_start = span_len * ((local_lengths - 1) // span_len)
    live_count = local_lengths - span_start
    offsets = jnp.arange(span_len)
    positions = (span_start[:, None] + offsets[None, :]).astype(jnp.float32)
    queries = rotate(query_span.astype(jnp.float32), positions[:, :, None]).astype(jnp.bfloat16)
    keys = (
        rotate(key_span.astype(jnp.float32), positions[:, :, None]) * key_width ** (-0.5)
    ).astype(jnp.bfloat16)
    valid_rows = offsets[None, :] < live_count[:, None]
    distance = (offsets[:, None] - offsets[None, :]).astype(jnp.float32)
    decay_table = jnp.where(
        distance[None] >= 0,
        jnp.exp(-local_rates[:, None, None] * jnp.maximum(distance, 0.0)[None]),
        0.0,
    )
    remaining = (live_count[:, None] - 1 - offsets[None, :]).astype(jnp.float32)
    key_weight = jnp.where(
        valid_rows[:, :, None],
        jnp.exp(-local_rates[None, None, :] * jnp.maximum(remaining, 0.0)[:, :, None]),
        0.0,
    )
    weighted = (keys.astype(jnp.float32) * key_weight[..., None]).astype(jnp.bfloat16)
    update = jnp.einsum("bjhk,bjhv->bhkv", weighted, value_span, preferred_element_type=jnp.float32)
    kept_share = jnp.exp(-local_rates[None, :] * live_count[:, None].astype(jnp.float32))
    state_new = (kept_share[:, :, None, None] * prior_state.astype(jnp.float32) + update).astype(
        jnp.bfloat16
    )
    slots = head_slots
    flat_inputs = decode_inputs.reshape(step_total * total_prompts, model_width)
    query_part = jnp.dot(
        flat_inputs, w_query.reshape(model_width, key_piece), preferred_element_type=jnp.float32
    ).astype(jnp.bfloat16)
    key_part = jnp.dot(
        flat_inputs, w_key.reshape(model_width, key_piece), preferred_element_type=jnp.float32
    ).astype(jnp.bfloat16)
    value_dec = jnp.dot(
        flat_inputs,
        w_value.reshape(model_width, heads_here * value_slice),
        preferred_element_type=jnp.float32,
    ).astype(jnp.bfloat16)
    gate_values = jnp.dot(
        flat_inputs,
        w_gate.reshape(model_width, heads_here * value_slice),
        preferred_element_type=jnp.float32,
    )
    packed = jnp.concatenate([query_part, key_part, value_dec], -1)
    packed = packed.reshape(step_total, slots, prompts_here, -1).transpose(1, 0, 2, 3)
    arrived = lax.all_to_all(packed, "heads", 0, 0, tiled=True)
    query_own = (
        arrived[..., :key_piece]
        .transpose(1, 2, 0, 3)
        .reshape(step_total, prompts_here, heads_here, key_width)
    )
    key_own = (
        arrived[..., key_piece : 2 * key_piece]
        .transpose(1, 2, 0, 3)
        .reshape(step_total, prompts_here, heads_here, key_width)
    )
    value_own = (
        arrived[..., 2 * key_piece :]
        .reshape(slots, step_total, prompts_here, heads_here, value_slice)
        .transpose(1, 2, 3, 0, 4)
        .reshape(step_total, prompts_here, heads_here, value_width)
    )
    steps = jnp.arange(step_total)
    dec_positions = (local_lengths[None, :] + steps[:, None]).astype(jnp.float32)
    query_rot = rotate(query_own.astype(jnp.float32), dec_positions[:, :, None]).astype(
        jnp.bfloat16
    )
    key_rot = (
        rotate(key_own.astype(jnp.float32), dec_positions[:, :, None]) * key_width ** (-0.5)
    ).astype(jnp.bfloat16)
    from_state = jnp.einsum(
        "tbhk,bhkv->tbhv", query_rot, state_new, preferred_element_type=jnp.float32
    )
    step_gap = (steps[:, None] - steps[None, :]).astype(jnp.float32)
    step_decay = jnp.where(
        step_gap[None] >= 0,
        jnp.exp(-local_rates[:, None, None] * jnp.maximum(step_gap, 0.0)[None]),
        0.0,
    )
    step_scores = jnp.einsum(
        "tbhk,ubhk->bhtu", query_rot, key_rot, preferred_element_type=jnp.float32
    )
    from_steps = jnp.einsum(
        "bhtu,ubhv->tbhv",
        step_scores * step_decay[None],
        value_own.astype(jnp.float32),
        precision=lax.Precision.HIGHEST,
    )
    state_decay = jnp.exp(-local_rates[None, :] * (steps[:, None] + 1).astype(jnp.float32))
    readout = state_decay[:, None, :, None] * from_state + from_steps
    read_mean = jnp.mean(readout, -1, keepdims=True)
    read_square = jnp.mean(readout * readout, -1, keepdims=True)
    normed = norm_with(readout, read_mean, read_square)
    normed = normed.reshape(step_total, prompts_here, heads_here, slots, value_slice)
    normed = normed.transpose(3, 0, 1, 2, 4)
    normed = lax.all_to_all(normed, "heads", 0, 0, tiled=True)
    normed = normed.transpose(1, 0, 2, 3, 4).reshape(
        step_total, total_prompts, heads_here, value_slice
    )
    gates_steps = gate_values.reshape(step_total, total_prompts, heads_here, value_slice)
    activated = (
        (jax.nn.silu(gates_steps) * normed)
        .astype(jnp.bfloat16)
        .reshape(-1, heads_here * value_slice)
    )
    partial_out = jnp.dot(
        activated,
        w_out.reshape(heads_here * value_slice, model_width),
        preferred_element_type=jnp.float32,
    )
    partial_out = partial_out.reshape(step_total, total_prompts, model_width)
    queries, keys, value_span, prior_state, _ = lax.optimization_barrier(
        (queries, keys, value_span, prior_state, partial_out)
    )
    scores = jnp.einsum("bihk,bjhk->bhij", queries, keys, preferred_element_type=jnp.float32)
    weights = jnp.where(valid_rows[:, None, None, :], scores * decay_table[None], 0.0).astype(
        jnp.bfloat16
    )
    inner_sum = jnp.einsum(
        "bhij,bjhv->bihv", weights, value_span, preferred_element_type=jnp.float32
    )
    carried = jnp.einsum(
        "bihk,bhkv->bihv", queries, prior_state, preferred_element_type=jnp.float32
    )
    lead_decay = jnp.exp(-local_rates[None, :] * (offsets[:, None] + 1).astype(jnp.float32))
    mixed = inner_sum + lead_decay[None, :, :, None] * carried
    mean_value = jnp.mean(mixed, -1, keepdims=True)
    mean_square = jnp.mean(mixed * mixed, -1, keepdims=True)
    prefill_out = jnp.where(
        valid_rows[:, :, None, None], norm_with(mixed, mean_value, mean_square), 0.0
    ).astype(jnp.bfloat16)
    out_slots = head_slots * lax.axis_size("tp")
    column_block = model_width // out_slots
    pieces = partial_out.reshape(step_total, total_prompts, out_slots, column_block)
    pieces = lax.all_to_all(pieces.transpose(2, 0, 1, 3), ("heads", "tp"), 0, 0, tiled=True)
    decode_out = jnp.sum(pieces, 0).astype(jnp.bfloat16)
    return (prefill_out, decode_out)


def solution(mesh):
    placed = (
        P(("groups", "heads"), None, "tp", None),
        P(("groups", "heads"), None, "tp", None),
        P(("groups", "heads"), None, "tp", None),
        P(("groups", "heads"), "tp", None, None),
        P(),
        P("groups"),
        P(None, "groups", None),
        P(None, "tp", "heads", None),
        P(None, "tp", "heads", None),
        P(None, "tp", None, "heads", None),
        P(None, "tp", None, "heads", None),
        P("tp", None, "heads", None, None),
    )
    return jax.shard_map(
        per_device,
        mesh=mesh,
        in_specs=placed,
        out_specs=(P(("groups", "heads"), None, "tp", None), P(None, "groups", ("heads", "tp"))),
        check_vma=False,
    )
```

```python
import jax
import jax.numpy as jnp
from jax import lax
from jax.experimental import pallas as pl
from jax.experimental.pallas import tpu as pltpu
from jax.sharding import PartitionSpec as P

EPSILON = 1e-05


def rotate(values, positions):
    halfway = values.shape[-1] // 2
    frequency = 10000.0 ** (-jnp.arange(halfway).astype(jnp.float32) / halfway)
    angles = positions[..., None] * frequency
    cosine = jnp.cos(angles)
    sine_part = jnp.sin(angles)
    paired = values.reshape(values.shape[:-1] + (halfway, 2))
    even_part = paired[..., 0]
    odd_part = paired[..., 1]
    turned = jnp.stack(
        [even_part * cosine - odd_part * sine_part, odd_part * cosine + even_part * sine_part], -1
    )
    return turned.reshape(values.shape)


def norm_with(output, mean_value, mean_square):
    return (output - mean_value) * lax.rsqrt(mean_square - mean_value * mean_value + EPSILON)


def prefill_kernel(
    q_ref, k_ref, v_ref, prior_ref, cos_ref, sin_ref, swap_ref, table_ref, rows_ref,
    out_ref, state_ref,
):
    swap = swap_ref[...]
    cosine = cos_ref[...]
    sine_part = sin_ref[...]
    q_raw = q_ref[...]
    k_raw = k_ref[...]
    q_partner = jnp.dot(q_raw, swap, preferred_element_type=jnp.float32)
    k_partner = jnp.dot(k_raw, swap, preferred_element_type=jnp.float32)
    queries = (q_raw.astype(jnp.float32) * cosine + q_partner * sine_part).astype(jnp.bfloat16)
    keys_wide = (k_raw.astype(jnp.float32) * cosine + k_partner * sine_part) * (
        q_raw.shape[-1] ** (-0.5)
    )
    keys = keys_wide.astype(jnp.bfloat16)
    values = v_ref[...]
    prior = prior_ref[...]
    rows = rows_ref[...]
    lead = rows[:, 0:1]
    valid = rows[:, 1:2]
    key_weight = rows[:, 2:3]
    kept = rows[0:1, 3:4]
    scores = lax.dot_general(
        queries, keys, (((1,), (1,)), ((), ())), preferred_element_type=jnp.float32
    )
    weights = (scores * table_ref[...]).astype(jnp.bfloat16)
    inner = jnp.dot(weights, values, preferred_element_type=jnp.float32)
    carried = jnp.dot(queries, prior, preferred_element_type=jnp.float32)
    mixed = inner + lead * carried
    mean_value = jnp.mean(mixed, -1, keepdims=True)
    mean_square = jnp.mean(mixed * mixed, -1, keepdims=True)
    normed = norm_with(mixed, mean_value, mean_square)
    out_ref[...] = jnp.where(valid > 0.5, normed, 0.0).astype(out_ref.dtype)
    weighted = (keys.astype(jnp.float32) * key_weight).astype(jnp.bfloat16)
    update = lax.dot_general(
        weighted, values, (((0,), (0,)), ((), ())), preferred_element_type=jnp.float32
    )
    state_ref[...] = (kept * prior.astype(jnp.float32) + update).astype(state_ref.dtype)


def prefill(query_span, key_span, value_span, prior_state, local_rates, span_start, live_count):
    prompts_here, span_len, heads_here, key_width = query_span.shape
    value_width = value_span.shape[3]
    halfway = key_width // 2
    offsets = jnp.arange(span_len)
    positions = (span_start[:, None] + offsets[None, :]).astype(jnp.float32)
    frequency = 10000.0 ** (-jnp.arange(halfway).astype(jnp.float32) / halfway)
    angles = positions[..., None] * frequency
    cosine = jnp.repeat(jnp.cos(angles), 2, axis=-1)
    sine_part = jnp.sin(angles)
    sine_part = jnp.stack([-sine_part, sine_part], -1).reshape(cosine.shape)
    lane = jnp.arange(key_width)
    swap = (lane[:, None] == (lane[None, :] ^ 1)).astype(jnp.bfloat16)
    valid_rows = offsets[None, :] < live_count[:, None]
    distance = (offsets[:, None] - offsets[None, :]).astype(jnp.float32)
    decay_table = jnp.where(
        distance[None] >= 0,
        jnp.exp(-local_rates[:, None, None] * jnp.maximum(distance, 0.0)[None]),
        0.0,
    )
    table = jnp.where(valid_rows[:, None, None, :], decay_table[None], 0.0)
    lead_decay = jnp.exp(-local_rates[:, None] * (offsets[None, :] + 1).astype(jnp.float32))
    remaining = (live_count[:, None] - 1 - offsets[None, :]).astype(jnp.float32)
    key_weight = jnp.where(
        valid_rows[:, None, :],
        jnp.exp(-local_rates[None, :, None] * jnp.maximum(remaining, 0.0)[:, None, :]),
        0.0,
    )
    kept_share = jnp.exp(-local_rates[None, :] * live_count[:, None].astype(jnp.float32))
    shape_rows = (prompts_here, heads_here, span_len)
    rows = jnp.stack(
        [
            jnp.broadcast_to(lead_decay[None], shape_rows),
            jnp.broadcast_to(valid_rows[:, None, :].astype(jnp.float32), shape_rows),
            key_weight,
            jnp.broadcast_to(kept_share[:, :, None], shape_rows),
        ]
        + [jnp.zeros(shape_rows, jnp.float32)] * 4,
        -1,
    )
    grid = (prompts_here, heads_here)
    out, state = pl.pallas_call(
        prefill_kernel,
        grid=grid,
        in_specs=[
            pl.BlockSpec((None, span_len, key_width), lambda b, h: (b, 0, h)),
            pl.BlockSpec((None, span_len, key_width), lambda b, h: (b, 0, h)),
            pl.BlockSpec((None, span_len, value_width), lambda b, h: (b, 0, h)),
            pl.BlockSpec((None, None, key_width, value_width), lambda b, h: (b, h, 0, 0)),
            pl.BlockSpec((None, span_len, key_width), lambda b, h: (b, 0, 0)),
            pl.BlockSpec((None, span_len, key_width), lambda b, h: (b, 0, 0)),
            pl.BlockSpec((key_width, key_width), lambda b, h: (0, 0)),
            pl.BlockSpec((None, None, span_len, span_len), lambda b, h: (b, h, 0, 0)),
            pl.BlockSpec((None, None, span_len, 8), lambda b, h: (b, h, 0, 0)),
        ],
        out_specs=[
            pl.BlockSpec((None, span_len, value_width), lambda b, h: (b, 0, h)),
            pl.BlockSpec((None, None, key_width, value_width), lambda b, h: (b, h, 0, 0)),
        ],
        out_shape=[
            jax.ShapeDtypeStruct((prompts_here, span_len, heads_here * value_width), jnp.bfloat16),
            jax.ShapeDtypeStruct(prior_state.shape, jnp.bfloat16),
        ],
    )(
        query_span.reshape(prompts_here, span_len, heads_here * key_width),
        key_span.reshape(prompts_here, span_len, heads_here * key_width),
        value_span.reshape(prompts_here, span_len, heads_here * value_width),
        prior_state,
        cosine,
        sine_part,
        swap,
        table,
        rows,
    )
    return out.reshape(value_span.shape), state


def per_device(
    query_span,
    key_span,
    value_span,
    prior_state,
    decay_rates,
    prompt_lengths,
    decode_inputs,
    w_query,
    w_key,
    w_value,
    w_gate,
    w_out,
):
    prompts_here, span_len, heads_here, key_width = query_span.shape
    value_width = value_span.shape[3]
    model_width = decode_inputs.shape[2]
    step_total = decode_inputs.shape[0]
    head_slots = lax.axis_size("heads")
    total_prompts = prompts_here * head_slots
    key_piece = w_query.shape[3]
    value_slice = w_value.shape[4]
    tp_index = lax.axis_index("tp")
    slot_index = lax.axis_index("heads")
    local_rates = lax.dynamic_slice_in_dim(decay_rates, tp_index * heads_here, heads_here)
    local_lengths = lax.dynamic_slice_in_dim(
        prompt_lengths, slot_index * prompts_here, prompts_here
    )
    span_start = span_len * ((local_lengths - 1) // span_len)
    live_count = local_lengths - span_start
    prefill_out, state_new = prefill(
        query_span, key_span, value_span, prior_state, local_rates, span_start, live_count
    )
    slots = head_slots
    flat_inputs = decode_inputs.reshape(step_total * total_prompts, model_width)
    query_part = jnp.dot(
        flat_inputs, w_query.reshape(model_width, key_piece), preferred_element_type=jnp.float32
    ).astype(jnp.bfloat16)
    key_part = jnp.dot(
        flat_inputs, w_key.reshape(model_width, key_piece), preferred_element_type=jnp.float32
    ).astype(jnp.bfloat16)
    value_dec = jnp.dot(
        flat_inputs,
        w_value.reshape(model_width, heads_here * value_slice),
        preferred_element_type=jnp.float32,
    ).astype(jnp.bfloat16)
    gate_values = jnp.dot(
        flat_inputs,
        w_gate.reshape(model_width, heads_here * value_slice),
        preferred_element_type=jnp.float32,
    )
    packed = jnp.concatenate([query_part, key_part, value_dec], -1)
    packed = packed.reshape(step_total, slots, prompts_here, -1).transpose(1, 0, 2, 3)
    arrived = lax.all_to_all(packed, "heads", 0, 0, tiled=True)
    query_own = (
        arrived[..., :key_piece]
        .transpose(1, 2, 0, 3)
        .reshape(step_total, prompts_here, heads_here, key_width)
    )
    key_own = (
        arrived[..., key_piece : 2 * key_piece]
        .transpose(1, 2, 0, 3)
        .reshape(step_total, prompts_here, heads_here, key_width)
    )
    value_own = (
        arrived[..., 2 * key_piece :]
        .reshape(slots, step_total, prompts_here, heads_here, value_slice)
        .transpose(1, 2, 3, 0, 4)
        .reshape(step_total, prompts_here, heads_here, value_width)
    )
    steps = jnp.arange(step_total)
    dec_positions = (local_lengths[None, :] + steps[:, None]).astype(jnp.float32)
    query_rot = rotate(query_own.astype(jnp.float32), dec_positions[:, :, None]).astype(
        jnp.bfloat16
    )
    key_rot = (
        rotate(key_own.astype(jnp.float32), dec_positions[:, :, None]) * key_width ** (-0.5)
    ).astype(jnp.bfloat16)
    from_state = jnp.einsum(
        "tbhk,bhkv->tbhv", query_rot, state_new, preferred_element_type=jnp.float32
    )
    step_gap = (steps[:, None] - steps[None, :]).astype(jnp.float32)
    step_decay = jnp.where(
        step_gap[None] >= 0,
        jnp.exp(-local_rates[:, None, None] * jnp.maximum(step_gap, 0.0)[None]),
        0.0,
    )
    step_scores = jnp.einsum(
        "tbhk,ubhk->bhtu", query_rot, key_rot, preferred_element_type=jnp.float32
    )
    from_steps = jnp.einsum(
        "bhtu,ubhv->tbhv",
        step_scores * step_decay[None],
        value_own.astype(jnp.float32),
        precision=lax.Precision.HIGHEST,
    )
    state_decay = jnp.exp(-local_rates[None, :] * (steps[:, None] + 1).astype(jnp.float32))
    readout = state_decay[:, None, :, None] * from_state + from_steps
    read_mean = jnp.mean(readout, -1, keepdims=True)
    read_square = jnp.mean(readout * readout, -1, keepdims=True)
    normed = norm_with(readout, read_mean, read_square)
    normed = normed.reshape(step_total, prompts_here, heads_here, slots, value_slice)
    normed = normed.transpose(3, 0, 1, 2, 4)
    normed = lax.all_to_all(normed, "heads", 0, 0, tiled=True)
    normed = normed.transpose(1, 0, 2, 3, 4).reshape(
        step_total, total_prompts, heads_here, value_slice
    )
    gates_steps = gate_values.reshape(step_total, total_prompts, heads_here, value_slice)
    activated = (
        (jax.nn.silu(gates_steps) * normed)
        .astype(jnp.bfloat16)
        .reshape(-1, heads_here * value_slice)
    )
    partial_out = jnp.dot(
        activated,
        w_out.reshape(heads_here * value_slice, model_width),
        preferred_element_type=jnp.float32,
    )
    partial_out = partial_out.reshape(step_total, total_prompts, model_width)
    out_slots = head_slots * lax.axis_size("tp")
    column_block = model_width // out_slots
    pieces = partial_out.reshape(step_total, total_prompts, out_slots, column_block)
    pieces = lax.all_to_all(pieces.transpose(2, 0, 1, 3), ("heads", "tp"), 0, 0, tiled=True)
    decode_out = jnp.sum(pieces, 0).astype(jnp.bfloat16)
    return (prefill_out, decode_out)


def solution(mesh):
    placed = (
        P(("groups", "heads"), None, "tp", None),
        P(("groups", "heads"), None, "tp", None),
        P(("groups", "heads"), None, "tp", None),
        P(("groups", "heads"), "tp", None, None),
        P(),
        P("groups"),
        P(None, "groups", None),
        P(None, "tp", "heads", None),
        P(None, "tp", "heads", None),
        P(None, "tp", None, "heads", None),
        P(None, "tp", None, "heads", None),
        P("tp", None, "heads", None, None),
    )
    return jax.shard_map(
        per_device,
        mesh=mesh,
        in_specs=placed,
        out_specs=(P(("groups", "heads"), None, "tp", None), P(None, "groups", ("heads", "tp"))),
        check_vma=False,
    )
```

```python
import jax
import jax.numpy as jnp
from jax import lax
from jax.experimental import pallas as pl
from jax.experimental.pallas import tpu as pltpu
from jax.sharding import PartitionSpec as P

EPSILON = 1e-05


def rotate(values, positions):
    halfway = values.shape[-1] // 2
    frequency = 10000.0 ** (-jnp.arange(halfway).astype(jnp.float32) / halfway)
    angles = positions[..., None] * frequency
    cosine = jnp.cos(angles)
    sine_part = jnp.sin(angles)
    paired = values.reshape(values.shape[:-1] + (halfway, 2))
    even_part = paired[..., 0]
    odd_part = paired[..., 1]
    turned = jnp.stack(
        [even_part * cosine - odd_part * sine_part, odd_part * cosine + even_part * sine_part], -1
    )
    return turned.reshape(values.shape)


def norm_with(output, mean_value, mean_square):
    return (output - mean_value) * lax.rsqrt(mean_square - mean_value * mean_value + EPSILON)


def prefill_kernel(
    q_ref, k_ref, v_ref, prior_ref, cos_ref, sin_ref, swap_ref, table_ref, rows_ref,
    out_ref, state_ref,
):
    swap = swap_ref[...]
    cosine = cos_ref[...]
    sine_part = sin_ref[...]
    for head in range(q_ref.shape[1]):
        q_raw = q_ref[:, head, :]
        k_raw = k_ref[:, head, :]
        q_partner = jnp.dot(q_raw, swap, preferred_element_type=jnp.float32)
        k_partner = jnp.dot(k_raw, swap, preferred_element_type=jnp.float32)
        queries = (q_raw.astype(jnp.float32) * cosine + q_partner * sine_part).astype(
            jnp.bfloat16
        )
        keys_wide = (k_raw.astype(jnp.float32) * cosine + k_partner * sine_part) * (
            q_raw.shape[-1] ** (-0.5)
        )
        keys = keys_wide.astype(jnp.bfloat16)
        values = v_ref[:, head, :]
        prior = prior_ref[head]
        rows = rows_ref[head]
        lead = rows[:, 0:1]
        valid = rows[:, 1:2]
        key_weight = rows[:, 2:3]
        kept = rows[0:1, 3:4]
        scores = lax.dot_general(
            queries, keys, (((1,), (1,)), ((), ())), preferred_element_type=jnp.float32
        )
        weights = (scores * table_ref[head]).astype(jnp.bfloat16)
        inner = jnp.dot(weights, values, preferred_element_type=jnp.float32)
        carried = jnp.dot(queries, prior, preferred_element_type=jnp.float32)
        mixed = inner + lead * carried
        mean_value = jnp.mean(mixed, -1, keepdims=True)
        mean_square = jnp.mean(mixed * mixed, -1, keepdims=True)
        normed = norm_with(mixed, mean_value, mean_square)
        out_ref[:, head, :] = jnp.where(valid > 0.5, normed, 0.0).astype(out_ref.dtype)
        weighted = (keys.astype(jnp.float32) * key_weight).astype(jnp.bfloat16)
        update = lax.dot_general(
            weighted, values, (((0,), (0,)), ((), ())), preferred_element_type=jnp.float32
        )
        state_ref[head] = (kept * prior.astype(jnp.float32) + update).astype(state_ref.dtype)


def prefill(query_span, key_span, value_span, prior_state, local_rates, span_start, live_count):
    prompts_here, span_len, heads_here, key_width = query_span.shape
    value_width = value_span.shape[3]
    halfway = key_width // 2
    offsets = jnp.arange(span_len)
    positions = (span_start[:, None] + offsets[None, :]).astype(jnp.float32)
    frequency = 10000.0 ** (-jnp.arange(halfway).astype(jnp.float32) / halfway)
    angles = positions[..., None] * frequency
    cosine = jnp.repeat(jnp.cos(angles), 2, axis=-1)
    sine_part = jnp.sin(angles)
    sine_part = jnp.stack([-sine_part, sine_part], -1).reshape(cosine.shape)
    lane = jnp.arange(key_width)
    swap = (lane[:, None] == (lane[None, :] ^ 1)).astype(jnp.bfloat16)
    valid_rows = offsets[None, :] < live_count[:, None]
    distance = (offsets[:, None] - offsets[None, :]).astype(jnp.float32)
    decay_table = jnp.where(
        distance[None] >= 0,
        jnp.exp(-local_rates[:, None, None] * jnp.maximum(distance, 0.0)[None]),
        0.0,
    )
    table = jnp.where(valid_rows[:, None, None, :], decay_table[None], 0.0)
    lead_decay = jnp.exp(-local_rates[:, None] * (offsets[None, :] + 1).astype(jnp.float32))
    remaining = (live_count[:, None] - 1 - offsets[None, :]).astype(jnp.float32)
    key_weight = jnp.where(
        valid_rows[:, None, :],
        jnp.exp(-local_rates[None, :, None] * jnp.maximum(remaining, 0.0)[:, None, :]),
        0.0,
    )
    kept_share = jnp.exp(-local_rates[None, :] * live_count[:, None].astype(jnp.float32))
    shape_rows = (prompts_here, heads_here, span_len)
    rows = jnp.stack(
        [
            jnp.broadcast_to(lead_decay[None], shape_rows),
            jnp.broadcast_to(valid_rows[:, None, :].astype(jnp.float32), shape_rows),
            key_weight,
            jnp.broadcast_to(kept_share[:, :, None], shape_rows),
        ]
        + [jnp.zeros(shape_rows, jnp.float32)] * 4,
        -1,
    )
    grid = (prompts_here,)
    out, state = pl.pallas_call(
        prefill_kernel,
        grid=grid,
        in_specs=[
            pl.BlockSpec((None, span_len, heads_here, key_width), lambda b: (b, 0, 0, 0)),
            pl.BlockSpec((None, span_len, heads_here, key_width), lambda b: (b, 0, 0, 0)),
            pl.BlockSpec((None, span_len, heads_here, value_width), lambda b: (b, 0, 0, 0)),
            pl.BlockSpec((None, heads_here, key_width, value_width), lambda b: (b, 0, 0, 0)),
            pl.BlockSpec((None, span_len, key_width), lambda b: (b, 0, 0)),
            pl.BlockSpec((None, span_len, key_width), lambda b: (b, 0, 0)),
            pl.BlockSpec((key_width, key_width), lambda b: (0, 0)),
            pl.BlockSpec((None, heads_here, span_len, span_len), lambda b: (b, 0, 0, 0)),
            pl.BlockSpec((None, heads_here, span_len, 8), lambda b: (b, 0, 0, 0)),
        ],
        out_specs=[
            pl.BlockSpec((None, span_len, heads_here, value_width), lambda b: (b, 0, 0, 0)),
            pl.BlockSpec((None, heads_here, key_width, value_width), lambda b: (b, 0, 0, 0)),
        ],
        out_shape=[
            jax.ShapeDtypeStruct(value_span.shape, jnp.bfloat16),
            jax.ShapeDtypeStruct(prior_state.shape, jnp.bfloat16),
        ],
    )(
        query_span,
        key_span,
        value_span,
        prior_state,
        cosine,
        sine_part,
        swap,
        table,
        rows,
    )
    return out, state


def per_device(
    query_span,
    key_span,
    value_span,
    prior_state,
    decay_rates,
    prompt_lengths,
    decode_inputs,
    w_query,
    w_key,
    w_value,
    w_gate,
    w_out,
):
    prompts_here, span_len, heads_here, key_width = query_span.shape
    value_width = value_span.shape[3]
    model_width = decode_inputs.shape[2]
    step_total = decode_inputs.shape[0]
    head_slots = lax.axis_size("heads")
    total_prompts = prompts_here * head_slots
    key_piece = w_query.shape[3]
    value_slice = w_value.shape[4]
    tp_index = lax.axis_index("tp")
    slot_index = lax.axis_index("heads")
    local_rates = lax.dynamic_slice_in_dim(decay_rates, tp_index * heads_here, heads_here)
    local_lengths = lax.dynamic_slice_in_dim(
        prompt_lengths, slot_index * prompts_here, prompts_here
    )
    span_start = span_len * ((local_lengths - 1) // span_len)
    live_count = local_lengths - span_start
    prefill_out, state_new = prefill(
        query_span, key_span, value_span, prior_state, local_rates, span_start, live_count
    )
    slots = head_slots
    flat_inputs = decode_inputs.reshape(step_total * total_prompts, model_width)
    query_part = jnp.dot(
        flat_inputs, w_query.reshape(model_width, key_piece), preferred_element_type=jnp.float32
    ).astype(jnp.bfloat16)
    key_part = jnp.dot(
        flat_inputs, w_key.reshape(model_width, key_piece), preferred_element_type=jnp.float32
    ).astype(jnp.bfloat16)
    value_dec = jnp.dot(
        flat_inputs,
        w_value.reshape(model_width, heads_here * value_slice),
        preferred_element_type=jnp.float32,
    ).astype(jnp.bfloat16)
    gate_values = jnp.dot(
        flat_inputs,
        w_gate.reshape(model_width, heads_here * value_slice),
        preferred_element_type=jnp.float32,
    )
    steps = jnp.arange(step_total)
    halfway = key_width // 2
    head_column = (slot_index * key_piece + jnp.arange(key_piece)) % key_width
    column_frequency = 10000.0 ** (-(head_column // 2).astype(jnp.float32) / halfway)
    dec_positions = (
        (prompt_lengths[None, :] + steps[:, None]).astype(jnp.float32).reshape(-1, 1)
    )
    dec_angles = dec_positions * column_frequency[None, :]
    dec_cosine = jnp.cos(dec_angles)
    dec_sine = jnp.where(head_column % 2 == 0, -1.0, 1.0)[None, :] * jnp.sin(dec_angles)
    lane = jnp.arange(key_piece)
    swap = (lane[:, None] == (lane[None, :] ^ 1)).astype(jnp.bfloat16)
    query_partner = jnp.dot(query_part, swap, preferred_element_type=jnp.float32)
    key_partner = jnp.dot(key_part, swap, preferred_element_type=jnp.float32)
    query_turned = (
        query_part.astype(jnp.float32) * dec_cosine + query_partner * dec_sine
    ).astype(jnp.bfloat16)
    key_turned = (
        (key_part.astype(jnp.float32) * dec_cosine + key_partner * dec_sine)
        * key_width ** (-0.5)
    ).astype(jnp.bfloat16)
    packed = jnp.concatenate([query_turned, key_turned, value_dec], -1)
    packed = packed.reshape(step_total, slots, prompts_here, -1).transpose(1, 0, 2, 3)
    arrived = lax.all_to_all(packed, "heads", 0, 0, tiled=True)
    query_rot = (
        arrived[..., :key_piece]
        .transpose(1, 2, 0, 3)
        .reshape(step_total, prompts_here, heads_here, key_width)
    )
    key_rot = (
        arrived[..., key_piece : 2 * key_piece]
        .transpose(1, 2, 0, 3)
        .reshape(step_total, prompts_here, heads_here, key_width)
    )
    value_own = (
        arrived[..., 2 * key_piece :]
        .reshape(slots, step_total, prompts_here, heads_here, value_slice)
        .transpose(1, 2, 3, 0, 4)
        .reshape(step_total, prompts_here, heads_here, value_width)
    )
    from_state = jnp.einsum(
        "tbhk,bhkv->tbhv", query_rot, state_new, preferred_element_type=jnp.float32
    )
    step_gap = (steps[:, None] - steps[None, :]).astype(jnp.float32)
    step_decay = jnp.where(
        step_gap[None] >= 0,
        jnp.exp(-local_rates[:, None, None] * jnp.maximum(step_gap, 0.0)[None]),
        0.0,
    )
    step_scores = jnp.einsum(
        "tbhk,ubhk->bhtu", query_rot, key_rot, preferred_element_type=jnp.float32
    )
    from_steps = jnp.einsum(
        "bhtu,ubhv->tbhv",
        step_scores * step_decay[None],
        value_own.astype(jnp.float32),
        precision=lax.Precision.HIGHEST,
    )
    state_decay = jnp.exp(-local_rates[None, :] * (steps[:, None] + 1).astype(jnp.float32))
    readout = state_decay[:, None, :, None] * from_state + from_steps
    read_mean = jnp.mean(readout, -1, keepdims=True)
    read_square = jnp.mean(readout * readout, -1, keepdims=True)
    normed = norm_with(readout, read_mean, read_square)
    normed = normed.reshape(step_total, prompts_here, heads_here, slots, value_slice)
    normed = normed.transpose(3, 0, 1, 2, 4)
    normed = lax.all_to_all(normed, "heads", 0, 0, tiled=True)
    normed = normed.transpose(1, 0, 2, 3, 4).reshape(
        step_total, total_prompts, heads_here, value_slice
    )
    gates_steps = gate_values.reshape(step_total, total_prompts, heads_here, value_slice)
    activated = (
        (jax.nn.silu(gates_steps) * normed)
        .astype(jnp.bfloat16)
        .reshape(-1, heads_here * value_slice)
    )
    partial_out = jnp.dot(
        activated,
        w_out.reshape(heads_here * value_slice, model_width),
        preferred_element_type=jnp.float32,
    )
    partial_out = partial_out.reshape(step_total, total_prompts, model_width)
    out_slots = head_slots * lax.axis_size("tp")
    column_block = model_width // out_slots
    pieces = partial_out.reshape(step_total, total_prompts, out_slots, column_block)
    pieces = lax.all_to_all(pieces.transpose(2, 0, 1, 3), ("heads", "tp"), 0, 0, tiled=True)
    decode_out = jnp.sum(pieces, 0).astype(jnp.bfloat16)
    return (prefill_out, decode_out)


def solution(mesh):
    placed = (
        P(("groups", "heads"), None, "tp", None),
        P(("groups", "heads"), None, "tp", None),
        P(("groups", "heads"), None, "tp", None),
        P(("groups", "heads"), "tp", None, None),
        P(),
        P("groups"),
        P(None, "groups", None),
        P(None, "tp", "heads", None),
        P(None, "tp", "heads", None),
        P(None, "tp", None, "heads", None),
        P(None, "tp", None, "heads", None),
        P("tp", None, "heads", None, None),
    )
    return jax.shard_map(
        per_device,
        mesh=mesh,
        in_specs=placed,
        out_specs=(P(("groups", "heads"), None, "tp", None), P(None, "groups", ("heads", "tp"))),
        check_vma=False,
    )
```

```python
import jax
import jax.numpy as jnp
from jax import lax
from jax.experimental import pallas as pl
from jax.experimental.pallas import tpu as pltpu
from jax.sharding import PartitionSpec as P

EPSILON = 1e-05


def rotate(values, positions):
    halfway = values.shape[-1] // 2
    frequency = 10000.0 ** (-jnp.arange(halfway).astype(jnp.float32) / halfway)
    angles = positions[..., None] * frequency
    cosine = jnp.cos(angles)
    sine_part = jnp.sin(angles)
    paired = values.reshape(values.shape[:-1] + (halfway, 2))
    even_part = paired[..., 0]
    odd_part = paired[..., 1]
    turned = jnp.stack(
        [even_part * cosine - odd_part * sine_part, odd_part * cosine + even_part * sine_part], -1
    )
    return turned.reshape(values.shape)


def norm_with(output, mean_value, mean_square):
    return (output - mean_value) * lax.rsqrt(mean_square - mean_value * mean_value + EPSILON)


def turn_lanes(raw, swap, cosine, sine_part):
    partner = jnp.dot(raw, swap, preferred_element_type=jnp.float32)
    return raw.astype(jnp.float32) * cosine + partner * sine_part


def state_kernel(k_ref, v_ref, prior_ref, cos_ref, sin_ref, swap_ref, rows_ref, state_ref):
    swap = swap_ref[...]
    cosine = cos_ref[...]
    sine_part = sin_ref[...]
    for head in range(k_ref.shape[1]):
        k_raw = k_ref[:, head, :]
        keys = (turn_lanes(k_raw, swap, cosine, sine_part) * (k_raw.shape[-1] ** (-0.5))).astype(
            jnp.bfloat16
        )
        rows = rows_ref[head]
        weighted = (keys.astype(jnp.float32) * rows[:, 2:3]).astype(jnp.bfloat16)
        update = lax.dot_general(
            weighted, v_ref[:, head, :], (((0,), (0,)), ((), ())),
            preferred_element_type=jnp.float32,
        )
        kept = rows[0:1, 3:4]
        state_ref[head] = (kept * prior_ref[head].astype(jnp.float32) + update).astype(
            state_ref.dtype
        )


def output_kernel(
    q_ref, k_ref, v_ref, prior_ref, cos_ref, sin_ref, swap_ref, table_ref, rows_ref, out_ref
):
    swap = swap_ref[...]
    cosine = cos_ref[...]
    sine_part = sin_ref[...]
    for head in range(q_ref.shape[1]):
        q_raw = q_ref[:, head, :]
        k_raw = k_ref[:, head, :]
        queries = turn_lanes(q_raw, swap, cosine, sine_part).astype(jnp.bfloat16)
        keys = (turn_lanes(k_raw, swap, cosine, sine_part) * (k_raw.shape[-1] ** (-0.5))).astype(
            jnp.bfloat16
        )
        rows = rows_ref[head]
        scores = lax.dot_general(
            queries, keys, (((1,), (1,)), ((), ())), preferred_element_type=jnp.float32
        )
        weights = (scores * table_ref[head]).astype(jnp.bfloat16)
        inner = jnp.dot(weights, v_ref[:, head, :], preferred_element_type=jnp.float32)
        carried = jnp.dot(queries, prior_ref[head], preferred_element_type=jnp.float32)
        mixed = inner + rows[:, 0:1] * carried
        mean_value = jnp.mean(mixed, -1, keepdims=True)
        mean_square = jnp.mean(mixed * mixed, -1, keepdims=True)
        normed = norm_with(mixed, mean_value, mean_square)
        out_ref[:, head, :] = jnp.where(rows[:, 1:2] > 0.5, normed, 0.0).astype(out_ref.dtype)


def prefill_tables(key_width, span_len, local_rates, span_start, live_count):
    halfway = key_width // 2
    offsets = jnp.arange(span_len)
    positions = (span_start[:, None] + offsets[None, :]).astype(jnp.float32)
    frequency = 10000.0 ** (-jnp.arange(halfway).astype(jnp.float32) / halfway)
    angles = positions[..., None] * frequency
    cosine = jnp.repeat(jnp.cos(angles), 2, axis=-1)
    sine_part = jnp.sin(angles)
    sine_part = jnp.stack([-sine_part, sine_part], -1).reshape(cosine.shape)
    lane = jnp.arange(key_width)
    swap = (lane[:, None] == (lane[None, :] ^ 1)).astype(jnp.bfloat16)
    valid_rows = offsets[None, :] < live_count[:, None]
    lead_decay = jnp.exp(-local_rates[:, None] * (offsets[None, :] + 1).astype(jnp.float32))
    remaining = (live_count[:, None] - 1 - offsets[None, :]).astype(jnp.float32)
    key_weight = jnp.where(
        valid_rows[:, None, :],
        jnp.exp(-local_rates[None, :, None] * jnp.maximum(remaining, 0.0)[:, None, :]),
        0.0,
    )
    kept_share = jnp.exp(-local_rates[None, :] * live_count[:, None].astype(jnp.float32))
    shape_rows = key_weight.shape
    rows = jnp.stack(
        [
            jnp.broadcast_to(lead_decay[None], shape_rows),
            jnp.broadcast_to(valid_rows[:, None, :].astype(jnp.float32), shape_rows),
            key_weight,
            jnp.broadcast_to(kept_share[:, :, None], shape_rows),
        ]
        + [jnp.zeros(shape_rows, jnp.float32)] * 4,
        -1,
    )
    return cosine, sine_part, swap, rows, valid_rows


def new_state(key_span, value_span, prior_state, tables):
    prompts_here, span_len, heads_here, key_width = key_span.shape
    cosine, sine_part, swap, rows, _ = tables
    column_block = 128
    return pl.pallas_call(
        state_kernel,
        grid=(prompts_here, value_span.shape[3] // column_block),
        in_specs=[
            pl.BlockSpec((None, span_len, heads_here, key_width), lambda b, c: (b, 0, 0, 0)),
            pl.BlockSpec((None, span_len, heads_here, column_block), lambda b, c: (b, 0, 0, c)),
            pl.BlockSpec((None, heads_here, key_width, column_block), lambda b, c: (b, 0, 0, c)),
            pl.BlockSpec((None, span_len, key_width), lambda b, c: (b, 0, 0)),
            pl.BlockSpec((None, span_len, key_width), lambda b, c: (b, 0, 0)),
            pl.BlockSpec((key_width, key_width), lambda b, c: (0, 0)),
            pl.BlockSpec((None, heads_here, span_len, 8), lambda b, c: (b, 0, 0, 0)),
        ],
        out_specs=pl.BlockSpec(
            (None, heads_here, key_width, column_block), lambda b, c: (b, 0, 0, c)
        ),
        out_shape=jax.ShapeDtypeStruct(prior_state.shape, jnp.bfloat16),
    )(key_span, value_span, prior_state, cosine, sine_part, swap, rows)


def prefill_output(query_span, key_span, value_span, prior_state, local_rates, tables):
    prompts_here, span_len, heads_here, key_width = query_span.shape
    value_width = value_span.shape[3]
    cosine, sine_part, swap, rows, valid_rows = tables
    offsets = jnp.arange(span_len)
    distance = (offsets[:, None] - offsets[None, :]).astype(jnp.float32)
    decay_table = jnp.where(
        distance[None] >= 0,
        jnp.exp(-local_rates[:, None, None] * jnp.maximum(distance, 0.0)[None]),
        0.0,
    )
    table = jnp.where(valid_rows[:, None, None, :], decay_table[None], 0.0)
    return pl.pallas_call(
        output_kernel,
        grid=(prompts_here,),
        in_specs=[
            pl.BlockSpec((None, span_len, heads_here, key_width), lambda b: (b, 0, 0, 0)),
            pl.BlockSpec((None, span_len, heads_here, key_width), lambda b: (b, 0, 0, 0)),
            pl.BlockSpec((None, span_len, heads_here, value_width), lambda b: (b, 0, 0, 0)),
            pl.BlockSpec((None, heads_here, key_width, value_width), lambda b: (b, 0, 0, 0)),
            pl.BlockSpec((None, span_len, key_width), lambda b: (b, 0, 0)),
            pl.BlockSpec((None, span_len, key_width), lambda b: (b, 0, 0)),
            pl.BlockSpec((key_width, key_width), lambda b: (0, 0)),
            pl.BlockSpec((None, heads_here, span_len, span_len), lambda b: (b, 0, 0, 0)),
            pl.BlockSpec((None, heads_here, span_len, 8), lambda b: (b, 0, 0, 0)),
        ],
        out_specs=pl.BlockSpec(
            (None, span_len, heads_here, value_width), lambda b: (b, 0, 0, 0)
        ),
        out_shape=jax.ShapeDtypeStruct(value_span.shape, jnp.bfloat16),
    )(query_span, key_span, value_span, prior_state, cosine, sine_part, swap, table, rows)


def per_device(
    query_span,
    key_span,
    value_span,
    prior_state,
    decay_rates,
    prompt_lengths,
    decode_inputs,
    w_query,
    w_key,
    w_value,
    w_gate,
    w_out,
):
    prompts_here, span_len, heads_here, key_width = query_span.shape
    value_width = value_span.shape[3]
    model_width = decode_inputs.shape[2]
    step_total = decode_inputs.shape[0]
    head_slots = lax.axis_size("heads")
    total_prompts = prompts_here * head_slots
    key_piece = w_query.shape[3]
    value_slice = w_value.shape[4]
    tp_index = lax.axis_index("tp")
    slot_index = lax.axis_index("heads")
    local_rates = lax.dynamic_slice_in_dim(decay_rates, tp_index * heads_here, heads_here)
    local_lengths = lax.dynamic_slice_in_dim(
        prompt_lengths, slot_index * prompts_here, prompts_here
    )
    span_start = span_len * ((local_lengths - 1) // span_len)
    live_count = local_lengths - span_start
    tables = prefill_tables(key_width, span_len, local_rates, span_start, live_count)
    state_new = new_state(key_span, value_span, prior_state, tables)
    slots = head_slots
    flat_inputs = decode_inputs.reshape(step_total * total_prompts, model_width)
    query_part = jnp.dot(
        flat_inputs, w_query.reshape(model_width, key_piece), preferred_element_type=jnp.float32
    ).astype(jnp.bfloat16)
    key_part = jnp.dot(
        flat_inputs, w_key.reshape(model_width, key_piece), preferred_element_type=jnp.float32
    ).astype(jnp.bfloat16)
    value_dec = jnp.dot(
        flat_inputs,
        w_value.reshape(model_width, heads_here * value_slice),
        preferred_element_type=jnp.float32,
    ).astype(jnp.bfloat16)
    gate_values = jnp.dot(
        flat_inputs,
        w_gate.reshape(model_width, heads_here * value_slice),
        preferred_element_type=jnp.float32,
    )
    steps = jnp.arange(step_total)
    halfway = key_width // 2
    head_column = (slot_index * key_piece + jnp.arange(key_piece)) % key_width
    column_frequency = 10000.0 ** (-(head_column // 2).astype(jnp.float32) / halfway)
    dec_positions = (
        (prompt_lengths[None, :] + steps[:, None]).astype(jnp.float32).reshape(-1, 1)
    )
    dec_angles = dec_positions * column_frequency[None, :]
    dec_cosine = jnp.cos(dec_angles)
    dec_sine = jnp.where(head_column % 2 == 0, -1.0, 1.0)[None, :] * jnp.sin(dec_angles)
    lane = jnp.arange(key_piece)
    swap = (lane[:, None] == (lane[None, :] ^ 1)).astype(jnp.bfloat16)
    query_partner = jnp.dot(query_part, swap, preferred_element_type=jnp.float32)
    key_partner = jnp.dot(key_part, swap, preferred_element_type=jnp.float32)
    query_turned = (
        query_part.astype(jnp.float32) * dec_cosine + query_partner * dec_sine
    ).astype(jnp.bfloat16)
    key_turned = (
        (key_part.astype(jnp.float32) * dec_cosine + key_partner * dec_sine)
        * key_width ** (-0.5)
    ).astype(jnp.bfloat16)
    packed = jnp.concatenate([query_turned, key_turned, value_dec], -1)
    packed = packed.reshape(step_total, slots, prompts_here, -1).transpose(1, 0, 2, 3)
    arrived = lax.all_to_all(packed, "heads", 0, 0, tiled=True)
    query_rot = (
        arrived[..., :key_piece]
        .transpose(1, 2, 0, 3)
        .reshape(step_total, prompts_here, heads_here, key_width)
    )
    key_rot = (
        arrived[..., key_piece : 2 * key_piece]
        .transpose(1, 2, 0, 3)
        .reshape(step_total, prompts_here, heads_here, key_width)
    )
    value_own = (
        arrived[..., 2 * key_piece :]
        .reshape(slots, step_total, prompts_here, heads_here, value_slice)
        .transpose(1, 2, 3, 0, 4)
        .reshape(step_total, prompts_here, heads_here, value_width)
    )
    from_state = jnp.einsum(
        "tbhk,bhkv->tbhv", query_rot, state_new, preferred_element_type=jnp.float32
    )
    step_gap = (steps[:, None] - steps[None, :]).astype(jnp.float32)
    step_decay = jnp.where(
        step_gap[None] >= 0,
        jnp.exp(-local_rates[:, None, None] * jnp.maximum(step_gap, 0.0)[None]),
        0.0,
    )
    step_scores = jnp.einsum(
        "tbhk,ubhk->bhtu", query_rot, key_rot, preferred_element_type=jnp.float32
    )
    from_steps = jnp.einsum(
        "bhtu,ubhv->tbhv",
        step_scores * step_decay[None],
        value_own.astype(jnp.float32),
        precision=lax.Precision.HIGHEST,
    )
    state_decay = jnp.exp(-local_rates[None, :] * (steps[:, None] + 1).astype(jnp.float32))
    readout = state_decay[:, None, :, None] * from_state + from_steps
    read_mean = jnp.mean(readout, -1, keepdims=True)
    read_square = jnp.mean(readout * readout, -1, keepdims=True)
    normed = norm_with(readout, read_mean, read_square)
    normed = normed.reshape(step_total, prompts_here, heads_here, slots, value_slice)
    normed = normed.transpose(3, 0, 1, 2, 4)
    normed = lax.all_to_all(normed, "heads", 0, 0, tiled=True)
    normed = normed.transpose(1, 0, 2, 3, 4).reshape(
        step_total, total_prompts, heads_here, value_slice
    )
    gates_steps = gate_values.reshape(step_total, total_prompts, heads_here, value_slice)
    activated = (
        (jax.nn.silu(gates_steps) * normed)
        .astype(jnp.bfloat16)
        .reshape(-1, heads_here * value_slice)
    )
    partial_out = jnp.dot(
        activated,
        w_out.reshape(heads_here * value_slice, model_width),
        preferred_element_type=jnp.float32,
    )
    partial_out = partial_out.reshape(step_total, total_prompts, model_width)
    query_span, key_span, value_span, prior_state, _ = lax.optimization_barrier(
        (query_span, key_span, value_span, prior_state, partial_out)
    )
    prefill_out = prefill_output(
        query_span, key_span, value_span, prior_state, local_rates, tables
    )
    out_slots = head_slots * lax.axis_size("tp")
    column_block = model_width // out_slots
    pieces = partial_out.reshape(step_total, total_prompts, out_slots, column_block)
    pieces = lax.all_to_all(pieces.transpose(2, 0, 1, 3), ("heads", "tp"), 0, 0, tiled=True)
    decode_out = jnp.sum(pieces, 0).astype(jnp.bfloat16)
    return (prefill_out, decode_out)


def solution(mesh):
    placed = (
        P(("groups", "heads"), None, "tp", None),
        P(("groups", "heads"), None, "tp", None),
        P(("groups", "heads"), None, "tp", None),
        P(("groups", "heads"), "tp", None, None),
        P(),
        P("groups"),
        P(None, "groups", None),
        P(None, "tp", "heads", None),
        P(None, "tp", "heads", None),
        P(None, "tp", None, "heads", None),
        P(None, "tp", None, "heads", None),
        P("tp", None, "heads", None, None),
    )
    return jax.shard_map(
        per_device,
        mesh=mesh,
        in_specs=placed,
        out_specs=(P(("groups", "heads"), None, "tp", None), P(None, "groups", ("heads", "tp"))),
        check_vma=False,
    )
```

```python
import jax
import jax.numpy as jnp
from jax import lax
from jax.experimental import pallas as pl
from jax.experimental.pallas import tpu as pltpu
from jax.sharding import PartitionSpec as P

EPSILON = 1e-05


def rotate(values, positions):
    halfway = values.shape[-1] // 2
    frequency = 10000.0 ** (-jnp.arange(halfway).astype(jnp.float32) / halfway)
    angles = positions[..., None] * frequency
    cosine = jnp.cos(angles)
    sine_part = jnp.sin(angles)
    paired = values.reshape(values.shape[:-1] + (halfway, 2))
    even_part = paired[..., 0]
    odd_part = paired[..., 1]
    turned = jnp.stack(
        [even_part * cosine - odd_part * sine_part, odd_part * cosine + even_part * sine_part], -1
    )
    return turned.reshape(values.shape)


def norm_with(output, mean_value, mean_square):
    return (output - mean_value) * lax.rsqrt(mean_square - mean_value * mean_value + EPSILON)


def turn_lanes(raw, swap, cosine, sine_part):
    partner = jnp.dot(raw, swap, preferred_element_type=jnp.float32)
    return raw.astype(jnp.float32) * cosine + partner * sine_part


def output_kernel(
    q_ref, k_ref, v_ref, prior_ref, cos_ref, sin_ref, swap_ref, table_ref, rows_ref, out_ref
):
    swap = swap_ref[...]
    cosine = cos_ref[...]
    sine_part = sin_ref[...]
    for head in range(q_ref.shape[1]):
        q_raw = q_ref[:, head, :]
        k_raw = k_ref[:, head, :]
        queries = turn_lanes(q_raw, swap, cosine, sine_part).astype(jnp.bfloat16)
        keys = (turn_lanes(k_raw, swap, cosine, sine_part) * (k_raw.shape[-1] ** (-0.5))).astype(
            jnp.bfloat16
        )
        rows = rows_ref[head]
        scores = lax.dot_general(
            queries, keys, (((1,), (1,)), ((), ())), preferred_element_type=jnp.float32
        )
        weights = (scores * table_ref[head]).astype(jnp.bfloat16)
        inner = jnp.dot(weights, v_ref[:, head, :], preferred_element_type=jnp.float32)
        carried = jnp.dot(queries, prior_ref[head], preferred_element_type=jnp.float32)
        mixed = inner + rows[:, 0:1] * carried
        mean_value = jnp.mean(mixed, -1, keepdims=True)
        mean_square = jnp.mean(mixed * mixed, -1, keepdims=True)
        normed = norm_with(mixed, mean_value, mean_square)
        out_ref[:, head, :] = jnp.where(rows[:, 1:2] > 0.5, normed, 0.0).astype(out_ref.dtype)


def prefill_tables(key_width, span_len, local_rates, span_start, live_count):
    halfway = key_width // 2
    offsets = jnp.arange(span_len)
    positions = (span_start[:, None] + offsets[None, :]).astype(jnp.float32)
    frequency = 10000.0 ** (-jnp.arange(halfway).astype(jnp.float32) / halfway)
    angles = positions[..., None] * frequency
    cosine = jnp.repeat(jnp.cos(angles), 2, axis=-1)
    sine_part = jnp.sin(angles)
    sine_part = jnp.stack([-sine_part, sine_part], -1).reshape(cosine.shape)
    lane = jnp.arange(key_width)
    swap = (lane[:, None] == (lane[None, :] ^ 1)).astype(jnp.bfloat16)
    valid_rows = offsets[None, :] < live_count[:, None]
    lead_decay = jnp.exp(-local_rates[:, None] * (offsets[None, :] + 1).astype(jnp.float32))
    remaining = (live_count[:, None] - 1 - offsets[None, :]).astype(jnp.float32)
    key_weight = jnp.where(
        valid_rows[:, None, :],
        jnp.exp(-local_rates[None, :, None] * jnp.maximum(remaining, 0.0)[:, None, :]),
        0.0,
    )
    kept_share = jnp.exp(-local_rates[None, :] * live_count[:, None].astype(jnp.float32))
    shape_rows = key_weight.shape
    rows = jnp.stack(
        [
            jnp.broadcast_to(lead_decay[None], shape_rows),
            jnp.broadcast_to(valid_rows[:, None, :].astype(jnp.float32), shape_rows),
            key_weight,
            jnp.broadcast_to(kept_share[:, :, None], shape_rows),
        ]
        + [jnp.zeros(shape_rows, jnp.float32)] * 4,
        -1,
    )
    return cosine, sine_part, swap, rows, valid_rows


def prefill_output(query_span, key_span, value_span, prior_state, local_rates, tables):
    prompts_here, span_len, heads_here, key_width = query_span.shape
    value_width = value_span.shape[3]
    cosine, sine_part, swap, rows, valid_rows = tables
    offsets = jnp.arange(span_len)
    distance = (offsets[:, None] - offsets[None, :]).astype(jnp.float32)
    decay_table = jnp.where(
        distance[None] >= 0,
        jnp.exp(-local_rates[:, None, None] * jnp.maximum(distance, 0.0)[None]),
        0.0,
    )
    table = jnp.where(valid_rows[:, None, None, :], decay_table[None], 0.0)
    return pl.pallas_call(
        output_kernel,
        grid=(prompts_here,),
        in_specs=[
            pl.BlockSpec((None, span_len, heads_here, key_width), lambda b: (b, 0, 0, 0)),
            pl.BlockSpec((None, span_len, heads_here, key_width), lambda b: (b, 0, 0, 0)),
            pl.BlockSpec((None, span_len, heads_here, value_width), lambda b: (b, 0, 0, 0)),
            pl.BlockSpec((None, heads_here, key_width, value_width), lambda b: (b, 0, 0, 0)),
            pl.BlockSpec((None, span_len, key_width), lambda b: (b, 0, 0)),
            pl.BlockSpec((None, span_len, key_width), lambda b: (b, 0, 0)),
            pl.BlockSpec((key_width, key_width), lambda b: (0, 0)),
            pl.BlockSpec((None, heads_here, span_len, span_len), lambda b: (b, 0, 0, 0)),
            pl.BlockSpec((None, heads_here, span_len, 8), lambda b: (b, 0, 0, 0)),
        ],
        out_specs=pl.BlockSpec(
            (None, span_len, heads_here, value_width), lambda b: (b, 0, 0, 0)
        ),
        out_shape=jax.ShapeDtypeStruct(value_span.shape, jnp.bfloat16),
    )(query_span, key_span, value_span, prior_state, cosine, sine_part, swap, table, rows)


def per_device(
    query_span,
    key_span,
    value_span,
    prior_state,
    decay_rates,
    prompt_lengths,
    decode_inputs,
    w_query,
    w_key,
    w_value,
    w_gate,
    w_out,
):
    prompts_here, span_len, heads_here, key_width = query_span.shape
    value_width = value_span.shape[3]
    model_width = decode_inputs.shape[2]
    step_total = decode_inputs.shape[0]
    head_slots = lax.axis_size("heads")
    total_prompts = prompts_here * head_slots
    key_piece = w_query.shape[3]
    value_slice = w_value.shape[4]
    tp_index = lax.axis_index("tp")
    slot_index = lax.axis_index("heads")
    local_rates = lax.dynamic_slice_in_dim(decay_rates, tp_index * heads_here, heads_here)
    local_lengths = lax.dynamic_slice_in_dim(
        prompt_lengths, slot_index * prompts_here, prompts_here
    )
    span_start = span_len * ((local_lengths - 1) // span_len)
    live_count = local_lengths - span_start
    tables = prefill_tables(key_width, span_len, local_rates, span_start, live_count)
    offsets = jnp.arange(span_len)
    positions = (span_start[:, None] + offsets[None, :]).astype(jnp.float32)
    keys = (
        rotate(key_span.astype(jnp.float32), positions[:, :, None]) * key_width ** (-0.5)
    ).astype(jnp.bfloat16)
    valid_rows = offsets[None, :] < live_count[:, None]
    remaining = (live_count[:, None] - 1 - offsets[None, :]).astype(jnp.float32)
    key_weight = jnp.where(
        valid_rows[:, :, None],
        jnp.exp(-local_rates[None, None, :] * jnp.maximum(remaining, 0.0)[:, :, None]),
        0.0,
    )
    weighted = (keys.astype(jnp.float32) * key_weight[..., None]).astype(jnp.bfloat16)
    update = jnp.einsum("bjhk,bjhv->bhkv", weighted, value_span, preferred_element_type=jnp.float32)
    kept_share = jnp.exp(-local_rates[None, :] * live_count[:, None].astype(jnp.float32))
    state_new = (kept_share[:, :, None, None] * prior_state.astype(jnp.float32) + update).astype(
        jnp.bfloat16
    )
    slots = head_slots
    flat_inputs = decode_inputs.reshape(step_total * total_prompts, model_width)
    query_part = jnp.dot(
        flat_inputs, w_query.reshape(model_width, key_piece), preferred_element_type=jnp.float32
    ).astype(jnp.bfloat16)
    key_part = jnp.dot(
        flat_inputs, w_key.reshape(model_width, key_piece), preferred_element_type=jnp.float32
    ).astype(jnp.bfloat16)
    value_dec = jnp.dot(
        flat_inputs,
        w_value.reshape(model_width, heads_here * value_slice),
        preferred_element_type=jnp.float32,
    ).astype(jnp.bfloat16)
    gate_values = jnp.dot(
        flat_inputs,
        w_gate.reshape(model_width, heads_here * value_slice),
        preferred_element_type=jnp.float32,
    )
    steps = jnp.arange(step_total)
    halfway = key_width // 2
    head_column = (slot_index * key_piece + jnp.arange(key_piece)) % key_width
    column_frequency = 10000.0 ** (-(head_column // 2).astype(jnp.float32) / halfway)
    dec_positions = (
        (prompt_lengths[None, :] + steps[:, None]).astype(jnp.float32).reshape(-1, 1)
    )
    dec_angles = dec_positions * column_frequency[None, :]
    dec_cosine = jnp.cos(dec_angles)
    dec_sine = jnp.where(head_column % 2 == 0, -1.0, 1.0)[None, :] * jnp.sin(dec_angles)
    lane = jnp.arange(key_piece)
    swap = (lane[:, None] == (lane[None, :] ^ 1)).astype(jnp.bfloat16)
    query_partner = jnp.dot(query_part, swap, preferred_element_type=jnp.float32)
    key_partner = jnp.dot(key_part, swap, preferred_element_type=jnp.float32)
    query_turned = (
        query_part.astype(jnp.float32) * dec_cosine + query_partner * dec_sine
    ).astype(jnp.bfloat16)
    key_turned = (
        (key_part.astype(jnp.float32) * dec_cosine + key_partner * dec_sine)
        * key_width ** (-0.5)
    ).astype(jnp.bfloat16)
    packed = jnp.concatenate([query_turned, key_turned, value_dec], -1)
    packed = packed.reshape(step_total, slots, prompts_here, -1).transpose(1, 0, 2, 3)
    arrived = lax.all_to_all(packed, "heads", 0, 0, tiled=True)
    query_rot = (
        arrived[..., :key_piece]
        .transpose(1, 2, 0, 3)
        .reshape(step_total, prompts_here, heads_here, key_width)
    )
    key_rot = (
        arrived[..., key_piece : 2 * key_piece]
        .transpose(1, 2, 0, 3)
        .reshape(step_total, prompts_here, heads_here, key_width)
    )
    value_own = (
        arrived[..., 2 * key_piece :]
        .reshape(slots, step_total, prompts_here, heads_here, value_slice)
        .transpose(1, 2, 3, 0, 4)
        .reshape(step_total, prompts_here, heads_here, value_width)
    )
    from_state = jnp.einsum(
        "tbhk,bhkv->tbhv", query_rot, state_new, preferred_element_type=jnp.float32
    )
    step_gap = (steps[:, None] - steps[None, :]).astype(jnp.float32)
    step_decay = jnp.where(
        step_gap[None] >= 0,
        jnp.exp(-local_rates[:, None, None] * jnp.maximum(step_gap, 0.0)[None]),
        0.0,
    )
    step_scores = jnp.einsum(
        "tbhk,ubhk->bhtu", query_rot, key_rot, preferred_element_type=jnp.float32
    )
    from_steps = jnp.einsum(
        "bhtu,ubhv->tbhv",
        step_scores * step_decay[None],
        value_own.astype(jnp.float32),
        precision=lax.Precision.HIGHEST,
    )
    state_decay = jnp.exp(-local_rates[None, :] * (steps[:, None] + 1).astype(jnp.float32))
    readout = state_decay[:, None, :, None] * from_state + from_steps
    read_mean = jnp.mean(readout, -1, keepdims=True)
    read_square = jnp.mean(readout * readout, -1, keepdims=True)
    normed = norm_with(readout, read_mean, read_square)
    normed = normed.reshape(step_total, prompts_here, heads_here, slots, value_slice)
    normed = normed.transpose(3, 0, 1, 2, 4)
    normed = lax.all_to_all(normed, "heads", 0, 0, tiled=True)
    normed = normed.transpose(1, 0, 2, 3, 4).reshape(
        step_total, total_prompts, heads_here, value_slice
    )
    gates_steps = gate_values.reshape(step_total, total_prompts, heads_here, value_slice)
    activated = (
        (jax.nn.silu(gates_steps) * normed)
        .astype(jnp.bfloat16)
        .reshape(-1, heads_here * value_slice)
    )
    partial_out = jnp.dot(
        activated,
        w_out.reshape(heads_here * value_slice, model_width),
        preferred_element_type=jnp.float32,
    )
    partial_out = partial_out.reshape(step_total, total_prompts, model_width)
    query_span, key_span, value_span, prior_state, _ = lax.optimization_barrier(
        (query_span, key_span, value_span, prior_state, partial_out)
    )
    prefill_out = prefill_output(
        query_span, key_span, value_span, prior_state, local_rates, tables
    )
    out_slots = head_slots * lax.axis_size("tp")
    column_block = model_width // out_slots
    pieces = partial_out.reshape(step_total, total_prompts, out_slots, column_block)
    pieces = lax.all_to_all(pieces.transpose(2, 0, 1, 3), ("heads", "tp"), 0, 0, tiled=True)
    decode_out = jnp.sum(pieces, 0).astype(jnp.bfloat16)
    return (prefill_out, decode_out)


def solution(mesh):
    placed = (
        P(("groups", "heads"), None, "tp", None),
        P(("groups", "heads"), None, "tp", None),
        P(("groups", "heads"), None, "tp", None),
        P(("groups", "heads"), "tp", None, None),
        P(),
        P("groups"),
        P(None, "groups", None),
        P(None, "tp", "heads", None),
        P(None, "tp", "heads", None),
        P(None, "tp", None, "heads", None),
        P(None, "tp", None, "heads", None),
        P("tp", None, "heads", None, None),
    )
    return jax.shard_map(
        per_device,
        mesh=mesh,
        in_specs=placed,
        out_specs=(P(("groups", "heads"), None, "tp", None), P(None, "groups", ("heads", "tp"))),
        check_vma=False,
    )
```

```python
import jax
import jax.numpy as jnp
from jax import lax
from jax.experimental import pallas as pl
from jax.experimental.pallas import tpu as pltpu
from jax.sharding import PartitionSpec as P

EPSILON = 1e-05


def rotate(values, positions):
    halfway = values.shape[-1] // 2
    frequency = 10000.0 ** (-jnp.arange(halfway).astype(jnp.float32) / halfway)
    angles = positions[..., None] * frequency
    cosine = jnp.cos(angles)
    sine_part = jnp.sin(angles)
    paired = values.reshape(values.shape[:-1] + (halfway, 2))
    even_part = paired[..., 0]
    odd_part = paired[..., 1]
    turned = jnp.stack(
        [even_part * cosine - odd_part * sine_part, odd_part * cosine + even_part * sine_part], -1
    )
    return turned.reshape(values.shape)


def norm_with(output, mean_value, mean_square):
    return (output - mean_value) * lax.rsqrt(mean_square - mean_value * mean_value + EPSILON)


def turn_lanes(raw, swap, cosine, sine_part):
    partner = jnp.dot(raw, swap, preferred_element_type=jnp.float32)
    return raw.astype(jnp.float32) * cosine + partner * sine_part


def output_kernel(
    q_ref, k_ref, v_ref, prior_ref, cos_ref, sin_ref, swap_ref, table_ref, rows_ref, out_ref
):
    swap = swap_ref[...]
    cosine = cos_ref[...]
    sine_part = sin_ref[...]
    for head in range(q_ref.shape[1]):
        q_raw = q_ref[:, head, :]
        k_raw = k_ref[:, head, :]
        queries = turn_lanes(q_raw, swap, cosine, sine_part).astype(jnp.bfloat16)
        keys = (turn_lanes(k_raw, swap, cosine, sine_part) * (k_raw.shape[-1] ** (-0.5))).astype(
            jnp.bfloat16
        )
        rows = rows_ref[head]
        scores = lax.dot_general(
            queries, keys, (((1,), (1,)), ((), ())), preferred_element_type=jnp.float32
        )
        weights = (scores * table_ref[head]).astype(jnp.bfloat16)
        inner = jnp.dot(weights, v_ref[:, head, :], preferred_element_type=jnp.float32)
        carried = jnp.dot(queries, prior_ref[head], preferred_element_type=jnp.float32)
        mixed = inner + rows[:, 0:1] * carried
        mean_value = jnp.mean(mixed, -1, keepdims=True)
        mean_square = jnp.mean(mixed * mixed, -1, keepdims=True)
        normed = norm_with(mixed, mean_value, mean_square)
        out_ref[:, head, :] = jnp.where(rows[:, 1:2] > 0.5, normed, 0.0).astype(out_ref.dtype)


def prefill_tables(key_width, span_len, local_rates, span_start, live_count):
    halfway = key_width // 2
    offsets = jnp.arange(span_len)
    positions = (span_start[:, None] + offsets[None, :]).astype(jnp.float32)
    frequency = 10000.0 ** (-jnp.arange(halfway).astype(jnp.float32) / halfway)
    angles = positions[..., None] * frequency
    cosine = jnp.repeat(jnp.cos(angles), 2, axis=-1)
    sine_part = jnp.sin(angles)
    sine_part = jnp.stack([-sine_part, sine_part], -1).reshape(cosine.shape)
    lane = jnp.arange(key_width)
    swap = (lane[:, None] == (lane[None, :] ^ 1)).astype(jnp.bfloat16)
    valid_rows = offsets[None, :] < live_count[:, None]
    lead_decay = jnp.exp(-local_rates[:, None] * (offsets[None, :] + 1).astype(jnp.float32))
    remaining = (live_count[:, None] - 1 - offsets[None, :]).astype(jnp.float32)
    key_weight = jnp.where(
        valid_rows[:, None, :],
        jnp.exp(-local_rates[None, :, None] * jnp.maximum(remaining, 0.0)[:, None, :]),
        0.0,
    )
    kept_share = jnp.exp(-local_rates[None, :] * live_count[:, None].astype(jnp.float32))
    shape_rows = key_weight.shape
    rows = jnp.stack(
        [
            jnp.broadcast_to(lead_decay[None], shape_rows),
            jnp.broadcast_to(valid_rows[:, None, :].astype(jnp.float32), shape_rows),
            key_weight,
            jnp.broadcast_to(kept_share[:, :, None], shape_rows),
        ]
        + [jnp.zeros(shape_rows, jnp.float32)] * 4,
        -1,
    )
    return cosine, sine_part, swap, rows, valid_rows


def prefill_output(query_span, key_span, value_span, prior_state, local_rates, tables):
    prompts_here, span_len, heads_here, key_width = query_span.shape
    value_width = value_span.shape[3]
    cosine, sine_part, swap, rows, valid_rows = tables
    offsets = jnp.arange(span_len)
    distance = (offsets[:, None] - offsets[None, :]).astype(jnp.float32)
    decay_table = jnp.where(
        distance[None] >= 0,
        jnp.exp(-local_rates[:, None, None] * jnp.maximum(distance, 0.0)[None]),
        0.0,
    )
    table = jnp.where(valid_rows[:, None, None, :], decay_table[None], 0.0)
    return pl.pallas_call(
        output_kernel,
        grid=(prompts_here,),
        in_specs=[
            pl.BlockSpec((None, span_len, heads_here, key_width), lambda b: (b, 0, 0, 0)),
            pl.BlockSpec((None, span_len, heads_here, key_width), lambda b: (b, 0, 0, 0)),
            pl.BlockSpec((None, span_len, heads_here, value_width), lambda b: (b, 0, 0, 0)),
            pl.BlockSpec((None, heads_here, key_width, value_width), lambda b: (b, 0, 0, 0)),
            pl.BlockSpec((None, span_len, key_width), lambda b: (b, 0, 0)),
            pl.BlockSpec((None, span_len, key_width), lambda b: (b, 0, 0)),
            pl.BlockSpec((key_width, key_width), lambda b: (0, 0)),
            pl.BlockSpec((None, heads_here, span_len, span_len), lambda b: (b, 0, 0, 0)),
            pl.BlockSpec((None, heads_here, span_len, 8), lambda b: (b, 0, 0, 0)),
        ],
        out_specs=pl.BlockSpec(
            (None, span_len, heads_here, value_width), lambda b: (b, 0, 0, 0)
        ),
        out_shape=jax.ShapeDtypeStruct(value_span.shape, jnp.bfloat16),
    )(query_span, key_span, value_span, prior_state, cosine, sine_part, swap, table, rows)


def per_device(
    query_span,
    key_span,
    value_span,
    prior_state,
    decay_rates,
    prompt_lengths,
    decode_inputs,
    w_query,
    w_key,
    w_value,
    w_gate,
    w_out,
):
    prompts_here, span_len, heads_here, key_width = query_span.shape
    value_width = value_span.shape[3]
    model_width = decode_inputs.shape[2]
    step_total = decode_inputs.shape[0]
    head_slots = lax.axis_size("heads")
    total_prompts = prompts_here * head_slots
    key_piece = w_query.shape[3]
    value_slice = w_value.shape[4]
    tp_index = lax.axis_index("tp")
    slot_index = lax.axis_index("heads")
    local_rates = lax.dynamic_slice_in_dim(decay_rates, tp_index * heads_here, heads_here)
    local_lengths = lax.dynamic_slice_in_dim(
        prompt_lengths, slot_index * prompts_here, prompts_here
    )
    span_start = span_len * ((local_lengths - 1) // span_len)
    live_count = local_lengths - span_start
    tables = prefill_tables(key_width, span_len, local_rates, span_start, live_count)
    offsets = jnp.arange(span_len)
    positions = (span_start[:, None] + offsets[None, :]).astype(jnp.float32)
    keys = (
        rotate(key_span.astype(jnp.float32), positions[:, :, None]) * key_width ** (-0.5)
    ).astype(jnp.bfloat16)
    valid_rows = offsets[None, :] < live_count[:, None]
    remaining = (live_count[:, None] - 1 - offsets[None, :]).astype(jnp.float32)
    key_weight = jnp.where(
        valid_rows[:, :, None],
        jnp.exp(-local_rates[None, None, :] * jnp.maximum(remaining, 0.0)[:, :, None]),
        0.0,
    )
    weighted = (keys.astype(jnp.float32) * key_weight[..., None]).astype(jnp.bfloat16)
    update = jnp.einsum("bjhk,bjhv->bhkv", weighted, value_span, preferred_element_type=jnp.float32)
    kept_share = jnp.exp(-local_rates[None, :] * live_count[:, None].astype(jnp.float32))
    state_new = (kept_share[:, :, None, None] * prior_state.astype(jnp.float32) + update).astype(
        jnp.bfloat16
    )
    slots = head_slots
    flat_inputs = decode_inputs.reshape(step_total * total_prompts, model_width)
    query_part = jnp.dot(
        flat_inputs, w_query.reshape(model_width, key_piece), preferred_element_type=jnp.float32
    ).astype(jnp.bfloat16)
    key_part = jnp.dot(
        flat_inputs, w_key.reshape(model_width, key_piece), preferred_element_type=jnp.float32
    ).astype(jnp.bfloat16)
    value_dec = jnp.dot(
        flat_inputs,
        w_value.reshape(model_width, heads_here * value_slice),
        preferred_element_type=jnp.float32,
    ).astype(jnp.bfloat16)
    gate_values = jnp.dot(
        flat_inputs,
        w_gate.reshape(model_width, heads_here * value_slice),
        preferred_element_type=jnp.float32,
    )
    steps = jnp.arange(step_total)
    halfway = key_width // 2
    head_column = (slot_index * key_piece + jnp.arange(key_piece)) % key_width
    column_frequency = 10000.0 ** (-(head_column // 2).astype(jnp.float32) / halfway)
    dec_positions = (
        (prompt_lengths[None, :] + steps[:, None]).astype(jnp.float32).reshape(-1, 1)
    )
    dec_angles = dec_positions * column_frequency[None, :]
    dec_cosine = jnp.cos(dec_angles)
    dec_sine = jnp.where(head_column % 2 == 0, -1.0, 1.0)[None, :] * jnp.sin(dec_angles)
    lane = jnp.arange(key_piece)
    swap = (lane[:, None] == (lane[None, :] ^ 1)).astype(jnp.bfloat16)
    query_partner = jnp.dot(query_part, swap, preferred_element_type=jnp.float32)
    key_partner = jnp.dot(key_part, swap, preferred_element_type=jnp.float32)
    query_turned = (
        query_part.astype(jnp.float32) * dec_cosine + query_partner * dec_sine
    ).astype(jnp.bfloat16)
    key_turned = (
        (key_part.astype(jnp.float32) * dec_cosine + key_partner * dec_sine)
        * key_width ** (-0.5)
    ).astype(jnp.bfloat16)
    packed = jnp.concatenate([query_turned, key_turned, value_dec], -1)
    packed = packed.reshape(step_total, slots, prompts_here, -1).transpose(1, 0, 2, 3)
    arrived = lax.all_to_all(packed, "heads", 0, 0, tiled=True)
    query_rot = (
        arrived[..., :key_piece]
        .transpose(1, 2, 0, 3)
        .reshape(step_total, prompts_here, heads_here, key_width)
    )
    key_rot = (
        arrived[..., key_piece : 2 * key_piece]
        .transpose(1, 2, 0, 3)
        .reshape(step_total, prompts_here, heads_here, key_width)
    )
    value_own = (
        arrived[..., 2 * key_piece :]
        .reshape(slots, step_total, prompts_here, heads_here, value_slice)
        .transpose(1, 2, 3, 0, 4)
        .reshape(step_total, prompts_here, heads_here, value_width)
    )
    from_state = jnp.einsum(
        "tbhk,bhkv->tbhv", query_rot, state_new, preferred_element_type=jnp.float32
    )
    step_gap = (steps[:, None] - steps[None, :]).astype(jnp.float32)
    step_decay = jnp.where(
        step_gap[None] >= 0,
        jnp.exp(-local_rates[:, None, None] * jnp.maximum(step_gap, 0.0)[None]),
        0.0,
    )
    step_scores = jnp.einsum(
        "tbhk,ubhk->bhtu", query_rot, key_rot, preferred_element_type=jnp.float32
    )
    from_steps = jnp.einsum(
        "bhtu,ubhv->tbhv",
        step_scores * step_decay[None],
        value_own.astype(jnp.float32),
        precision=lax.Precision.HIGHEST,
    )
    state_decay = jnp.exp(-local_rates[None, :] * (steps[:, None] + 1).astype(jnp.float32))
    readout = state_decay[:, None, :, None] * from_state + from_steps
    read_mean = jnp.mean(readout, -1, keepdims=True)
    read_square = jnp.mean(readout * readout, -1, keepdims=True)
    normed = norm_with(readout, read_mean, read_square)
    normed = normed.reshape(step_total, prompts_here, heads_here, slots, value_slice)
    normed = normed.transpose(3, 0, 1, 2, 4)
    normed = lax.all_to_all(normed, "heads", 0, 0, tiled=True)
    normed = normed.transpose(1, 0, 2, 3, 4).reshape(
        step_total, total_prompts, heads_here, value_slice
    )
    gates_steps = gate_values.reshape(step_total, total_prompts, heads_here, value_slice)
    activated = (
        (jax.nn.silu(gates_steps) * normed)
        .astype(jnp.bfloat16)
        .reshape(-1, heads_here * value_slice)
    )
    partial_out = jnp.dot(
        activated,
        w_out.reshape(heads_here * value_slice, model_width),
        preferred_element_type=jnp.float32,
    )
    partial_out = partial_out.reshape(step_total, total_prompts, model_width)
    query_span, key_span, value_span, prior_state, partial_out = lax.optimization_barrier(
        (query_span, key_span, value_span, prior_state, partial_out)
    )
    prefill_out = prefill_output(
        query_span, key_span, value_span, prior_state, local_rates, tables
    )
    out_slots = head_slots * lax.axis_size("tp")
    column_block = model_width // out_slots
    pieces = partial_out.reshape(step_total, total_prompts, out_slots, column_block)
    pieces = lax.all_to_all(pieces, ("heads", "tp"), 2, 2, tiled=True)
    decode_out = jnp.sum(pieces, 2).astype(jnp.bfloat16)
    return (prefill_out, decode_out)


def solution(mesh):
    placed = (
        P(("groups", "heads"), None, "tp", None),
        P(("groups", "heads"), None, "tp", None),
        P(("groups", "heads"), None, "tp", None),
        P(("groups", "heads"), "tp", None, None),
        P(),
        P("groups"),
        P(None, "groups", None),
        P(None, "tp", "heads", None),
        P(None, "tp", "heads", None),
        P(None, "tp", None, "heads", None),
        P(None, "tp", None, "heads", None),
        P("tp", None, "heads", None, None),
    )
    return jax.shard_map(
        per_device,
        mesh=mesh,
        in_specs=placed,
        out_specs=(P(("groups", "heads"), None, "tp", None), P(None, "groups", ("heads", "tp"))),
        check_vma=False,
    )
```

```python
import jax
import jax.numpy as jnp
from jax import lax
from jax.experimental import pallas as pl
from jax.experimental.pallas import tpu as pltpu
from jax.sharding import PartitionSpec as P

EPSILON = 1e-05


def rotate(values, positions):
    halfway = values.shape[-1] // 2
    frequency = 10000.0 ** (-jnp.arange(halfway).astype(jnp.float32) / halfway)
    angles = positions[..., None] * frequency
    cosine = jnp.cos(angles)
    sine_part = jnp.sin(angles)
    paired = values.reshape(values.shape[:-1] + (halfway, 2))
    even_part = paired[..., 0]
    odd_part = paired[..., 1]
    turned = jnp.stack(
        [even_part * cosine - odd_part * sine_part, odd_part * cosine + even_part * sine_part], -1
    )
    return turned.reshape(values.shape)


def norm_with(output, mean_value, mean_square):
    return (output - mean_value) * lax.rsqrt(mean_square - mean_value * mean_value + EPSILON)


def turn_lanes(raw, swap, cosine, sine_part):
    partner = jnp.dot(raw, swap, preferred_element_type=jnp.float32)
    return raw.astype(jnp.float32) * cosine + partner * sine_part


def output_kernel(
    q_ref, k_ref, v_ref, prior_ref, cos_ref, sin_ref, swap_ref, table_ref, rows_ref, out_ref
):
    swap = swap_ref[...]
    cosine = cos_ref[...]
    sine_part = sin_ref[...]
    for head in range(q_ref.shape[1]):
        q_raw = q_ref[:, head, :]
        k_raw = k_ref[:, head, :]
        queries = turn_lanes(q_raw, swap, cosine, sine_part).astype(jnp.bfloat16)
        keys = (turn_lanes(k_raw, swap, cosine, sine_part) * (k_raw.shape[-1] ** (-0.5))).astype(
            jnp.bfloat16
        )
        rows = rows_ref[head]
        scores = lax.dot_general(
            queries, keys, (((1,), (1,)), ((), ())), preferred_element_type=jnp.float32
        )
        weights = (scores * table_ref[head]).astype(jnp.bfloat16)
        inner = jnp.dot(weights, v_ref[:, head, :], preferred_element_type=jnp.float32)
        carried = jnp.dot(queries, prior_ref[head], preferred_element_type=jnp.float32)
        mixed = inner + rows[:, 0:1] * carried
        mean_value = jnp.mean(mixed, -1, keepdims=True)
        mean_square = jnp.mean(mixed * mixed, -1, keepdims=True)
        normed = norm_with(mixed, mean_value, mean_square)
        out_ref[:, head, :] = jnp.where(rows[:, 1:2] > 0.5, normed, 0.0).astype(out_ref.dtype)


def prefill_tables(key_width, span_len, local_rates, span_start, live_count):
    halfway = key_width // 2
    offsets = jnp.arange(span_len)
    positions = (span_start[:, None] + offsets[None, :]).astype(jnp.float32)
    frequency = 10000.0 ** (-jnp.arange(halfway).astype(jnp.float32) / halfway)
    angles = positions[..., None] * frequency
    cosine = jnp.repeat(jnp.cos(angles), 2, axis=-1)
    sine_part = jnp.sin(angles)
    sine_part = jnp.stack([-sine_part, sine_part], -1).reshape(cosine.shape)
    lane = jnp.arange(key_width)
    swap = (lane[:, None] == (lane[None, :] ^ 1)).astype(jnp.bfloat16)
    valid_rows = offsets[None, :] < live_count[:, None]
    lead_decay = jnp.exp(-local_rates[:, None] * (offsets[None, :] + 1).astype(jnp.float32))
    remaining = (live_count[:, None] - 1 - offsets[None, :]).astype(jnp.float32)
    key_weight = jnp.where(
        valid_rows[:, None, :],
        jnp.exp(-local_rates[None, :, None] * jnp.maximum(remaining, 0.0)[:, None, :]),
        0.0,
    )
    kept_share = jnp.exp(-local_rates[None, :] * live_count[:, None].astype(jnp.float32))
    shape_rows = key_weight.shape
    rows = jnp.stack(
        [
            jnp.broadcast_to(lead_decay[None], shape_rows),
            jnp.broadcast_to(valid_rows[:, None, :].astype(jnp.float32), shape_rows),
            key_weight,
            jnp.broadcast_to(kept_share[:, :, None], shape_rows),
        ]
        + [jnp.zeros(shape_rows, jnp.float32)] * 4,
        -1,
    )
    return cosine, sine_part, swap, rows, valid_rows


def prefill_output(
    query_span, key_span, value_span, prior_state, local_rates, tables, first, count, earlier
):
    prompts_here, span_len, heads_here, key_width = query_span.shape
    value_width = value_span.shape[3]
    cosine, sine_part, swap, rows, valid_rows = tables
    offsets = jnp.arange(span_len)
    distance = (offsets[:, None] - offsets[None, :]).astype(jnp.float32)
    decay_table = jnp.where(
        distance[None] >= 0,
        jnp.exp(-local_rates[:, None, None] * jnp.maximum(distance, 0.0)[None]),
        0.0,
    )
    table = jnp.where(valid_rows[:, None, None, :], decay_table[None], 0.0)
    def pick(*shape_tail):
        return lambda i: (first + i,) + (0,) * len(shape_tail)

    in_specs = [
        pl.BlockSpec((None, span_len, heads_here, key_width), pick(0, 0, 0)),
        pl.BlockSpec((None, span_len, heads_here, key_width), pick(0, 0, 0)),
        pl.BlockSpec((None, span_len, heads_here, value_width), pick(0, 0, 0)),
        pl.BlockSpec((None, heads_here, key_width, value_width), pick(0, 0, 0)),
        pl.BlockSpec((None, span_len, key_width), pick(0, 0)),
        pl.BlockSpec((None, span_len, key_width), pick(0, 0)),
        pl.BlockSpec((key_width, key_width), lambda i: (0, 0)),
        pl.BlockSpec((None, heads_here, span_len, span_len), pick(0, 0, 0)),
        pl.BlockSpec((None, heads_here, span_len, 8), pick(0, 0, 0)),
    ]
    operands = [query_span, key_span, value_span, prior_state, cosine, sine_part, swap, table, rows]
    kernel = output_kernel
    aliases = {}
    if earlier is not None:
        in_specs.append(pl.BlockSpec(memory_space=pl.ANY))
        operands.append(earlier)
        aliases = {len(operands) - 1: 0}

        def kernel(*refs):
            output_kernel(*refs[:9], refs[10])

    return pl.pallas_call(
        kernel,
        grid=(count,),
        in_specs=in_specs,
        out_specs=pl.BlockSpec((None, span_len, heads_here, value_width), pick(0, 0, 0)),
        out_shape=jax.ShapeDtypeStruct(value_span.shape, jnp.bfloat16),
        input_output_aliases=aliases,
    )(*operands)


def per_device(
    query_span,
    key_span,
    value_span,
    prior_state,
    decay_rates,
    prompt_lengths,
    decode_inputs,
    w_query,
    w_key,
    w_value,
    w_gate,
    w_out,
):
    prompts_here, span_len, heads_here, key_width = query_span.shape
    value_width = value_span.shape[3]
    model_width = decode_inputs.shape[2]
    step_total = decode_inputs.shape[0]
    head_slots = lax.axis_size("heads")
    total_prompts = prompts_here * head_slots
    key_piece = w_query.shape[3]
    value_slice = w_value.shape[4]
    tp_index = lax.axis_index("tp")
    slot_index = lax.axis_index("heads")
    local_rates = lax.dynamic_slice_in_dim(decay_rates, tp_index * heads_here, heads_here)
    local_lengths = lax.dynamic_slice_in_dim(
        prompt_lengths, slot_index * prompts_here, prompts_here
    )
    span_start = span_len * ((local_lengths - 1) // span_len)
    live_count = local_lengths - span_start
    tables = prefill_tables(key_width, span_len, local_rates, span_start, live_count)
    offsets = jnp.arange(span_len)
    positions = (span_start[:, None] + offsets[None, :]).astype(jnp.float32)
    keys = (
        rotate(key_span.astype(jnp.float32), positions[:, :, None]) * key_width ** (-0.5)
    ).astype(jnp.bfloat16)
    valid_rows = offsets[None, :] < live_count[:, None]
    remaining = (live_count[:, None] - 1 - offsets[None, :]).astype(jnp.float32)
    key_weight = jnp.where(
        valid_rows[:, :, None],
        jnp.exp(-local_rates[None, None, :] * jnp.maximum(remaining, 0.0)[:, :, None]),
        0.0,
    )
    weighted = (keys.astype(jnp.float32) * key_weight[..., None]).astype(jnp.bfloat16)
    update = jnp.einsum("bjhk,bjhv->bhkv", weighted, value_span, preferred_element_type=jnp.float32)
    kept_share = jnp.exp(-local_rates[None, :] * live_count[:, None].astype(jnp.float32))
    state_new = (kept_share[:, :, None, None] * prior_state.astype(jnp.float32) + update).astype(
        jnp.bfloat16
    )
    slots = head_slots
    flat_inputs = decode_inputs.reshape(step_total * total_prompts, model_width)
    query_part = jnp.dot(
        flat_inputs, w_query.reshape(model_width, key_piece), preferred_element_type=jnp.float32
    ).astype(jnp.bfloat16)
    key_part = jnp.dot(
        flat_inputs, w_key.reshape(model_width, key_piece), preferred_element_type=jnp.float32
    ).astype(jnp.bfloat16)
    value_dec = jnp.dot(
        flat_inputs,
        w_value.reshape(model_width, heads_here * value_slice),
        preferred_element_type=jnp.float32,
    ).astype(jnp.bfloat16)
    gate_values = jnp.dot(
        flat_inputs,
        w_gate.reshape(model_width, heads_here * value_slice),
        preferred_element_type=jnp.float32,
    )
    steps = jnp.arange(step_total)
    halfway = key_width // 2
    head_column = (slot_index * key_piece + jnp.arange(key_piece)) % key_width
    column_frequency = 10000.0 ** (-(head_column // 2).astype(jnp.float32) / halfway)
    dec_positions = (
        (prompt_lengths[None, :] + steps[:, None]).astype(jnp.float32).reshape(-1, 1)
    )
    dec_angles = dec_positions * column_frequency[None, :]
    dec_cosine = jnp.cos(dec_angles)
    dec_sine = jnp.where(head_column % 2 == 0, -1.0, 1.0)[None, :] * jnp.sin(dec_angles)
    lane = jnp.arange(key_piece)
    swap = (lane[:, None] == (lane[None, :] ^ 1)).astype(jnp.bfloat16)
    query_partner = jnp.dot(query_part, swap, preferred_element_type=jnp.float32)
    key_partner = jnp.dot(key_part, swap, preferred_element_type=jnp.float32)
    query_turned = (
        query_part.astype(jnp.float32) * dec_cosine + query_partner * dec_sine
    ).astype(jnp.bfloat16)
    key_turned = (
        (key_part.astype(jnp.float32) * dec_cosine + key_partner * dec_sine)
        * key_width ** (-0.5)
    ).astype(jnp.bfloat16)
    packed = jnp.concatenate([query_turned, key_turned, value_dec], -1)
    packed = packed.reshape(step_total, slots, prompts_here, -1).transpose(1, 0, 2, 3)
    arrived = lax.all_to_all(packed, "heads", 0, 0, tiled=True)
    query_rot = (
        arrived[..., :key_piece]
        .transpose(1, 2, 0, 3)
        .reshape(step_total, prompts_here, heads_here, key_width)
    )
    key_rot = (
        arrived[..., key_piece : 2 * key_piece]
        .transpose(1, 2, 0, 3)
        .reshape(step_total, prompts_here, heads_here, key_width)
    )
    value_own = (
        arrived[..., 2 * key_piece :]
        .reshape(slots, step_total, prompts_here, heads_here, value_slice)
        .transpose(1, 2, 3, 0, 4)
        .reshape(step_total, prompts_here, heads_here, value_width)
    )
    from_state = jnp.einsum(
        "tbhk,bhkv->tbhv", query_rot, state_new, preferred_element_type=jnp.float32
    )
    step_gap = (steps[:, None] - steps[None, :]).astype(jnp.float32)
    step_decay = jnp.where(
        step_gap[None] >= 0,
        jnp.exp(-local_rates[:, None, None] * jnp.maximum(step_gap, 0.0)[None]),
        0.0,
    )
    step_scores = jnp.einsum(
        "tbhk,ubhk->bhtu", query_rot, key_rot, preferred_element_type=jnp.float32
    )
    from_steps = jnp.einsum(
        "bhtu,ubhv->tbhv",
        step_scores * step_decay[None],
        value_own.astype(jnp.float32),
        precision=lax.Precision.HIGHEST,
    )
    state_decay = jnp.exp(-local_rates[None, :] * (steps[:, None] + 1).astype(jnp.float32))
    readout = state_decay[:, None, :, None] * from_state + from_steps
    read_mean = jnp.mean(readout, -1, keepdims=True)
    read_square = jnp.mean(readout * readout, -1, keepdims=True)
    normed = norm_with(readout, read_mean, read_square)
    normed = normed.reshape(step_total, prompts_here, heads_here, slots, value_slice)
    normed = normed.transpose(3, 0, 1, 2, 4)
    first_half = prompts_here // 2
    q_early, k_early, v_early, prior_early, normed = lax.optimization_barrier(
        (query_span, key_span, value_span, prior_state, normed)
    )
    prefill_early = prefill_output(
        q_early, k_early, v_early, prior_early, local_rates, tables, 0, first_half, None
    )
    normed = lax.all_to_all(normed, "heads", 0, 0, tiled=True)
    normed, prefill_early = lax.optimization_barrier((normed, prefill_early))
    normed = normed.transpose(1, 0, 2, 3, 4).reshape(
        step_total, total_prompts, heads_here, value_slice
    )
    gates_steps = gate_values.reshape(step_total, total_prompts, heads_here, value_slice)
    activated = (
        (jax.nn.silu(gates_steps) * normed)
        .astype(jnp.bfloat16)
        .reshape(-1, heads_here * value_slice)
    )
    partial_out = jnp.dot(
        activated,
        w_out.reshape(heads_here * value_slice, model_width),
        preferred_element_type=jnp.float32,
    )
    partial_out = partial_out.reshape(step_total, total_prompts, model_width)
    query_span, key_span, value_span, prior_state, partial_out = lax.optimization_barrier(
        (query_span, key_span, value_span, prior_state, partial_out)
    )
    prefill_out = prefill_output(
        query_span, key_span, value_span, prior_state, local_rates, tables,
        first_half, prompts_here - first_half, prefill_early,
    )
    out_slots = head_slots * lax.axis_size("tp")
    column_block = model_width // out_slots
    pieces = partial_out.reshape(step_total, total_prompts, out_slots, column_block)
    pieces = lax.all_to_all(pieces, ("heads", "tp"), 2, 2, tiled=True)
    decode_out = jnp.sum(pieces, 2).astype(jnp.bfloat16)
    return (prefill_out, decode_out)


def solution(mesh):
    placed = (
        P(("groups", "heads"), None, "tp", None),
        P(("groups", "heads"), None, "tp", None),
        P(("groups", "heads"), None, "tp", None),
        P(("groups", "heads"), "tp", None, None),
        P(),
        P("groups"),
        P(None, "groups", None),
        P(None, "tp", "heads", None),
        P(None, "tp", "heads", None),
        P(None, "tp", None, "heads", None),
        P(None, "tp", None, "heads", None),
        P("tp", None, "heads", None, None),
    )
    return jax.shard_map(
        per_device,
        mesh=mesh,
        in_specs=placed,
        out_specs=(P(("groups", "heads"), None, "tp", None), P(None, "groups", ("heads", "tp"))),
        check_vma=False,
    )
```

```python
import jax
import jax.numpy as jnp
from jax import lax
from jax.experimental import pallas as pl
from jax.experimental.pallas import tpu as pltpu
from jax.sharding import PartitionSpec as P

EPSILON = 1e-05


def rotate(values, positions):
    halfway = values.shape[-1] // 2
    frequency = 10000.0 ** (-jnp.arange(halfway).astype(jnp.float32) / halfway)
    angles = positions[..., None] * frequency
    cosine = jnp.cos(angles)
    sine_part = jnp.sin(angles)
    paired = values.reshape(values.shape[:-1] + (halfway, 2))
    even_part = paired[..., 0]
    odd_part = paired[..., 1]
    turned = jnp.stack(
        [even_part * cosine - odd_part * sine_part, odd_part * cosine + even_part * sine_part], -1
    )
    return turned.reshape(values.shape)


def norm_with(output, mean_value, mean_square):
    return (output - mean_value) * lax.rsqrt(mean_square - mean_value * mean_value + EPSILON)


def turn_lanes(raw, swap, cosine, sine_part):
    partner = jnp.dot(raw, swap, preferred_element_type=jnp.float32)
    return raw.astype(jnp.float32) * cosine + partner * sine_part


def output_kernel(
    rates_ref, live_ref, q_ref, k_ref, v_ref, prior_ref, cos_ref, sin_ref, swap_ref, out_ref
):
    swap = swap_ref[...]
    cosine = cos_ref[...]
    sine_part = sin_ref[...]
    span_len = q_ref.shape[0]
    live = live_ref[pl.program_id(0)]
    row = lax.broadcasted_iota(jnp.int32, (span_len, span_len), 0)
    column = lax.broadcasted_iota(jnp.int32, (span_len, span_len), 1)
    distance = jnp.maximum(row - column, 0).astype(jnp.float32)
    keep = (row >= column) & (column < live)
    row_index = lax.broadcasted_iota(jnp.int32, (span_len, 1), 0)
    valid = row_index < live
    for head in range(q_ref.shape[1]):
        rate = rates_ref[head]
        q_raw = q_ref[:, head, :]
        k_raw = k_ref[:, head, :]
        queries = turn_lanes(q_raw, swap, cosine, sine_part).astype(jnp.bfloat16)
        keys = (turn_lanes(k_raw, swap, cosine, sine_part) * (k_raw.shape[-1] ** (-0.5))).astype(
            jnp.bfloat16
        )
        scores = lax.dot_general(
            queries, keys, (((1,), (1,)), ((), ())), preferred_element_type=jnp.float32
        )
        table = jnp.where(keep, jnp.exp(-rate * distance), 0.0)
        weights = (scores * table).astype(jnp.bfloat16)
        inner = jnp.dot(weights, v_ref[:, head, :], preferred_element_type=jnp.float32)
        carried = jnp.dot(queries, prior_ref[head], preferred_element_type=jnp.float32)
        lead = jnp.exp(-rate * (row_index + 1).astype(jnp.float32))
        mixed = inner + lead * carried
        mean_value = jnp.mean(mixed, -1, keepdims=True)
        mean_square = jnp.mean(mixed * mixed, -1, keepdims=True)
        normed = norm_with(mixed, mean_value, mean_square)
        out_ref[:, head, :] = jnp.where(valid, normed, 0.0).astype(out_ref.dtype)


def prefill_tables(key_width, span_len, local_rates, span_start, live_count):
    halfway = key_width // 2
    offsets = jnp.arange(span_len)
    positions = (span_start[:, None] + offsets[None, :]).astype(jnp.float32)
    frequency = 10000.0 ** (-jnp.arange(halfway).astype(jnp.float32) / halfway)
    angles = positions[..., None] * frequency
    cosine = jnp.repeat(jnp.cos(angles), 2, axis=-1)
    sine_part = jnp.sin(angles)
    sine_part = jnp.stack([-sine_part, sine_part], -1).reshape(cosine.shape)
    lane = jnp.arange(key_width)
    swap = (lane[:, None] == (lane[None, :] ^ 1)).astype(jnp.bfloat16)
    valid_rows = offsets[None, :] < live_count[:, None]
    lead_decay = jnp.exp(-local_rates[:, None] * (offsets[None, :] + 1).astype(jnp.float32))
    remaining = (live_count[:, None] - 1 - offsets[None, :]).astype(jnp.float32)
    key_weight = jnp.where(
        valid_rows[:, None, :],
        jnp.exp(-local_rates[None, :, None] * jnp.maximum(remaining, 0.0)[:, None, :]),
        0.0,
    )
    kept_share = jnp.exp(-local_rates[None, :] * live_count[:, None].astype(jnp.float32))
    shape_rows = key_weight.shape
    rows = jnp.stack(
        [
            jnp.broadcast_to(lead_decay[None], shape_rows),
            jnp.broadcast_to(valid_rows[:, None, :].astype(jnp.float32), shape_rows),
            key_weight,
            jnp.broadcast_to(kept_share[:, :, None], shape_rows),
        ]
        + [jnp.zeros(shape_rows, jnp.float32)] * 4,
        -1,
    )
    return cosine, sine_part, swap, rows, valid_rows


def prefill_output(query_span, key_span, value_span, prior_state, local_rates, tables, live_count):
    prompts_here, span_len, heads_here, key_width = query_span.shape
    value_width = value_span.shape[3]
    cosine, sine_part, swap, rows, valid_rows = tables
    whole = pl.BlockSpec(memory_space=pltpu.SMEM)
    return pl.pallas_call(
        output_kernel,
        grid=(prompts_here,),
        in_specs=[
            whole,
            whole,
            pl.BlockSpec((None, span_len, heads_here, key_width), lambda b: (b, 0, 0, 0)),
            pl.BlockSpec((None, span_len, heads_here, key_width), lambda b: (b, 0, 0, 0)),
            pl.BlockSpec((None, span_len, heads_here, value_width), lambda b: (b, 0, 0, 0)),
            pl.BlockSpec((None, heads_here, key_width, value_width), lambda b: (b, 0, 0, 0)),
            pl.BlockSpec((None, span_len, key_width), lambda b: (b, 0, 0)),
            pl.BlockSpec((None, span_len, key_width), lambda b: (b, 0, 0)),
            pl.BlockSpec((key_width, key_width), lambda b: (0, 0)),
        ],
        out_specs=pl.BlockSpec(
            (None, span_len, heads_here, value_width), lambda b: (b, 0, 0, 0)
        ),
        out_shape=jax.ShapeDtypeStruct(value_span.shape, jnp.bfloat16),
    )(
        local_rates, live_count.astype(jnp.int32), query_span, key_span, value_span,
        prior_state, cosine, sine_part, swap,
    )


def per_device(
    query_span,
    key_span,
    value_span,
    prior_state,
    decay_rates,
    prompt_lengths,
    decode_inputs,
    w_query,
    w_key,
    w_value,
    w_gate,
    w_out,
):
    prompts_here, span_len, heads_here, key_width = query_span.shape
    value_width = value_span.shape[3]
    model_width = decode_inputs.shape[2]
    step_total = decode_inputs.shape[0]
    head_slots = lax.axis_size("heads")
    total_prompts = prompts_here * head_slots
    key_piece = w_query.shape[3]
    value_slice = w_value.shape[4]
    tp_index = lax.axis_index("tp")
    slot_index = lax.axis_index("heads")
    local_rates = lax.dynamic_slice_in_dim(decay_rates, tp_index * heads_here, heads_here)
    local_lengths = lax.dynamic_slice_in_dim(
        prompt_lengths, slot_index * prompts_here, prompts_here
    )
    span_start = span_len * ((local_lengths - 1) // span_len)
    live_count = local_lengths - span_start
    tables = prefill_tables(key_width, span_len, local_rates, span_start, live_count)
    offsets = jnp.arange(span_len)
    positions = (span_start[:, None] + offsets[None, :]).astype(jnp.float32)
    keys = (
        rotate(key_span.astype(jnp.float32), positions[:, :, None]) * key_width ** (-0.5)
    ).astype(jnp.bfloat16)
    valid_rows = offsets[None, :] < live_count[:, None]
    remaining = (live_count[:, None] - 1 - offsets[None, :]).astype(jnp.float32)
    key_weight = jnp.where(
        valid_rows[:, :, None],
        jnp.exp(-local_rates[None, None, :] * jnp.maximum(remaining, 0.0)[:, :, None]),
        0.0,
    )
    weighted = (keys.astype(jnp.float32) * key_weight[..., None]).astype(jnp.bfloat16)
    update = jnp.einsum("bjhk,bjhv->bhkv", weighted, value_span, preferred_element_type=jnp.float32)
    kept_share = jnp.exp(-local_rates[None, :] * live_count[:, None].astype(jnp.float32))
    state_new = (kept_share[:, :, None, None] * prior_state.astype(jnp.float32) + update).astype(
        jnp.bfloat16
    )
    slots = head_slots
    flat_inputs = decode_inputs.reshape(step_total * total_prompts, model_width)
    query_part = jnp.dot(
        flat_inputs, w_query.reshape(model_width, key_piece), preferred_element_type=jnp.float32
    ).astype(jnp.bfloat16)
    key_part = jnp.dot(
        flat_inputs, w_key.reshape(model_width, key_piece), preferred_element_type=jnp.float32
    ).astype(jnp.bfloat16)
    value_dec = jnp.dot(
        flat_inputs,
        w_value.reshape(model_width, heads_here * value_slice),
        preferred_element_type=jnp.float32,
    ).astype(jnp.bfloat16)
    gate_values = jnp.dot(
        flat_inputs,
        w_gate.reshape(model_width, heads_here * value_slice),
        preferred_element_type=jnp.float32,
    )
    steps = jnp.arange(step_total)
    halfway = key_width // 2
    head_column = (slot_index * key_piece + jnp.arange(key_piece)) % key_width
    column_frequency = 10000.0 ** (-(head_column // 2).astype(jnp.float32) / halfway)
    dec_positions = (
        (prompt_lengths[None, :] + steps[:, None]).astype(jnp.float32).reshape(-1, 1)
    )
    dec_angles = dec_positions * column_frequency[None, :]
    dec_cosine = jnp.cos(dec_angles)
    dec_sine = jnp.where(head_column % 2 == 0, -1.0, 1.0)[None, :] * jnp.sin(dec_angles)
    lane = jnp.arange(key_piece)
    swap = (lane[:, None] == (lane[None, :] ^ 1)).astype(jnp.bfloat16)
    query_partner = jnp.dot(query_part, swap, preferred_element_type=jnp.float32)
    key_partner = jnp.dot(key_part, swap, preferred_element_type=jnp.float32)
    query_turned = (
        query_part.astype(jnp.float32) * dec_cosine + query_partner * dec_sine
    ).astype(jnp.bfloat16)
    key_turned = (
        (key_part.astype(jnp.float32) * dec_cosine + key_partner * dec_sine)
        * key_width ** (-0.5)
    ).astype(jnp.bfloat16)
    packed = jnp.concatenate([query_turned, key_turned, value_dec], -1)
    packed = packed.reshape(step_total, slots, prompts_here, -1).transpose(1, 0, 2, 3)
    arrived = lax.all_to_all(packed, "heads", 0, 0, tiled=True)
    query_rot = (
        arrived[..., :key_piece]
        .transpose(1, 2, 0, 3)
        .reshape(step_total, prompts_here, heads_here, key_width)
    )
    key_rot = (
        arrived[..., key_piece : 2 * key_piece]
        .transpose(1, 2, 0, 3)
        .reshape(step_total, prompts_here, heads_here, key_width)
    )
    value_own = (
        arrived[..., 2 * key_piece :]
        .reshape(slots, step_total, prompts_here, heads_here, value_slice)
        .transpose(1, 2, 3, 0, 4)
        .reshape(step_total, prompts_here, heads_here, value_width)
    )
    from_state = jnp.einsum(
        "tbhk,bhkv->tbhv", query_rot, state_new, preferred_element_type=jnp.float32
    )
    step_gap = (steps[:, None] - steps[None, :]).astype(jnp.float32)
    step_decay = jnp.where(
        step_gap[None] >= 0,
        jnp.exp(-local_rates[:, None, None] * jnp.maximum(step_gap, 0.0)[None]),
        0.0,
    )
    step_scores = jnp.einsum(
        "tbhk,ubhk->bhtu", query_rot, key_rot, preferred_element_type=jnp.float32
    )
    from_steps = jnp.einsum(
        "bhtu,ubhv->tbhv",
        step_scores * step_decay[None],
        value_own.astype(jnp.float32),
        precision=lax.Precision.HIGHEST,
    )
    state_decay = jnp.exp(-local_rates[None, :] * (steps[:, None] + 1).astype(jnp.float32))
    readout = state_decay[:, None, :, None] * from_state + from_steps
    read_mean = jnp.mean(readout, -1, keepdims=True)
    read_square = jnp.mean(readout * readout, -1, keepdims=True)
    normed = norm_with(readout, read_mean, read_square)
    normed = normed.reshape(step_total, prompts_here, heads_here, slots, value_slice)
    normed = normed.transpose(3, 0, 1, 2, 4)
    normed = lax.all_to_all(normed, "heads", 0, 0, tiled=True)
    normed = normed.transpose(1, 0, 2, 3, 4).reshape(
        step_total, total_prompts, heads_here, value_slice
    )
    gates_steps = gate_values.reshape(step_total, total_prompts, heads_here, value_slice)
    activated = (
        (jax.nn.silu(gates_steps) * normed)
        .astype(jnp.bfloat16)
        .reshape(-1, heads_here * value_slice)
    )
    partial_out = jnp.dot(
        activated,
        w_out.reshape(heads_here * value_slice, model_width),
        preferred_element_type=jnp.float32,
    )
    partial_out = partial_out.reshape(step_total, total_prompts, model_width)
    query_span, key_span, value_span, prior_state, partial_out = lax.optimization_barrier(
        (query_span, key_span, value_span, prior_state, partial_out)
    )
    prefill_out = prefill_output(
        query_span, key_span, value_span, prior_state, local_rates, tables, live_count
    )
    out_slots = head_slots * lax.axis_size("tp")
    column_block = model_width // out_slots
    pieces = partial_out.reshape(step_total, total_prompts, out_slots, column_block)
    pieces = lax.all_to_all(pieces, ("heads", "tp"), 2, 2, tiled=True)
    decode_out = jnp.sum(pieces, 2).astype(jnp.bfloat16)
    return (prefill_out, decode_out)


def solution(mesh):
    placed = (
        P(("groups", "heads"), None, "tp", None),
        P(("groups", "heads"), None, "tp", None),
        P(("groups", "heads"), None, "tp", None),
        P(("groups", "heads"), "tp", None, None),
        P(),
        P("groups"),
        P(None, "groups", None),
        P(None, "tp", "heads", None),
        P(None, "tp", "heads", None),
        P(None, "tp", None, "heads", None),
        P(None, "tp", None, "heads", None),
        P("tp", None, "heads", None, None),
    )
    return jax.shard_map(
        per_device,
        mesh=mesh,
        in_specs=placed,
        out_specs=(P(("groups", "heads"), None, "tp", None), P(None, "groups", ("heads", "tp"))),
        check_vma=False,
    )
```

```python
import jax
import jax.numpy as jnp
from jax import lax
from jax.experimental import pallas as pl
from jax.experimental.pallas import tpu as pltpu
from jax.sharding import PartitionSpec as P

EPSILON = 1e-05


def rotate(values, positions):
    halfway = values.shape[-1] // 2
    frequency = 10000.0 ** (-jnp.arange(halfway).astype(jnp.float32) / halfway)
    angles = positions[..., None] * frequency
    cosine = jnp.cos(angles)
    sine_part = jnp.sin(angles)
    paired = values.reshape(values.shape[:-1] + (halfway, 2))
    even_part = paired[..., 0]
    odd_part = paired[..., 1]
    turned = jnp.stack(
        [even_part * cosine - odd_part * sine_part, odd_part * cosine + even_part * sine_part], -1
    )
    return turned.reshape(values.shape)


def norm_with(output, mean_value, mean_square):
    return (output - mean_value) * lax.rsqrt(mean_square - mean_value * mean_value + EPSILON)


def turn_lanes(raw, swap, cosine, sine_part):
    partner = jnp.dot(raw, swap, preferred_element_type=jnp.float32)
    return raw.astype(jnp.float32) * cosine + partner * sine_part


def output_kernel(
    rates_ref, live_ref, q_ref, k_ref, v_ref, prior_ref, cos_ref, sin_ref, swap_ref, out_ref
):
    swap = swap_ref[...]
    cosine = cos_ref[...]
    sine_part = sin_ref[...]
    span_len = q_ref.shape[0]
    live = live_ref[pl.program_id(0)]
    row = lax.broadcasted_iota(jnp.int32, (span_len, span_len), 0)
    column = lax.broadcasted_iota(jnp.int32, (span_len, span_len), 1)
    distance = jnp.maximum(row - column, 0).astype(jnp.float32)
    keep = (row >= column) & (column < live)
    row_index = lax.broadcasted_iota(jnp.int32, (span_len, 1), 0)
    valid = row_index < live
    for head in range(q_ref.shape[1]):
        rate = rates_ref[head]
        q_raw = q_ref[:, head, :]
        k_raw = k_ref[:, head, :]
        queries = turn_lanes(q_raw, swap, cosine, sine_part).astype(jnp.bfloat16)
        keys = (turn_lanes(k_raw, swap, cosine, sine_part) * (k_raw.shape[-1] ** (-0.5))).astype(
            jnp.bfloat16
        )
        scores = lax.dot_general(
            queries, keys, (((1,), (1,)), ((), ())), preferred_element_type=jnp.float32
        )
        table = jnp.where(keep, jnp.exp(-rate * distance), 0.0)
        weights = (scores * table).astype(jnp.bfloat16)
        inner = jnp.dot(weights, v_ref[:, head, :], preferred_element_type=jnp.float32)
        carried = jnp.dot(queries, prior_ref[head], preferred_element_type=jnp.float32)
        lead = jnp.exp(-rate * (row_index + 1).astype(jnp.float32))
        mixed = inner + lead * carried
        mean_value = jnp.mean(mixed, -1, keepdims=True)
        mean_square = jnp.mean(mixed * mixed, -1, keepdims=True)
        normed = norm_with(mixed, mean_value, mean_square)
        out_ref[:, head, :] = jnp.where(valid, normed, 0.0).astype(out_ref.dtype)


def prefill_tables(key_width, span_len, local_rates, span_start, live_count):
    halfway = key_width // 2
    offsets = jnp.arange(span_len)
    positions = (span_start[:, None] + offsets[None, :]).astype(jnp.float32)
    frequency = 10000.0 ** (-jnp.arange(halfway).astype(jnp.float32) / halfway)
    angles = positions[..., None] * frequency
    cosine = jnp.repeat(jnp.cos(angles), 2, axis=-1)
    sine_part = jnp.sin(angles)
    sine_part = jnp.stack([-sine_part, sine_part], -1).reshape(cosine.shape)
    lane = jnp.arange(key_width)
    swap = (lane[:, None] == (lane[None, :] ^ 1)).astype(jnp.bfloat16)
    valid_rows = offsets[None, :] < live_count[:, None]
    lead_decay = jnp.exp(-local_rates[:, None] * (offsets[None, :] + 1).astype(jnp.float32))
    remaining = (live_count[:, None] - 1 - offsets[None, :]).astype(jnp.float32)
    key_weight = jnp.where(
        valid_rows[:, None, :],
        jnp.exp(-local_rates[None, :, None] * jnp.maximum(remaining, 0.0)[:, None, :]),
        0.0,
    )
    kept_share = jnp.exp(-local_rates[None, :] * live_count[:, None].astype(jnp.float32))
    shape_rows = key_weight.shape
    rows = jnp.stack(
        [
            jnp.broadcast_to(lead_decay[None], shape_rows),
            jnp.broadcast_to(valid_rows[:, None, :].astype(jnp.float32), shape_rows),
            key_weight,
            jnp.broadcast_to(kept_share[:, :, None], shape_rows),
        ]
        + [jnp.zeros(shape_rows, jnp.float32)] * 4,
        -1,
    )
    return cosine, sine_part, swap, rows, valid_rows


def prefill_output(query_span, key_span, value_span, prior_state, local_rates, tables, live_count):
    prompts_here, span_len, heads_here, key_width = query_span.shape
    value_width = value_span.shape[3]
    cosine, sine_part, swap, rows, valid_rows = tables
    whole = pl.BlockSpec(memory_space=pltpu.SMEM)
    return pl.pallas_call(
        output_kernel,
        grid=(prompts_here,),
        in_specs=[
            whole,
            whole,
            pl.BlockSpec((None, span_len, heads_here, key_width), lambda b: (b, 0, 0, 0)),
            pl.BlockSpec((None, span_len, heads_here, key_width), lambda b: (b, 0, 0, 0)),
            pl.BlockSpec((None, span_len, heads_here, value_width), lambda b: (b, 0, 0, 0)),
            pl.BlockSpec((None, heads_here, key_width, value_width), lambda b: (b, 0, 0, 0)),
            pl.BlockSpec((None, span_len, key_width), lambda b: (b, 0, 0)),
            pl.BlockSpec((None, span_len, key_width), lambda b: (b, 0, 0)),
            pl.BlockSpec((key_width, key_width), lambda b: (0, 0)),
        ],
        out_specs=pl.BlockSpec(
            (None, span_len, heads_here, value_width), lambda b: (b, 0, 0, 0)
        ),
        out_shape=jax.ShapeDtypeStruct(value_span.shape, jnp.bfloat16),
    )(
        local_rates, live_count.astype(jnp.int32), query_span, key_span, value_span,
        prior_state, cosine, sine_part, swap,
    )


def per_device(
    query_span,
    key_span,
    value_span,
    prior_state,
    decay_rates,
    prompt_lengths,
    decode_inputs,
    w_query,
    w_key,
    w_value,
    w_gate,
    w_out,
):
    prompts_here, span_len, heads_here, key_width = query_span.shape
    value_width = value_span.shape[3]
    model_width = decode_inputs.shape[2]
    step_total = decode_inputs.shape[0]
    head_slots = lax.axis_size("heads")
    total_prompts = prompts_here * head_slots
    key_piece = w_query.shape[3]
    value_slice = w_value.shape[4]
    tp_index = lax.axis_index("tp")
    slot_index = lax.axis_index("heads")
    local_rates = lax.dynamic_slice_in_dim(decay_rates, tp_index * heads_here, heads_here)
    local_lengths = lax.dynamic_slice_in_dim(
        prompt_lengths, slot_index * prompts_here, prompts_here
    )
    span_start = span_len * ((local_lengths - 1) // span_len)
    live_count = local_lengths - span_start
    tables = prefill_tables(key_width, span_len, local_rates, span_start, live_count)
    offsets = jnp.arange(span_len)
    positions = (span_start[:, None] + offsets[None, :]).astype(jnp.float32)
    keys = (
        rotate(key_span.astype(jnp.float32), positions[:, :, None]) * key_width ** (-0.5)
    ).astype(jnp.bfloat16)
    valid_rows = offsets[None, :] < live_count[:, None]
    remaining = (live_count[:, None] - 1 - offsets[None, :]).astype(jnp.float32)
    key_weight = jnp.where(
        valid_rows[:, :, None],
        jnp.exp(-local_rates[None, None, :] * jnp.maximum(remaining, 0.0)[:, :, None]),
        0.0,
    )
    weighted = (keys.astype(jnp.float32) * key_weight[..., None]).astype(jnp.bfloat16)
    update = jnp.einsum("bjhk,bjhv->bhkv", weighted, value_span, preferred_element_type=jnp.float32)
    kept_share = jnp.exp(-local_rates[None, :] * live_count[:, None].astype(jnp.float32))
    state_new = (kept_share[:, :, None, None] * prior_state.astype(jnp.float32) + update).astype(
        jnp.bfloat16
    )
    slots = head_slots
    flat_inputs = decode_inputs.reshape(step_total * total_prompts, model_width)
    query_part = jnp.dot(
        flat_inputs, w_query.reshape(model_width, key_piece), preferred_element_type=jnp.float32
    ).astype(jnp.bfloat16)
    key_part = jnp.dot(
        flat_inputs, w_key.reshape(model_width, key_piece), preferred_element_type=jnp.float32
    ).astype(jnp.bfloat16)
    value_dec = jnp.dot(
        flat_inputs,
        w_value.reshape(model_width, heads_here * value_slice),
        preferred_element_type=jnp.float32,
    ).astype(jnp.bfloat16)
    gate_values = lax.optimization_barrier(
        jnp.dot(
            flat_inputs,
            w_gate.reshape(model_width, heads_here * value_slice),
            preferred_element_type=jnp.float32,
        )
    )
    steps = jnp.arange(step_total)
    halfway = key_width // 2
    head_column = (slot_index * key_piece + jnp.arange(key_piece)) % key_width
    column_frequency = 10000.0 ** (-(head_column // 2).astype(jnp.float32) / halfway)
    dec_positions = (
        (prompt_lengths[None, :] + steps[:, None]).astype(jnp.float32).reshape(-1, 1)
    )
    dec_angles = dec_positions * column_frequency[None, :]
    dec_cosine = jnp.cos(dec_angles)
    dec_sine = jnp.where(head_column % 2 == 0, -1.0, 1.0)[None, :] * jnp.sin(dec_angles)
    lane = jnp.arange(key_piece)
    swap = (lane[:, None] == (lane[None, :] ^ 1)).astype(jnp.bfloat16)
    query_partner = jnp.dot(query_part, swap, preferred_element_type=jnp.float32)
    key_partner = jnp.dot(key_part, swap, preferred_element_type=jnp.float32)
    query_turned = (
        query_part.astype(jnp.float32) * dec_cosine + query_partner * dec_sine
    ).astype(jnp.bfloat16)
    key_turned = (
        (key_part.astype(jnp.float32) * dec_cosine + key_partner * dec_sine)
        * key_width ** (-0.5)
    ).astype(jnp.bfloat16)
    packed = jnp.concatenate([query_turned, key_turned, value_dec], -1)
    packed = packed.reshape(step_total, slots, prompts_here, -1).transpose(1, 0, 2, 3)
    arrived = lax.all_to_all(packed, "heads", 0, 0, tiled=True)
    query_rot = (
        arrived[..., :key_piece]
        .transpose(1, 2, 0, 3)
        .reshape(step_total, prompts_here, heads_here, key_width)
    )
    key_rot = (
        arrived[..., key_piece : 2 * key_piece]
        .transpose(1, 2, 0, 3)
        .reshape(step_total, prompts_here, heads_here, key_width)
    )
    value_own = (
        arrived[..., 2 * key_piece :]
        .reshape(slots, step_total, prompts_here, heads_here, value_slice)
        .transpose(1, 2, 3, 0, 4)
        .reshape(step_total, prompts_here, heads_here, value_width)
    )
    from_state = jnp.einsum(
        "tbhk,bhkv->tbhv", query_rot, state_new, preferred_element_type=jnp.float32
    )
    step_gap = (steps[:, None] - steps[None, :]).astype(jnp.float32)
    step_decay = jnp.where(
        step_gap[None] >= 0,
        jnp.exp(-local_rates[:, None, None] * jnp.maximum(step_gap, 0.0)[None]),
        0.0,
    )
    step_scores = jnp.einsum(
        "tbhk,ubhk->bhtu", query_rot, key_rot, preferred_element_type=jnp.float32
    )
    from_steps = jnp.einsum(
        "bhtu,ubhv->tbhv",
        step_scores * step_decay[None],
        value_own.astype(jnp.float32),
        precision=lax.Precision.HIGHEST,
    )
    state_decay = jnp.exp(-local_rates[None, :] * (steps[:, None] + 1).astype(jnp.float32))
    readout = state_decay[:, None, :, None] * from_state + from_steps
    read_mean = jnp.mean(readout, -1, keepdims=True)
    read_square = jnp.mean(readout * readout, -1, keepdims=True)
    normed = norm_with(readout, read_mean, read_square)
    normed = normed.reshape(step_total, prompts_here, heads_here, slots, value_slice)
    normed = normed.transpose(3, 0, 1, 2, 4)
    normed = lax.all_to_all(normed, "heads", 0, 0, tiled=True)
    normed = normed.transpose(1, 0, 2, 3, 4).reshape(
        step_total, total_prompts, heads_here, value_slice
    )
    gates_steps = gate_values.reshape(step_total, total_prompts, heads_here, value_slice)
    activated = (
        (jax.nn.silu(gates_steps) * normed)
        .astype(jnp.bfloat16)
        .reshape(-1, heads_here * value_slice)
    )
    partial_out = jnp.dot(
        activated,
        w_out.reshape(heads_here * value_slice, model_width),
        preferred_element_type=jnp.float32,
    )
    partial_out = partial_out.reshape(step_total, total_prompts, model_width)
    query_span, key_span, value_span, prior_state, partial_out = lax.optimization_barrier(
        (query_span, key_span, value_span, prior_state, partial_out)
    )
    prefill_out = prefill_output(
        query_span, key_span, value_span, prior_state, local_rates, tables, live_count
    )
    out_slots = head_slots * lax.axis_size("tp")
    column_block = model_width // out_slots
    pieces = partial_out.reshape(step_total, total_prompts, out_slots, column_block)
    pieces = lax.all_to_all(pieces, ("heads", "tp"), 2, 2, tiled=True)
    decode_out = jnp.sum(pieces, 2).astype(jnp.bfloat16)
    return (prefill_out, decode_out)


def solution(mesh):
    placed = (
        P(("groups", "heads"), None, "tp", None),
        P(("groups", "heads"), None, "tp", None),
        P(("groups", "heads"), None, "tp", None),
        P(("groups", "heads"), "tp", None, None),
        P(),
        P("groups"),
        P(None, "groups", None),
        P(None, "tp", "heads", None),
        P(None, "tp", "heads", None),
        P(None, "tp", None, "heads", None),
        P(None, "tp", None, "heads", None),
        P("tp", None, "heads", None, None),
    )
    return jax.shard_map(
        per_device,
        mesh=mesh,
        in_specs=placed,
        out_specs=(P(("groups", "heads"), None, "tp", None), P(None, "groups", ("heads", "tp"))),
        check_vma=False,
    )
```

```python
import jax
import jax.numpy as jnp
from jax import lax
from jax.experimental import pallas as pl
from jax.experimental.pallas import tpu as pltpu
from jax.sharding import PartitionSpec as P

EPSILON = 1e-05


def rotate(values, positions):
    halfway = values.shape[-1] // 2
    frequency = 10000.0 ** (-jnp.arange(halfway).astype(jnp.float32) / halfway)
    angles = positions[..., None] * frequency
    cosine = jnp.cos(angles)
    sine_part = jnp.sin(angles)
    paired = values.reshape(values.shape[:-1] + (halfway, 2))
    even_part = paired[..., 0]
    odd_part = paired[..., 1]
    turned = jnp.stack(
        [even_part * cosine - odd_part * sine_part, odd_part * cosine + even_part * sine_part], -1
    )
    return turned.reshape(values.shape)


def norm_with(output, mean_value, mean_square):
    return (output - mean_value) * lax.rsqrt(mean_square - mean_value * mean_value + EPSILON)


def turn_lanes(raw, swap, cosine, sine_part):
    partner = jnp.dot(raw, swap, preferred_element_type=jnp.float32)
    return raw.astype(jnp.float32) * cosine + partner * sine_part


def output_kernel(
    rates_ref, live_ref, q_ref, k_ref, v_ref, prior_ref, cos_ref, sin_ref, swap_ref, out_ref
):
    swap = swap_ref[...]
    cosine = cos_ref[...]
    sine_part = sin_ref[...]
    span_len = q_ref.shape[0]
    live = live_ref[pl.program_id(0)]
    row = lax.broadcasted_iota(jnp.int32, (span_len, span_len), 0)
    column = lax.broadcasted_iota(jnp.int32, (span_len, span_len), 1)
    distance = jnp.maximum(row - column, 0).astype(jnp.float32)
    keep = (row >= column) & (column < live)
    row_index = lax.broadcasted_iota(jnp.int32, (span_len, 1), 0)
    valid = row_index < live
    for head in range(q_ref.shape[1]):
        rate = rates_ref[head]
        q_raw = q_ref[:, head, :]
        k_raw = k_ref[:, head, :]
        queries = turn_lanes(q_raw, swap, cosine, sine_part).astype(jnp.bfloat16)
        keys = (turn_lanes(k_raw, swap, cosine, sine_part) * (k_raw.shape[-1] ** (-0.5))).astype(
            jnp.bfloat16
        )
        scores = lax.dot_general(
            queries, keys, (((1,), (1,)), ((), ())), preferred_element_type=jnp.float32
        )
        table = jnp.where(keep, jnp.exp(-rate * distance), 0.0)
        weights = (scores * table).astype(jnp.bfloat16)
        inner = jnp.dot(weights, v_ref[:, head, :], preferred_element_type=jnp.float32)
        carried = jnp.dot(queries, prior_ref[head], preferred_element_type=jnp.float32)
        lead = jnp.exp(-rate * (row_index + 1).astype(jnp.float32))
        mixed = inner + lead * carried
        mean_value = jnp.mean(mixed, -1, keepdims=True)
        mean_square = jnp.mean(mixed * mixed, -1, keepdims=True)
        normed = norm_with(mixed, mean_value, mean_square)
        out_ref[:, head, :] = jnp.where(valid, normed, 0.0).astype(out_ref.dtype)


def prefill_tables(key_width, span_len, local_rates, span_start, live_count):
    halfway = key_width // 2
    offsets = jnp.arange(span_len)
    positions = (span_start[:, None] + offsets[None, :]).astype(jnp.float32)
    lane = jnp.arange(key_width)
    frequency = 10000.0 ** (-(lane // 2).astype(jnp.float32) / halfway)
    angles = positions[..., None] * frequency
    cosine = jnp.cos(angles)
    sine_part = jnp.where(lane % 2 == 0, -1.0, 1.0) * jnp.sin(angles)
    swap = (lane[:, None] == (lane[None, :] ^ 1)).astype(jnp.bfloat16)
    return cosine, sine_part, swap


def prefill_output(query_span, key_span, value_span, prior_state, local_rates, tables, live_count):
    prompts_here, span_len, heads_here, key_width = query_span.shape
    value_width = value_span.shape[3]
    cosine, sine_part, swap = tables
    whole = pl.BlockSpec(memory_space=pltpu.SMEM)
    return pl.pallas_call(
        output_kernel,
        grid=(prompts_here,),
        in_specs=[
            whole,
            whole,
            pl.BlockSpec((None, span_len, heads_here, key_width), lambda b: (b, 0, 0, 0)),
            pl.BlockSpec((None, span_len, heads_here, key_width), lambda b: (b, 0, 0, 0)),
            pl.BlockSpec((None, span_len, heads_here, value_width), lambda b: (b, 0, 0, 0)),
            pl.BlockSpec((None, heads_here, key_width, value_width), lambda b: (b, 0, 0, 0)),
            pl.BlockSpec((None, span_len, key_width), lambda b: (b, 0, 0)),
            pl.BlockSpec((None, span_len, key_width), lambda b: (b, 0, 0)),
            pl.BlockSpec((key_width, key_width), lambda b: (0, 0)),
        ],
        out_specs=pl.BlockSpec(
            (None, span_len, heads_here, value_width), lambda b: (b, 0, 0, 0)
        ),
        out_shape=jax.ShapeDtypeStruct(value_span.shape, jnp.bfloat16),
    )(
        local_rates, live_count.astype(jnp.int32), query_span, key_span, value_span,
        prior_state, cosine, sine_part, swap,
    )


def per_device(
    query_span,
    key_span,
    value_span,
    prior_state,
    decay_rates,
    prompt_lengths,
    decode_inputs,
    w_query,
    w_key,
    w_value,
    w_gate,
    w_out,
):
    prompts_here, span_len, heads_here, key_width = query_span.shape
    value_width = value_span.shape[3]
    model_width = decode_inputs.shape[2]
    step_total = decode_inputs.shape[0]
    head_slots = lax.axis_size("heads")
    total_prompts = prompts_here * head_slots
    key_piece = w_query.shape[3]
    value_slice = w_value.shape[4]
    tp_index = lax.axis_index("tp")
    slot_index = lax.axis_index("heads")
    local_rates = lax.dynamic_slice_in_dim(decay_rates, tp_index * heads_here, heads_here)
    local_lengths = lax.dynamic_slice_in_dim(
        prompt_lengths, slot_index * prompts_here, prompts_here
    )
    span_start = span_len * ((local_lengths - 1) // span_len)
    live_count = local_lengths - span_start
    offsets = jnp.arange(span_len)
    positions = (span_start[:, None] + offsets[None, :]).astype(jnp.float32)
    keys = (
        rotate(key_span.astype(jnp.float32), positions[:, :, None]) * key_width ** (-0.5)
    ).astype(jnp.bfloat16)
    valid_rows = offsets[None, :] < live_count[:, None]
    remaining = (live_count[:, None] - 1 - offsets[None, :]).astype(jnp.float32)
    key_weight = jnp.where(
        valid_rows[:, :, None],
        jnp.exp(-local_rates[None, None, :] * jnp.maximum(remaining, 0.0)[:, :, None]),
        0.0,
    )
    weighted = (keys.astype(jnp.float32) * key_weight[..., None]).astype(jnp.bfloat16)
    update = jnp.einsum("bjhk,bjhv->bhkv", weighted, value_span, preferred_element_type=jnp.float32)
    kept_share = jnp.exp(-local_rates[None, :] * live_count[:, None].astype(jnp.float32))
    state_new = (kept_share[:, :, None, None] * prior_state.astype(jnp.float32) + update).astype(
        jnp.bfloat16
    )
    slots = head_slots
    flat_inputs = decode_inputs.reshape(step_total * total_prompts, model_width)
    query_part = jnp.dot(
        flat_inputs, w_query.reshape(model_width, key_piece), preferred_element_type=jnp.float32
    ).astype(jnp.bfloat16)
    key_part = jnp.dot(
        flat_inputs, w_key.reshape(model_width, key_piece), preferred_element_type=jnp.float32
    ).astype(jnp.bfloat16)
    value_dec = jnp.dot(
        flat_inputs,
        w_value.reshape(model_width, heads_here * value_slice),
        preferred_element_type=jnp.float32,
    ).astype(jnp.bfloat16)
    gate_values = lax.optimization_barrier(
        jnp.dot(
            flat_inputs,
            w_gate.reshape(model_width, heads_here * value_slice),
            preferred_element_type=jnp.float32,
        )
    )
    steps = jnp.arange(step_total)
    halfway = key_width // 2
    head_column = (slot_index * key_piece + jnp.arange(key_piece)) % key_width
    column_frequency = 10000.0 ** (-(head_column // 2).astype(jnp.float32) / halfway)
    dec_positions = (
        (prompt_lengths[None, :] + steps[:, None]).astype(jnp.float32).reshape(-1, 1)
    )
    dec_angles = dec_positions * column_frequency[None, :]
    dec_cosine = jnp.cos(dec_angles)
    dec_sine = jnp.where(head_column % 2 == 0, -1.0, 1.0)[None, :] * jnp.sin(dec_angles)
    lane = jnp.arange(key_piece)
    swap = (lane[:, None] == (lane[None, :] ^ 1)).astype(jnp.bfloat16)
    query_partner = jnp.dot(query_part, swap, preferred_element_type=jnp.float32)
    key_partner = jnp.dot(key_part, swap, preferred_element_type=jnp.float32)
    query_turned = (
        query_part.astype(jnp.float32) * dec_cosine + query_partner * dec_sine
    ).astype(jnp.bfloat16)
    key_turned = (
        (key_part.astype(jnp.float32) * dec_cosine + key_partner * dec_sine)
        * key_width ** (-0.5)
    ).astype(jnp.bfloat16)
    packed = jnp.concatenate([query_turned, key_turned, value_dec], -1)
    packed = packed.reshape(step_total, slots, prompts_here, -1).transpose(1, 0, 2, 3)
    arrived = lax.all_to_all(packed, "heads", 0, 0, tiled=True)
    query_rot = (
        arrived[..., :key_piece]
        .transpose(1, 2, 0, 3)
        .reshape(step_total, prompts_here, heads_here, key_width)
    )
    key_rot = (
        arrived[..., key_piece : 2 * key_piece]
        .transpose(1, 2, 0, 3)
        .reshape(step_total, prompts_here, heads_here, key_width)
    )
    value_own = (
        arrived[..., 2 * key_piece :]
        .reshape(slots, step_total, prompts_here, heads_here, value_slice)
        .transpose(1, 2, 3, 0, 4)
        .reshape(step_total, prompts_here, heads_here, value_width)
    )
    from_state = jnp.einsum(
        "tbhk,bhkv->tbhv", query_rot, state_new, preferred_element_type=jnp.float32
    )
    step_gap = (steps[:, None] - steps[None, :]).astype(jnp.float32)
    step_decay = jnp.where(
        step_gap[None] >= 0,
        jnp.exp(-local_rates[:, None, None] * jnp.maximum(step_gap, 0.0)[None]),
        0.0,
    )
    step_scores = jnp.einsum(
        "tbhk,ubhk->bhtu", query_rot, key_rot, preferred_element_type=jnp.float32
    )
    from_steps = jnp.einsum(
        "bhtu,ubhv->tbhv",
        step_scores * step_decay[None],
        value_own.astype(jnp.float32),
        precision=lax.Precision.HIGHEST,
    )
    state_decay = jnp.exp(-local_rates[None, :] * (steps[:, None] + 1).astype(jnp.float32))
    readout = state_decay[:, None, :, None] * from_state + from_steps
    read_mean = jnp.mean(readout, -1, keepdims=True)
    read_square = jnp.mean(readout * readout, -1, keepdims=True)
    normed = norm_with(readout, read_mean, read_square)
    normed = normed.reshape(step_total, prompts_here, heads_here, slots, value_slice)
    normed = normed.transpose(3, 0, 1, 2, 4)
    table_rates, table_start, table_live, normed = lax.optimization_barrier(
        (local_rates, span_start, live_count, normed)
    )
    tables = prefill_tables(key_width, span_len, table_rates, table_start, table_live)
    normed = lax.all_to_all(normed, "heads", 0, 0, tiled=True)
    normed, tables = lax.optimization_barrier((normed, tables))
    normed = normed.transpose(1, 0, 2, 3, 4).reshape(
        step_total, total_prompts, heads_here, value_slice
    )
    gates_steps = gate_values.reshape(step_total, total_prompts, heads_here, value_slice)
    activated = (
        (jax.nn.silu(gates_steps) * normed)
        .astype(jnp.bfloat16)
        .reshape(-1, heads_here * value_slice)
    )
    partial_out = jnp.dot(
        activated,
        w_out.reshape(heads_here * value_slice, model_width),
        preferred_element_type=jnp.float32,
    )
    partial_out = partial_out.reshape(step_total, total_prompts, model_width)
    query_span, key_span, value_span, prior_state, partial_out = lax.optimization_barrier(
        (query_span, key_span, value_span, prior_state, partial_out)
    )
    prefill_out = prefill_output(
        query_span, key_span, value_span, prior_state, local_rates, tables, live_count
    )
    out_slots = head_slots * lax.axis_size("tp")
    column_block = model_width // out_slots
    pieces = partial_out.reshape(step_total, total_prompts, out_slots, column_block)
    pieces = lax.all_to_all(pieces, ("heads", "tp"), 2, 2, tiled=True)
    decode_out = jnp.sum(pieces, 2).astype(jnp.bfloat16)
    return (prefill_out, decode_out)


def solution(mesh):
    placed = (
        P(("groups", "heads"), None, "tp", None),
        P(("groups", "heads"), None, "tp", None),
        P(("groups", "heads"), None, "tp", None),
        P(("groups", "heads"), "tp", None, None),
        P(),
        P("groups"),
        P(None, "groups", None),
        P(None, "tp", "heads", None),
        P(None, "tp", "heads", None),
        P(None, "tp", None, "heads", None),
        P(None, "tp", None, "heads", None),
        P("tp", None, "heads", None, None),
    )
    return jax.shard_map(
        per_device,
        mesh=mesh,
        in_specs=placed,
        out_specs=(P(("groups", "heads"), None, "tp", None), P(None, "groups", ("heads", "tp"))),
        check_vma=False,
    )
```

```python
import jax
import jax.numpy as jnp
from jax import lax
from jax.experimental import pallas as pl
from jax.experimental.pallas import tpu as pltpu
from jax.sharding import PartitionSpec as P

EPSILON = 1e-05


def rotate(values, positions):
    halfway = values.shape[-1] // 2
    frequency = 10000.0 ** (-jnp.arange(halfway).astype(jnp.float32) / halfway)
    angles = positions[..., None] * frequency
    cosine = jnp.cos(angles)
    sine_part = jnp.sin(angles)
    paired = values.reshape(values.shape[:-1] + (halfway, 2))
    even_part = paired[..., 0]
    odd_part = paired[..., 1]
    turned = jnp.stack(
        [even_part * cosine - odd_part * sine_part, odd_part * cosine + even_part * sine_part], -1
    )
    return turned.reshape(values.shape)


def norm_with(output, mean_value, mean_square):
    return (output - mean_value) * lax.rsqrt(mean_square - mean_value * mean_value + EPSILON)


def turn_lanes(raw, swap, cosine, sine_part):
    partner = jnp.dot(raw, swap, preferred_element_type=jnp.float32)
    return raw.astype(jnp.float32) * cosine + partner * sine_part


def output_kernel(
    rates_ref, live_ref, q_ref, k_ref, v_ref, prior_ref, cos_ref, sin_ref, swap_ref, out_ref
):
    swap = swap_ref[...]
    cosine = cos_ref[...]
    sine_part = sin_ref[...]
    span_len = q_ref.shape[0]
    live = live_ref[pl.program_id(0)]
    row = lax.broadcasted_iota(jnp.int32, (span_len, span_len), 0)
    column = lax.broadcasted_iota(jnp.int32, (span_len, span_len), 1)
    distance = jnp.maximum(row - column, 0).astype(jnp.float32)
    keep = (row >= column) & (column < live)
    row_index = lax.broadcasted_iota(jnp.int32, (span_len, 1), 0)
    valid = row_index < live
    for head in range(q_ref.shape[1]):
        rate = rates_ref[head]
        q_raw = q_ref[:, head, :]
        k_raw = k_ref[:, head, :]
        queries = turn_lanes(q_raw, swap, cosine, sine_part).astype(jnp.bfloat16)
        keys = (turn_lanes(k_raw, swap, cosine, sine_part) * (k_raw.shape[-1] ** (-0.5))).astype(
            jnp.bfloat16
        )
        scores = lax.dot_general(
            queries, keys, (((1,), (1,)), ((), ())), preferred_element_type=jnp.float32
        )
        table = jnp.where(keep, jnp.exp(-rate * distance), 0.0)
        weights = (scores * table).astype(jnp.bfloat16)
        inner = jnp.dot(weights, v_ref[:, head, :], preferred_element_type=jnp.float32)
        carried = jnp.dot(queries, prior_ref[head], preferred_element_type=jnp.float32)
        lead = jnp.exp(-rate * (row_index + 1).astype(jnp.float32))
        mixed = inner + lead * carried
        mean_value = jnp.mean(mixed, -1, keepdims=True)
        mean_square = jnp.mean(mixed * mixed, -1, keepdims=True)
        normed = norm_with(mixed, mean_value, mean_square)
        out_ref[:, head, :] = jnp.where(valid, normed, 0.0).astype(out_ref.dtype)


def prefill_tables(key_width, span_len, local_rates, span_start, live_count):
    halfway = key_width // 2
    offsets = jnp.arange(span_len)
    positions = (span_start[:, None] + offsets[None, :]).astype(jnp.float32)
    frequency = 10000.0 ** (-jnp.arange(halfway).astype(jnp.float32) / halfway)
    angles = positions[..., None] * frequency
    cosine = jnp.repeat(jnp.cos(angles), 2, axis=-1)
    sine_part = jnp.sin(angles)
    sine_part = jnp.stack([-sine_part, sine_part], -1).reshape(cosine.shape)
    lane = jnp.arange(key_width)
    swap = (lane[:, None] == (lane[None, :] ^ 1)).astype(jnp.bfloat16)
    valid_rows = offsets[None, :] < live_count[:, None]
    lead_decay = jnp.exp(-local_rates[:, None] * (offsets[None, :] + 1).astype(jnp.float32))
    remaining = (live_count[:, None] - 1 - offsets[None, :]).astype(jnp.float32)
    key_weight = jnp.where(
        valid_rows[:, None, :],
        jnp.exp(-local_rates[None, :, None] * jnp.maximum(remaining, 0.0)[:, None, :]),
        0.0,
    )
    kept_share = jnp.exp(-local_rates[None, :] * live_count[:, None].astype(jnp.float32))
    shape_rows = key_weight.shape
    rows = jnp.stack(
        [
            jnp.broadcast_to(lead_decay[None], shape_rows),
            jnp.broadcast_to(valid_rows[:, None, :].astype(jnp.float32), shape_rows),
            key_weight,
            jnp.broadcast_to(kept_share[:, :, None], shape_rows),
        ]
        + [jnp.zeros(shape_rows, jnp.float32)] * 4,
        -1,
    )
    return cosine, sine_part, swap, rows, valid_rows


def prefill_output(query_span, key_span, value_span, prior_state, local_rates, tables, live_count):
    prompts_here, span_len, heads_here, key_width = query_span.shape
    value_width = value_span.shape[3]
    cosine, sine_part, swap, rows, valid_rows = tables
    whole = pl.BlockSpec(memory_space=pltpu.SMEM)
    return pl.pallas_call(
        output_kernel,
        grid=(prompts_here,),
        in_specs=[
            whole,
            whole,
            pl.BlockSpec((None, span_len, heads_here, key_width), lambda b: (b, 0, 0, 0)),
            pl.BlockSpec((None, span_len, heads_here, key_width), lambda b: (b, 0, 0, 0)),
            pl.BlockSpec((None, span_len, heads_here, value_width), lambda b: (b, 0, 0, 0)),
            pl.BlockSpec((None, heads_here, key_width, value_width), lambda b: (b, 0, 0, 0)),
            pl.BlockSpec((None, span_len, key_width), lambda b: (b, 0, 0)),
            pl.BlockSpec((None, span_len, key_width), lambda b: (b, 0, 0)),
            pl.BlockSpec((key_width, key_width), lambda b: (0, 0)),
        ],
        out_specs=pl.BlockSpec(
            (None, span_len, heads_here, value_width), lambda b: (b, 0, 0, 0)
        ),
        out_shape=jax.ShapeDtypeStruct(value_span.shape, jnp.bfloat16),
    )(
        local_rates, live_count.astype(jnp.int32), query_span, key_span, value_span,
        prior_state, cosine, sine_part, swap,
    )


def per_device(
    query_span,
    key_span,
    value_span,
    prior_state,
    decay_rates,
    prompt_lengths,
    decode_inputs,
    w_query,
    w_key,
    w_value,
    w_gate,
    w_out,
):
    prompts_here, span_len, heads_here, key_width = query_span.shape
    value_width = value_span.shape[3]
    model_width = decode_inputs.shape[2]
    step_total = decode_inputs.shape[0]
    head_slots = lax.axis_size("heads")
    total_prompts = prompts_here * head_slots
    key_piece = w_query.shape[3]
    value_slice = w_value.shape[4]
    tp_index = lax.axis_index("tp")
    slot_index = lax.axis_index("heads")
    local_rates = lax.dynamic_slice_in_dim(decay_rates, tp_index * heads_here, heads_here)
    local_lengths = lax.dynamic_slice_in_dim(
        prompt_lengths, slot_index * prompts_here, prompts_here
    )
    span_start = span_len * ((local_lengths - 1) // span_len)
    live_count = local_lengths - span_start
    tables = prefill_tables(key_width, span_len, local_rates, span_start, live_count)
    offsets = jnp.arange(span_len)
    positions = (span_start[:, None] + offsets[None, :]).astype(jnp.float32)
    cosine, sine_part, swap = tables[:3]
    key_partner = jnp.einsum("bihk,kl->bihl", key_span, swap, preferred_element_type=jnp.float32)
    keys = (
        (key_span.astype(jnp.float32) * cosine[:, :, None, :] + key_partner * sine_part[:, :, None, :])
        * key_width ** (-0.5)
    ).astype(jnp.bfloat16)
    valid_rows = offsets[None, :] < live_count[:, None]
    remaining = (live_count[:, None] - 1 - offsets[None, :]).astype(jnp.float32)
    key_weight = jnp.where(
        valid_rows[:, :, None],
        jnp.exp(-local_rates[None, None, :] * jnp.maximum(remaining, 0.0)[:, :, None]),
        0.0,
    )
    weighted = (keys.astype(jnp.float32) * key_weight[..., None]).astype(jnp.bfloat16)
    update = jnp.einsum("bjhk,bjhv->bhkv", weighted, value_span, preferred_element_type=jnp.float32)
    kept_share = jnp.exp(-local_rates[None, :] * live_count[:, None].astype(jnp.float32))
    state_new = (kept_share[:, :, None, None] * prior_state.astype(jnp.float32) + update).astype(
        jnp.bfloat16
    )
    slots = head_slots
    flat_inputs = decode_inputs.reshape(step_total * total_prompts, model_width)
    query_part = jnp.dot(
        flat_inputs, w_query.reshape(model_width, key_piece), preferred_element_type=jnp.float32
    ).astype(jnp.bfloat16)
    key_part = jnp.dot(
        flat_inputs, w_key.reshape(model_width, key_piece), preferred_element_type=jnp.float32
    ).astype(jnp.bfloat16)
    value_dec = jnp.dot(
        flat_inputs,
        w_value.reshape(model_width, heads_here * value_slice),
        preferred_element_type=jnp.float32,
    ).astype(jnp.bfloat16)
    gate_values = lax.optimization_barrier(
        jnp.dot(
            flat_inputs,
            w_gate.reshape(model_width, heads_here * value_slice),
            preferred_element_type=jnp.float32,
        )
    )
    steps = jnp.arange(step_total)
    halfway = key_width // 2
    head_column = (slot_index * key_piece + jnp.arange(key_piece)) % key_width
    column_frequency = 10000.0 ** (-(head_column // 2).astype(jnp.float32) / halfway)
    dec_positions = (
        (prompt_lengths[None, :] + steps[:, None]).astype(jnp.float32).reshape(-1, 1)
    )
    dec_angles = dec_positions * column_frequency[None, :]
    dec_cosine = jnp.cos(dec_angles)
    dec_sine = jnp.where(head_column % 2 == 0, -1.0, 1.0)[None, :] * jnp.sin(dec_angles)
    lane = jnp.arange(key_piece)
    swap = (lane[:, None] == (lane[None, :] ^ 1)).astype(jnp.bfloat16)
    query_partner = jnp.dot(query_part, swap, preferred_element_type=jnp.float32)
    key_partner = jnp.dot(key_part, swap, preferred_element_type=jnp.float32)
    query_turned = (
        query_part.astype(jnp.float32) * dec_cosine + query_partner * dec_sine
    ).astype(jnp.bfloat16)
    key_turned = (
        (key_part.astype(jnp.float32) * dec_cosine + key_partner * dec_sine)
        * key_width ** (-0.5)
    ).astype(jnp.bfloat16)
    packed = jnp.concatenate([query_turned, key_turned, value_dec], -1)
    packed = packed.reshape(step_total, slots, prompts_here, -1).transpose(1, 0, 2, 3)
    arrived = lax.all_to_all(packed, "heads", 0, 0, tiled=True)
    query_rot = (
        arrived[..., :key_piece]
        .transpose(1, 2, 0, 3)
        .reshape(step_total, prompts_here, heads_here, key_width)
    )
    key_rot = (
        arrived[..., key_piece : 2 * key_piece]
        .transpose(1, 2, 0, 3)
        .reshape(step_total, prompts_here, heads_here, key_width)
    )
    value_own = (
        arrived[..., 2 * key_piece :]
        .reshape(slots, step_total, prompts_here, heads_here, value_slice)
        .transpose(1, 2, 3, 0, 4)
        .reshape(step_total, prompts_here, heads_here, value_width)
    )
    from_state = jnp.einsum(
        "tbhk,bhkv->tbhv", query_rot, state_new, preferred_element_type=jnp.float32
    )
    step_gap = (steps[:, None] - steps[None, :]).astype(jnp.float32)
    step_decay = jnp.where(
        step_gap[None] >= 0,
        jnp.exp(-local_rates[:, None, None] * jnp.maximum(step_gap, 0.0)[None]),
        0.0,
    )
    step_scores = jnp.einsum(
        "tbhk,ubhk->bhtu", query_rot, key_rot, preferred_element_type=jnp.float32
    )
    from_steps = jnp.einsum(
        "bhtu,ubhv->tbhv",
        step_scores * step_decay[None],
        value_own.astype(jnp.float32),
        precision=lax.Precision.HIGHEST,
    )
    state_decay = jnp.exp(-local_rates[None, :] * (steps[:, None] + 1).astype(jnp.float32))
    readout = state_decay[:, None, :, None] * from_state + from_steps
    read_mean = jnp.mean(readout, -1, keepdims=True)
    read_square = jnp.mean(readout * readout, -1, keepdims=True)
    normed = norm_with(readout, read_mean, read_square)
    normed = normed.reshape(step_total, prompts_here, heads_here, slots, value_slice)
    normed = normed.transpose(3, 0, 1, 2, 4)
    normed = lax.all_to_all(normed, "heads", 0, 0, tiled=True)
    normed = normed.transpose(1, 0, 2, 3, 4).reshape(
        step_total, total_prompts, heads_here, value_slice
    )
    gates_steps = gate_values.reshape(step_total, total_prompts, heads_here, value_slice)
    activated = (
        (jax.nn.silu(gates_steps) * normed)
        .astype(jnp.bfloat16)
        .reshape(-1, heads_here * value_slice)
    )
    partial_out = jnp.dot(
        activated,
        w_out.reshape(heads_here * value_slice, model_width),
        preferred_element_type=jnp.float32,
    )
    partial_out = partial_out.reshape(step_total, total_prompts, model_width)
    query_span, key_span, value_span, prior_state, partial_out = lax.optimization_barrier(
        (query_span, key_span, value_span, prior_state, partial_out)
    )
    prefill_out = prefill_output(
        query_span, key_span, value_span, prior_state, local_rates, tables, live_count
    )
    out_slots = head_slots * lax.axis_size("tp")
    column_block = model_width // out_slots
    pieces = partial_out.reshape(step_total, total_prompts, out_slots, column_block)
    pieces = lax.all_to_all(pieces, ("heads", "tp"), 2, 2, tiled=True)
    decode_out = jnp.sum(pieces, 2).astype(jnp.bfloat16)
    return (prefill_out, decode_out)


def solution(mesh):
    placed = (
        P(("groups", "heads"), None, "tp", None),
        P(("groups", "heads"), None, "tp", None),
        P(("groups", "heads"), None, "tp", None),
        P(("groups", "heads"), "tp", None, None),
        P(),
        P("groups"),
        P(None, "groups", None),
        P(None, "tp", "heads", None),
        P(None, "tp", "heads", None),
        P(None, "tp", None, "heads", None),
        P(None, "tp", None, "heads", None),
        P("tp", None, "heads", None, None),
    )
    return jax.shard_map(
        per_device,
        mesh=mesh,
        in_specs=placed,
        out_specs=(P(("groups", "heads"), None, "tp", None), P(None, "groups", ("heads", "tp"))),
        check_vma=False,
    )
```

```python
import jax
import jax.numpy as jnp
from jax import lax
from jax.experimental import pallas as pl
from jax.experimental.pallas import tpu as pltpu
from jax.sharding import PartitionSpec as P

EPSILON = 1e-05


def rotate(values, positions):
    halfway = values.shape[-1] // 2
    frequency = 10000.0 ** (-jnp.arange(halfway).astype(jnp.float32) / halfway)
    angles = positions[..., None] * frequency
    cosine = jnp.cos(angles)
    sine_part = jnp.sin(angles)
    paired = values.reshape(values.shape[:-1] + (halfway, 2))
    even_part = paired[..., 0]
    odd_part = paired[..., 1]
    turned = jnp.stack(
        [even_part * cosine - odd_part * sine_part, odd_part * cosine + even_part * sine_part], -1
    )
    return turned.reshape(values.shape)


def norm_with(output, mean_value, mean_square):
    return (output - mean_value) * lax.rsqrt(mean_square - mean_value * mean_value + EPSILON)


def turn_lanes(raw, swap, cosine, sine_part):
    partner = jnp.dot(raw, swap, preferred_element_type=jnp.float32)
    return raw.astype(jnp.float32) * cosine + partner * sine_part


def output_kernel(
    rates_ref, live_ref, q_ref, k_ref, v_ref, prior_ref, cos_ref, sin_ref, swap_ref, out_ref
):
    swap = swap_ref[...]
    cosine = cos_ref[...]
    sine_part = sin_ref[...]
    span_len = q_ref.shape[0]
    live = live_ref[pl.program_id(0)]
    row = lax.broadcasted_iota(jnp.int32, (span_len, span_len), 0)
    column = lax.broadcasted_iota(jnp.int32, (span_len, span_len), 1)
    distance = jnp.maximum(row - column, 0).astype(jnp.float32)
    keep = (row >= column) & (column < live)
    row_index = lax.broadcasted_iota(jnp.int32, (span_len, 1), 0)
    valid = row_index < live
    for head in range(q_ref.shape[1]):
        rate = rates_ref[head]
        q_raw = q_ref[:, head, :]
        k_raw = k_ref[:, head, :]
        queries = turn_lanes(q_raw, swap, cosine, sine_part).astype(jnp.bfloat16)
        keys = (turn_lanes(k_raw, swap, cosine, sine_part) * (k_raw.shape[-1] ** (-0.5))).astype(
            jnp.bfloat16
        )
        scores = lax.dot_general(
            queries, keys, (((1,), (1,)), ((), ())), preferred_element_type=jnp.float32
        )
        table = jnp.where(keep, jnp.exp(-rate * distance), 0.0)
        weights = (scores * table).astype(jnp.bfloat16)
        inner = jnp.dot(weights, v_ref[:, head, :], preferred_element_type=jnp.float32)
        carried = jnp.dot(queries, prior_ref[head], preferred_element_type=jnp.float32)
        lead = jnp.exp(-rate * (row_index + 1).astype(jnp.float32))
        mixed = inner + lead * carried
        mean_value = jnp.mean(mixed, -1, keepdims=True)
        mean_square = jnp.mean(mixed * mixed, -1, keepdims=True)
        normed = norm_with(mixed, mean_value, mean_square)
        out_ref[:, head, :] = jnp.where(valid, normed, 0.0).astype(out_ref.dtype)


def prefill_tables(key_width, span_len, local_rates, span_start, live_count):
    halfway = key_width // 2
    offsets = jnp.arange(span_len)
    positions = (span_start[:, None] + offsets[None, :]).astype(jnp.float32)
    frequency = 10000.0 ** (-jnp.arange(halfway).astype(jnp.float32) / halfway)
    angles = positions[..., None] * frequency
    cosine = jnp.repeat(jnp.cos(angles), 2, axis=-1)
    sine_part = jnp.sin(angles)
    sine_part = jnp.stack([-sine_part, sine_part], -1).reshape(cosine.shape)
    lane = jnp.arange(key_width)
    swap = (lane[:, None] == (lane[None, :] ^ 1)).astype(jnp.bfloat16)
    valid_rows = offsets[None, :] < live_count[:, None]
    lead_decay = jnp.exp(-local_rates[:, None] * (offsets[None, :] + 1).astype(jnp.float32))
    remaining = (live_count[:, None] - 1 - offsets[None, :]).astype(jnp.float32)
    key_weight = jnp.where(
        valid_rows[:, None, :],
        jnp.exp(-local_rates[None, :, None] * jnp.maximum(remaining, 0.0)[:, None, :]),
        0.0,
    )
    kept_share = jnp.exp(-local_rates[None, :] * live_count[:, None].astype(jnp.float32))
    shape_rows = key_weight.shape
    rows = jnp.stack(
        [
            jnp.broadcast_to(lead_decay[None], shape_rows),
            jnp.broadcast_to(valid_rows[:, None, :].astype(jnp.float32), shape_rows),
            key_weight,
            jnp.broadcast_to(kept_share[:, :, None], shape_rows),
        ]
        + [jnp.zeros(shape_rows, jnp.float32)] * 4,
        -1,
    )
    return cosine, sine_part, swap, rows, valid_rows


def prefill_output(query_span, key_span, value_span, prior_state, local_rates, tables, live_count):
    prompts_here, span_len, heads_here, key_width = query_span.shape
    value_width = value_span.shape[3]
    cosine, sine_part, swap, rows, valid_rows = tables
    whole = pl.BlockSpec(memory_space=pltpu.SMEM)
    return pl.pallas_call(
        output_kernel,
        grid=(prompts_here,),
        in_specs=[
            whole,
            whole,
            pl.BlockSpec((None, span_len, heads_here, key_width), lambda b: (b, 0, 0, 0)),
            pl.BlockSpec((None, span_len, heads_here, key_width), lambda b: (b, 0, 0, 0)),
            pl.BlockSpec((None, span_len, heads_here, value_width), lambda b: (b, 0, 0, 0)),
            pl.BlockSpec((None, heads_here, key_width, value_width), lambda b: (b, 0, 0, 0)),
            pl.BlockSpec((None, span_len, key_width), lambda b: (b, 0, 0)),
            pl.BlockSpec((None, span_len, key_width), lambda b: (b, 0, 0)),
            pl.BlockSpec((key_width, key_width), lambda b: (0, 0)),
        ],
        out_specs=pl.BlockSpec(
            (None, span_len, heads_here, value_width), lambda b: (b, 0, 0, 0)
        ),
        out_shape=jax.ShapeDtypeStruct(value_span.shape, jnp.bfloat16),
    )(
        local_rates, live_count.astype(jnp.int32), query_span, key_span, value_span,
        prior_state, cosine, sine_part, swap,
    )


def per_device(
    query_span,
    key_span,
    value_span,
    prior_state,
    decay_rates,
    prompt_lengths,
    decode_inputs,
    w_query,
    w_key,
    w_value,
    w_gate,
    w_out,
):
    prompts_here, span_len, heads_here, key_width = query_span.shape
    value_width = value_span.shape[3]
    model_width = decode_inputs.shape[2]
    step_total = decode_inputs.shape[0]
    head_slots = lax.axis_size("heads")
    total_prompts = prompts_here * head_slots
    key_piece = w_query.shape[3]
    value_slice = w_value.shape[4]
    tp_index = lax.axis_index("tp")
    slot_index = lax.axis_index("heads")
    local_rates = lax.dynamic_slice_in_dim(decay_rates, tp_index * heads_here, heads_here)
    local_lengths = lax.dynamic_slice_in_dim(
        prompt_lengths, slot_index * prompts_here, prompts_here
    )
    span_start = span_len * ((local_lengths - 1) // span_len)
    live_count = local_lengths - span_start
    tables = prefill_tables(key_width, span_len, local_rates, span_start, live_count)
    offsets = jnp.arange(span_len)
    positions = (span_start[:, None] + offsets[None, :]).astype(jnp.float32)
    cosine, sine_part, swap = tables[:3]
    key_partner = jnp.einsum("bihk,kl->bihl", key_span, swap, preferred_element_type=jnp.float32)
    keys = (
        (key_span.astype(jnp.float32) * cosine[:, :, None, :] + key_partner * sine_part[:, :, None, :])
        * key_width ** (-0.5)
    ).astype(jnp.bfloat16)
    valid_rows = offsets[None, :] < live_count[:, None]
    remaining = (live_count[:, None] - 1 - offsets[None, :]).astype(jnp.float32)
    key_weight = jnp.where(
        valid_rows[:, :, None],
        jnp.exp(-local_rates[None, None, :] * jnp.maximum(remaining, 0.0)[:, :, None]),
        0.0,
    )
    weighted = (keys.astype(jnp.float32) * key_weight[..., None]).astype(jnp.bfloat16)
    update = jnp.einsum("bjhk,bjhv->bhkv", weighted, value_span, preferred_element_type=jnp.float32)
    kept_share = jnp.exp(-local_rates[None, :] * live_count[:, None].astype(jnp.float32))
    state_new = (kept_share[:, :, None, None] * prior_state.astype(jnp.float32) + update).astype(
        jnp.bfloat16
    )
    slots = head_slots
    flat_inputs = decode_inputs.reshape(step_total * total_prompts, model_width)
    query_part = jnp.dot(
        flat_inputs, w_query.reshape(model_width, key_piece), preferred_element_type=jnp.float32
    ).astype(jnp.bfloat16)
    key_part = jnp.dot(
        flat_inputs, w_key.reshape(model_width, key_piece), preferred_element_type=jnp.float32
    ).astype(jnp.bfloat16)
    value_dec = jnp.dot(
        flat_inputs,
        w_value.reshape(model_width, heads_here * value_slice),
        preferred_element_type=jnp.float32,
    ).astype(jnp.bfloat16)
    gate_values = lax.optimization_barrier(
        jnp.dot(
            flat_inputs,
            w_gate.reshape(model_width, heads_here * value_slice),
            preferred_element_type=jnp.float32,
        )
    )
    steps = jnp.arange(step_total)
    halfway = key_width // 2
    head_column = (slot_index * key_piece + jnp.arange(key_piece)) % key_width
    column_frequency = 10000.0 ** (-(head_column // 2).astype(jnp.float32) / halfway)
    dec_positions = (
        (prompt_lengths[None, :] + steps[:, None]).astype(jnp.float32).reshape(-1, 1)
    )
    dec_angles = dec_positions * column_frequency[None, :]
    dec_cosine = jnp.cos(dec_angles)
    dec_sine = jnp.where(head_column % 2 == 0, -1.0, 1.0)[None, :] * jnp.sin(dec_angles)
    lane = jnp.arange(key_piece)
    swap = (lane[:, None] == (lane[None, :] ^ 1)).astype(jnp.bfloat16)
    query_partner = jnp.dot(query_part, swap, preferred_element_type=jnp.float32)
    key_partner = jnp.dot(key_part, swap, preferred_element_type=jnp.float32)
    query_turned = (
        query_part.astype(jnp.float32) * dec_cosine + query_partner * dec_sine
    ).astype(jnp.bfloat16)
    key_turned = (
        (key_part.astype(jnp.float32) * dec_cosine + key_partner * dec_sine)
        * key_width ** (-0.5)
    ).astype(jnp.bfloat16)
    packed = jnp.concatenate([query_turned, key_turned, value_dec], -1)
    packed = packed.reshape(step_total, slots, prompts_here, -1).transpose(1, 0, 2, 3)
    arrived = lax.all_to_all(packed, "heads", 0, 0, tiled=True)
    query_rot = (
        arrived[..., :key_piece]
        .transpose(1, 2, 0, 3)
        .reshape(step_total, prompts_here, heads_here, key_width)
    )
    key_rot = (
        arrived[..., key_piece : 2 * key_piece]
        .transpose(1, 2, 0, 3)
        .reshape(step_total, prompts_here, heads_here, key_width)
    )
    value_own = (
        arrived[..., 2 * key_piece :]
        .reshape(slots, step_total, prompts_here, heads_here, value_slice)
        .transpose(1, 2, 3, 0, 4)
        .reshape(step_total, prompts_here, heads_here, value_width)
    )
    from_state = jnp.einsum(
        "tbhk,bhkv->tbhv", query_rot, state_new, preferred_element_type=jnp.float32
    )
    step_gap = (steps[:, None] - steps[None, :]).astype(jnp.float32)
    step_decay = jnp.where(
        step_gap[None] >= 0,
        jnp.exp(-local_rates[:, None, None] * jnp.maximum(step_gap, 0.0)[None]),
        0.0,
    )
    step_scores = jnp.einsum(
        "tbhk,ubhk->bhtu", query_rot, key_rot, preferred_element_type=jnp.float32
    )
    from_steps = jnp.einsum(
        "bhtu,ubhv->tbhv",
        step_scores * step_decay[None],
        value_own.astype(jnp.float32),
        precision=lax.Precision.HIGHEST,
    )
    state_decay = jnp.exp(-local_rates[None, :] * (steps[:, None] + 1).astype(jnp.float32))
    readout = state_decay[:, None, :, None] * from_state + from_steps
    read_mean = jnp.mean(readout, -1, keepdims=True)
    read_square = jnp.mean(readout * readout, -1, keepdims=True)
    normed = norm_with(readout, read_mean, read_square)
    normed = normed.reshape(step_total, prompts_here, heads_here, slots, value_slice)
    normed = normed.transpose(3, 0, 1, 2, 4)
    normed = lax.all_to_all(normed, "heads", 0, 0, tiled=True)
    normed = normed.transpose(1, 0, 2, 3, 4).reshape(
        step_total, total_prompts, heads_here, value_slice
    )
    gates_steps = gate_values.reshape(step_total, total_prompts, heads_here, value_slice)
    activated = (
        (jax.nn.silu(gates_steps) * normed)
        .astype(jnp.bfloat16)
        .reshape(-1, heads_here * value_slice)
    )
    partial_out = jnp.dot(
        activated,
        w_out.reshape(heads_here * value_slice, model_width),
        preferred_element_type=jnp.float32,
    )
    partial_out = partial_out.reshape(step_total, total_prompts, model_width)
    query_span, key_span, value_span, prior_state, partial_out = lax.optimization_barrier(
        (query_span, key_span, value_span, prior_state, partial_out)
    )
    prefill_out = prefill_output(
        query_span, key_span, value_span, prior_state, local_rates, tables, live_count
    )
    out_slots = head_slots * lax.axis_size("tp")
    column_block = model_width // out_slots
    pieces = partial_out.reshape(step_total, total_prompts, out_slots, column_block)
    pieces = lax.all_to_all(pieces.astype(jnp.bfloat16), ("heads", "tp"), 2, 2, tiled=True)
    decode_out = jnp.sum(pieces.astype(jnp.float32), 2).astype(jnp.bfloat16)
    return (prefill_out, decode_out)


def solution(mesh):
    placed = (
        P(("groups", "heads"), None, "tp", None),
        P(("groups", "heads"), None, "tp", None),
        P(("groups", "heads"), None, "tp", None),
        P(("groups", "heads"), "tp", None, None),
        P(),
        P("groups"),
        P(None, "groups", None),
        P(None, "tp", "heads", None),
        P(None, "tp", "heads", None),
        P(None, "tp", None, "heads", None),
        P(None, "tp", None, "heads", None),
        P("tp", None, "heads", None, None),
    )
    return jax.shard_map(
        per_device,
        mesh=mesh,
        in_specs=placed,
        out_specs=(P(("groups", "heads"), None, "tp", None), P(None, "groups", ("heads", "tp"))),
        check_vma=False,
    )
```

```python
import jax
import jax.numpy as jnp
from jax import lax
from jax.experimental import pallas as pl
from jax.experimental.pallas import tpu as pltpu
from jax.sharding import PartitionSpec as P

EPSILON = 1e-05


def rotate(values, positions):
    halfway = values.shape[-1] // 2
    frequency = 10000.0 ** (-jnp.arange(halfway).astype(jnp.float32) / halfway)
    angles = positions[..., None] * frequency
    cosine = jnp.cos(angles)
    sine_part = jnp.sin(angles)
    paired = values.reshape(values.shape[:-1] + (halfway, 2))
    even_part = paired[..., 0]
    odd_part = paired[..., 1]
    turned = jnp.stack(
        [even_part * cosine - odd_part * sine_part, odd_part * cosine + even_part * sine_part], -1
    )
    return turned.reshape(values.shape)


def norm_with(output, mean_value, mean_square):
    return (output - mean_value) * lax.rsqrt(mean_square - mean_value * mean_value + EPSILON)


def turn_lanes(raw, swap, cosine, sine_part):
    partner = jnp.dot(raw, swap, preferred_element_type=jnp.float32)
    return raw.astype(jnp.float32) * cosine + partner * sine_part


def output_kernel(
    rates_ref, live_ref, q_ref, k_ref, v_ref, prior_ref, cos_ref, sin_ref, swap_ref, out_ref
):
    swap = swap_ref[...]
    cosine = cos_ref[...]
    sine_part = sin_ref[...]
    span_len = q_ref.shape[0]
    live = live_ref[pl.program_id(0)]
    row = lax.broadcasted_iota(jnp.int32, (span_len, span_len), 0)
    column = lax.broadcasted_iota(jnp.int32, (span_len, span_len), 1)
    distance = jnp.maximum(row - column, 0).astype(jnp.float32)
    keep = (row >= column) & (column < live)
    row_index = lax.broadcasted_iota(jnp.int32, (span_len, 1), 0)
    valid = row_index < live
    q_all = q_ref[...]
    k_all = k_ref[...]
    v_all = v_ref[...]
    for head in range(q_ref.shape[1]):
        rate = rates_ref[head]
        q_raw = q_all[:, head, :]
        k_raw = k_all[:, head, :]
        queries = turn_lanes(q_raw, swap, cosine, sine_part).astype(jnp.bfloat16)
        keys = (turn_lanes(k_raw, swap, cosine, sine_part) * (k_raw.shape[-1] ** (-0.5))).astype(
            jnp.bfloat16
        )
        scores = lax.dot_general(
            queries, keys, (((1,), (1,)), ((), ())), preferred_element_type=jnp.float32
        )
        table = jnp.where(keep, jnp.exp(-rate * distance), 0.0)
        weights = (scores * table).astype(jnp.bfloat16)
        inner = jnp.dot(weights, v_all[:, head, :], preferred_element_type=jnp.float32)
        carried = jnp.dot(queries, prior_ref[head], preferred_element_type=jnp.float32)
        lead = jnp.exp(-rate * (row_index + 1).astype(jnp.float32))
        mixed = inner + lead * carried
        mean_value = jnp.mean(mixed, -1, keepdims=True)
        mean_square = jnp.mean(mixed * mixed, -1, keepdims=True)
        normed = norm_with(mixed, mean_value, mean_square)
        out_ref[:, head, :] = jnp.where(valid, normed, 0.0).astype(out_ref.dtype)


def prefill_tables(key_width, span_len, local_rates, span_start, live_count):
    halfway = key_width // 2
    offsets = jnp.arange(span_len)
    positions = (span_start[:, None] + offsets[None, :]).astype(jnp.float32)
    frequency = 10000.0 ** (-jnp.arange(halfway).astype(jnp.float32) / halfway)
    angles = positions[..., None] * frequency
    cosine = jnp.repeat(jnp.cos(angles), 2, axis=-1)
    sine_part = jnp.sin(angles)
    sine_part = jnp.stack([-sine_part, sine_part], -1).reshape(cosine.shape)
    lane = jnp.arange(key_width)
    swap = (lane[:, None] == (lane[None, :] ^ 1)).astype(jnp.bfloat16)
    valid_rows = offsets[None, :] < live_count[:, None]
    lead_decay = jnp.exp(-local_rates[:, None] * (offsets[None, :] + 1).astype(jnp.float32))
    remaining = (live_count[:, None] - 1 - offsets[None, :]).astype(jnp.float32)
    key_weight = jnp.where(
        valid_rows[:, None, :],
        jnp.exp(-local_rates[None, :, None] * jnp.maximum(remaining, 0.0)[:, None, :]),
        0.0,
    )
    kept_share = jnp.exp(-local_rates[None, :] * live_count[:, None].astype(jnp.float32))
    shape_rows = key_weight.shape
    rows = jnp.stack(
        [
            jnp.broadcast_to(lead_decay[None], shape_rows),
            jnp.broadcast_to(valid_rows[:, None, :].astype(jnp.float32), shape_rows),
            key_weight,
            jnp.broadcast_to(kept_share[:, :, None], shape_rows),
        ]
        + [jnp.zeros(shape_rows, jnp.float32)] * 4,
        -1,
    )
    return cosine, sine_part, swap, rows, valid_rows


def prefill_output(query_span, key_span, value_span, prior_state, local_rates, tables, live_count):
    prompts_here, span_len, heads_here, key_width = query_span.shape
    value_width = value_span.shape[3]
    cosine, sine_part, swap, rows, valid_rows = tables
    whole = pl.BlockSpec(memory_space=pltpu.SMEM)
    return pl.pallas_call(
        output_kernel,
        grid=(prompts_here,),
        in_specs=[
            whole,
            whole,
            pl.BlockSpec((None, span_len, heads_here, key_width), lambda b: (b, 0, 0, 0)),
            pl.BlockSpec((None, span_len, heads_here, key_width), lambda b: (b, 0, 0, 0)),
            pl.BlockSpec((None, span_len, heads_here, value_width), lambda b: (b, 0, 0, 0)),
            pl.BlockSpec((None, heads_here, key_width, value_width), lambda b: (b, 0, 0, 0)),
            pl.BlockSpec((None, span_len, key_width), lambda b: (b, 0, 0)),
            pl.BlockSpec((None, span_len, key_width), lambda b: (b, 0, 0)),
            pl.BlockSpec((key_width, key_width), lambda b: (0, 0)),
        ],
        out_specs=pl.BlockSpec(
            (None, span_len, heads_here, value_width), lambda b: (b, 0, 0, 0)
        ),
        out_shape=jax.ShapeDtypeStruct(value_span.shape, jnp.bfloat16),
    )(
        local_rates, live_count.astype(jnp.int32), query_span, key_span, value_span,
        prior_state, cosine, sine_part, swap,
    )


def per_device(
    query_span,
    key_span,
    value_span,
    prior_state,
    decay_rates,
    prompt_lengths,
    decode_inputs,
    w_query,
    w_key,
    w_value,
    w_gate,
    w_out,
):
    prompts_here, span_len, heads_here, key_width = query_span.shape
    value_width = value_span.shape[3]
    model_width = decode_inputs.shape[2]
    step_total = decode_inputs.shape[0]
    head_slots = lax.axis_size("heads")
    total_prompts = prompts_here * head_slots
    key_piece = w_query.shape[3]
    value_slice = w_value.shape[4]
    tp_index = lax.axis_index("tp")
    slot_index = lax.axis_index("heads")
    local_rates = lax.dynamic_slice_in_dim(decay_rates, tp_index * heads_here, heads_here)
    local_lengths = lax.dynamic_slice_in_dim(
        prompt_lengths, slot_index * prompts_here, prompts_here
    )
    span_start = span_len * ((local_lengths - 1) // span_len)
    live_count = local_lengths - span_start
    tables = prefill_tables(key_width, span_len, local_rates, span_start, live_count)
    offsets = jnp.arange(span_len)
    positions = (span_start[:, None] + offsets[None, :]).astype(jnp.float32)
    cosine, sine_part, swap = tables[:3]
    key_partner = jnp.einsum("bihk,kl->bihl", key_span, swap, preferred_element_type=jnp.float32)
    keys = (
        (key_span.astype(jnp.float32) * cosine[:, :, None, :] + key_partner * sine_part[:, :, None, :])
        * key_width ** (-0.5)
    ).astype(jnp.bfloat16)
    valid_rows = offsets[None, :] < live_count[:, None]
    remaining = (live_count[:, None] - 1 - offsets[None, :]).astype(jnp.float32)
    key_weight = jnp.where(
        valid_rows[:, :, None],
        jnp.exp(-local_rates[None, None, :] * jnp.maximum(remaining, 0.0)[:, :, None]),
        0.0,
    )
    weighted = (keys.astype(jnp.float32) * key_weight[..., None]).astype(jnp.bfloat16)
    update = jnp.einsum("bjhk,bjhv->bhkv", weighted, value_span, preferred_element_type=jnp.float32)
    kept_share = jnp.exp(-local_rates[None, :] * live_count[:, None].astype(jnp.float32))
    state_new = (kept_share[:, :, None, None] * prior_state.astype(jnp.float32) + update).astype(
        jnp.bfloat16
    )
    slots = head_slots
    flat_inputs = decode_inputs.reshape(step_total * total_prompts, model_width)
    query_part = jnp.dot(
        flat_inputs, w_query.reshape(model_width, key_piece), preferred_element_type=jnp.float32
    ).astype(jnp.bfloat16)
    key_part = jnp.dot(
        flat_inputs, w_key.reshape(model_width, key_piece), preferred_element_type=jnp.float32
    ).astype(jnp.bfloat16)
    value_dec = jnp.dot(
        flat_inputs,
        w_value.reshape(model_width, heads_here * value_slice),
        preferred_element_type=jnp.float32,
    ).astype(jnp.bfloat16)
    gate_values = lax.optimization_barrier(
        jnp.dot(
            flat_inputs,
            w_gate.reshape(model_width, heads_here * value_slice),
            preferred_element_type=jnp.float32,
        )
    )
    steps = jnp.arange(step_total)
    halfway = key_width // 2
    head_column = (slot_index * key_piece + jnp.arange(key_piece)) % key_width
    column_frequency = 10000.0 ** (-(head_column // 2).astype(jnp.float32) / halfway)
    dec_positions = (
        (prompt_lengths[None, :] + steps[:, None]).astype(jnp.float32).reshape(-1, 1)
    )
    dec_angles = dec_positions * column_frequency[None, :]
    dec_cosine = jnp.cos(dec_angles)
    dec_sine = jnp.where(head_column % 2 == 0, -1.0, 1.0)[None, :] * jnp.sin(dec_angles)
    lane = jnp.arange(key_piece)
    swap = (lane[:, None] == (lane[None, :] ^ 1)).astype(jnp.bfloat16)
    query_partner = jnp.dot(query_part, swap, preferred_element_type=jnp.float32)
    key_partner = jnp.dot(key_part, swap, preferred_element_type=jnp.float32)
    query_turned = (
        query_part.astype(jnp.float32) * dec_cosine + query_partner * dec_sine
    ).astype(jnp.bfloat16)
    key_turned = (
        (key_part.astype(jnp.float32) * dec_cosine + key_partner * dec_sine)
        * key_width ** (-0.5)
    ).astype(jnp.bfloat16)
    packed = jnp.concatenate([query_turned, key_turned, value_dec], -1)
    packed = packed.reshape(step_total, slots, prompts_here, -1).transpose(1, 0, 2, 3)
    arrived = lax.all_to_all(packed, "heads", 0, 0, tiled=True)
    query_rot = (
        arrived[..., :key_piece]
        .transpose(1, 2, 0, 3)
        .reshape(step_total, prompts_here, heads_here, key_width)
    )
    key_rot = (
        arrived[..., key_piece : 2 * key_piece]
        .transpose(1, 2, 0, 3)
        .reshape(step_total, prompts_here, heads_here, key_width)
    )
    value_own = (
        arrived[..., 2 * key_piece :]
        .reshape(slots, step_total, prompts_here, heads_here, value_slice)
        .transpose(1, 2, 3, 0, 4)
        .reshape(step_total, prompts_here, heads_here, value_width)
    )
    from_state = jnp.einsum(
        "tbhk,bhkv->tbhv", query_rot, state_new, preferred_element_type=jnp.float32
    )
    step_gap = (steps[:, None] - steps[None, :]).astype(jnp.float32)
    step_decay = jnp.where(
        step_gap[None] >= 0,
        jnp.exp(-local_rates[:, None, None] * jnp.maximum(step_gap, 0.0)[None]),
        0.0,
    )
    step_scores = jnp.einsum(
        "tbhk,ubhk->bhtu", query_rot, key_rot, preferred_element_type=jnp.float32
    )
    from_steps = jnp.einsum(
        "bhtu,ubhv->tbhv",
        step_scores * step_decay[None],
        value_own.astype(jnp.float32),
        precision=lax.Precision.HIGHEST,
    )
    state_decay = jnp.exp(-local_rates[None, :] * (steps[:, None] + 1).astype(jnp.float32))
    readout = state_decay[:, None, :, None] * from_state + from_steps
    read_mean = jnp.mean(readout, -1, keepdims=True)
    read_square = jnp.mean(readout * readout, -1, keepdims=True)
    normed = norm_with(readout, read_mean, read_square)
    normed = normed.reshape(step_total, prompts_here, heads_here, slots, value_slice)
    normed = normed.transpose(3, 0, 1, 2, 4)
    normed = lax.all_to_all(normed, "heads", 0, 0, tiled=True)
    normed = normed.transpose(1, 0, 2, 3, 4).reshape(
        step_total, total_prompts, heads_here, value_slice
    )
    gates_steps = gate_values.reshape(step_total, total_prompts, heads_here, value_slice)
    activated = (
        (jax.nn.silu(gates_steps) * normed)
        .astype(jnp.bfloat16)
        .reshape(-1, heads_here * value_slice)
    )
    partial_out = jnp.dot(
        activated,
        w_out.reshape(heads_here * value_slice, model_width),
        preferred_element_type=jnp.float32,
    )
    partial_out = partial_out.reshape(step_total, total_prompts, model_width)
    query_span, key_span, value_span, prior_state, partial_out = lax.optimization_barrier(
        (query_span, key_span, value_span, prior_state, partial_out)
    )
    prefill_out = prefill_output(
        query_span, key_span, value_span, prior_state, local_rates, tables, live_count
    )
    out_slots = head_slots * lax.axis_size("tp")
    column_block = model_width // out_slots
    pieces = partial_out.reshape(step_total, total_prompts, out_slots, column_block)
    pieces = lax.all_to_all(pieces.astype(jnp.bfloat16), ("heads", "tp"), 2, 2, tiled=True)
    decode_out = jnp.sum(pieces.astype(jnp.float32), 2).astype(jnp.bfloat16)
    return (prefill_out, decode_out)


def solution(mesh):
    placed = (
        P(("groups", "heads"), None, "tp", None),
        P(("groups", "heads"), None, "tp", None),
        P(("groups", "heads"), None, "tp", None),
        P(("groups", "heads"), "tp", None, None),
        P(),
        P("groups"),
        P(None, "groups", None),
        P(None, "tp", "heads", None),
        P(None, "tp", "heads", None),
        P(None, "tp", None, "heads", None),
        P(None, "tp", None, "heads", None),
        P("tp", None, "heads", None, None),
    )
    return jax.shard_map(
        per_device,
        mesh=mesh,
        in_specs=placed,
        out_specs=(P(("groups", "heads"), None, "tp", None), P(None, "groups", ("heads", "tp"))),
        check_vma=False,
    )
```

```python
import jax
import jax.numpy as jnp
from jax import lax
from jax.experimental import pallas as pl
from jax.experimental.pallas import tpu as pltpu
from jax.sharding import PartitionSpec as P

EPSILON = 1e-05


def rotate(values, positions):
    halfway = values.shape[-1] // 2
    frequency = 10000.0 ** (-jnp.arange(halfway).astype(jnp.float32) / halfway)
    angles = positions[..., None] * frequency
    cosine = jnp.cos(angles)
    sine_part = jnp.sin(angles)
    paired = values.reshape(values.shape[:-1] + (halfway, 2))
    even_part = paired[..., 0]
    odd_part = paired[..., 1]
    turned = jnp.stack(
        [even_part * cosine - odd_part * sine_part, odd_part * cosine + even_part * sine_part], -1
    )
    return turned.reshape(values.shape)


def norm_with(output, mean_value, mean_square):
    return (output - mean_value) * lax.rsqrt(mean_square - mean_value * mean_value + EPSILON)


def turn_lanes(raw, swap, cosine, sine_part):
    partner = jnp.dot(raw, swap, preferred_element_type=jnp.float32)
    return raw.astype(jnp.float32) * cosine + partner * sine_part


def output_kernel(
    rates_ref, live_ref, q_ref, k_ref, v_ref, prior_ref, cos_ref, sin_ref, swap_ref, out_ref
):
    swap = swap_ref[...]
    cosine = cos_ref[...]
    sine_part = sin_ref[...]
    span_len = q_ref.shape[0]
    live = live_ref[pl.program_id(0)]
    row = lax.broadcasted_iota(jnp.int32, (span_len, span_len), 0)
    column = lax.broadcasted_iota(jnp.int32, (span_len, span_len), 1)
    distance = jnp.maximum(row - column, 0).astype(jnp.float32)
    keep = (row >= column) & (column < live)
    row_index = lax.broadcasted_iota(jnp.int32, (span_len, 1), 0)
    valid = row_index < live
    q_all = q_ref[...]
    k_all = k_ref[...]
    v_all = v_ref[...]
    for head in range(q_ref.shape[1]):
        rate = rates_ref[head]
        q_raw = q_all[:, head, :]
        k_raw = k_all[:, head, :]
        queries = turn_lanes(q_raw, swap, cosine, sine_part).astype(jnp.bfloat16)
        keys = (turn_lanes(k_raw, swap, cosine, sine_part) * (k_raw.shape[-1] ** (-0.5))).astype(
            jnp.bfloat16
        )
        scores = lax.dot_general(
            queries, keys, (((1,), (1,)), ((), ())), preferred_element_type=jnp.float32
        )
        table = jnp.where(keep, jnp.exp(-rate * distance), 0.0)
        weights = (scores * table).astype(jnp.bfloat16)
        inner = jnp.dot(weights, v_all[:, head, :], preferred_element_type=jnp.float32)
        carried = jnp.dot(queries, prior_ref[head], preferred_element_type=jnp.float32)
        lead = jnp.exp(-rate * (row_index + 1).astype(jnp.float32))
        mixed = inner + lead * carried
        mean_value = jnp.mean(mixed, -1, keepdims=True)
        mean_square = jnp.mean(mixed * mixed, -1, keepdims=True)
        normed = norm_with(mixed, mean_value, mean_square)
        out_ref[:, head, :] = jnp.where(valid, normed, 0.0).astype(out_ref.dtype)


def prefill_tables(key_width, span_len, local_rates, span_start, live_count):
    halfway = key_width // 2
    offsets = jnp.arange(span_len)
    positions = (span_start[:, None] + offsets[None, :]).astype(jnp.float32)
    frequency = 10000.0 ** (-jnp.arange(halfway).astype(jnp.float32) / halfway)
    angles = positions[..., None] * frequency
    cosine = jnp.repeat(jnp.cos(angles), 2, axis=-1)
    sine_part = jnp.sin(angles)
    sine_part = jnp.stack([-sine_part, sine_part], -1).reshape(cosine.shape)
    lane = jnp.arange(key_width)
    swap = (lane[:, None] == (lane[None, :] ^ 1)).astype(jnp.bfloat16)
    valid_rows = offsets[None, :] < live_count[:, None]
    lead_decay = jnp.exp(-local_rates[:, None] * (offsets[None, :] + 1).astype(jnp.float32))
    remaining = (live_count[:, None] - 1 - offsets[None, :]).astype(jnp.float32)
    key_weight = jnp.where(
        valid_rows[:, None, :],
        jnp.exp(-local_rates[None, :, None] * jnp.maximum(remaining, 0.0)[:, None, :]),
        0.0,
    )
    kept_share = jnp.exp(-local_rates[None, :] * live_count[:, None].astype(jnp.float32))
    shape_rows = key_weight.shape
    rows = jnp.stack(
        [
            jnp.broadcast_to(lead_decay[None], shape_rows),
            jnp.broadcast_to(valid_rows[:, None, :].astype(jnp.float32), shape_rows),
            key_weight,
            jnp.broadcast_to(kept_share[:, :, None], shape_rows),
        ]
        + [jnp.zeros(shape_rows, jnp.float32)] * 4,
        -1,
    )
    return cosine, sine_part, swap, rows, valid_rows


def prefill_output(query_span, key_span, value_span, prior_state, local_rates, tables, live_count):
    prompts_here, span_len, heads_here, key_width = query_span.shape
    value_width = value_span.shape[3]
    cosine, sine_part, swap, rows, valid_rows = tables
    whole = pl.BlockSpec(memory_space=pltpu.SMEM)
    return pl.pallas_call(
        output_kernel,
        grid=(prompts_here,),
        in_specs=[
            whole,
            whole,
            pl.BlockSpec((None, span_len, heads_here, key_width), lambda b: (b, 0, 0, 0)),
            pl.BlockSpec((None, span_len, heads_here, key_width), lambda b: (b, 0, 0, 0)),
            pl.BlockSpec((None, span_len, heads_here, value_width), lambda b: (b, 0, 0, 0)),
            pl.BlockSpec((None, heads_here, key_width, value_width), lambda b: (b, 0, 0, 0)),
            pl.BlockSpec((None, span_len, key_width), lambda b: (b, 0, 0)),
            pl.BlockSpec((None, span_len, key_width), lambda b: (b, 0, 0)),
            pl.BlockSpec((key_width, key_width), lambda b: (0, 0)),
        ],
        out_specs=pl.BlockSpec(
            (None, span_len, heads_here, value_width), lambda b: (b, 0, 0, 0)
        ),
        out_shape=jax.ShapeDtypeStruct(value_span.shape, jnp.bfloat16),
    )(
        local_rates, live_count.astype(jnp.int32), query_span, key_span, value_span,
        prior_state, cosine, sine_part, swap,
    )


def per_device(
    query_span,
    key_span,
    value_span,
    prior_state,
    decay_rates,
    prompt_lengths,
    decode_inputs,
    w_query,
    w_key,
    w_value,
    w_gate,
    w_out,
):
    prompts_here, span_len, heads_here, key_width = query_span.shape
    value_width = value_span.shape[3]
    model_width = decode_inputs.shape[2]
    step_total = decode_inputs.shape[0]
    head_slots = lax.axis_size("heads")
    total_prompts = prompts_here * head_slots
    key_piece = w_query.shape[3]
    value_slice = w_value.shape[4]
    tp_index = lax.axis_index("tp")
    slot_index = lax.axis_index("heads")
    local_rates = lax.dynamic_slice_in_dim(decay_rates, tp_index * heads_here, heads_here)
    local_lengths = lax.dynamic_slice_in_dim(
        prompt_lengths, slot_index * prompts_here, prompts_here
    )
    span_start = span_len * ((local_lengths - 1) // span_len)
    live_count = local_lengths - span_start
    tables = prefill_tables(key_width, span_len, local_rates, span_start, live_count)
    offsets = jnp.arange(span_len)
    positions = (span_start[:, None] + offsets[None, :]).astype(jnp.float32)
    cosine, sine_part, swap = tables[:3]
    key_partner = jnp.einsum("bihk,kl->bihl", key_span, swap, preferred_element_type=jnp.float32)
    keys = (
        (key_span.astype(jnp.float32) * cosine[:, :, None, :] + key_partner * sine_part[:, :, None, :])
        * key_width ** (-0.5)
    ).astype(jnp.bfloat16)
    valid_rows = offsets[None, :] < live_count[:, None]
    remaining = (live_count[:, None] - 1 - offsets[None, :]).astype(jnp.float32)
    key_weight = jnp.where(
        valid_rows[:, :, None],
        jnp.exp(-local_rates[None, None, :] * jnp.maximum(remaining, 0.0)[:, :, None]),
        0.0,
    )
    weighted = (keys.astype(jnp.float32) * key_weight[..., None]).astype(jnp.bfloat16)
    update = jnp.einsum("bjhk,bjhv->bhkv", weighted, value_span, preferred_element_type=jnp.float32)
    kept_share = jnp.exp(-local_rates[None, :] * live_count[:, None].astype(jnp.float32))
    state_new = (kept_share[:, :, None, None] * prior_state.astype(jnp.float32) + update).astype(
        jnp.bfloat16
    )
    slots = head_slots
    flat_inputs = decode_inputs.reshape(step_total * total_prompts, model_width)
    query_part = jnp.dot(
        flat_inputs, w_query.reshape(model_width, key_piece), preferred_element_type=jnp.float32
    ).astype(jnp.bfloat16)
    key_part = jnp.dot(
        flat_inputs, w_key.reshape(model_width, key_piece), preferred_element_type=jnp.float32
    ).astype(jnp.bfloat16)
    value_dec = jnp.dot(
        flat_inputs,
        w_value.reshape(model_width, heads_here * value_slice),
        preferred_element_type=jnp.float32,
    ).astype(jnp.bfloat16)
    gate_values = lax.optimization_barrier(
        jnp.dot(
            flat_inputs,
            w_gate.reshape(model_width, heads_here * value_slice),
            preferred_element_type=jnp.float32,
        )
    )
    steps = jnp.arange(step_total)
    halfway = key_width // 2
    head_column = (slot_index * key_piece + jnp.arange(key_piece)) % key_width
    column_frequency = 10000.0 ** (-(head_column // 2).astype(jnp.float32) / halfway)
    dec_positions = (
        (prompt_lengths[None, :] + steps[:, None]).astype(jnp.float32).reshape(-1, 1)
    )
    dec_angles = dec_positions * column_frequency[None, :]
    dec_cosine = jnp.cos(dec_angles)
    dec_sine = jnp.where(head_column % 2 == 0, -1.0, 1.0)[None, :] * jnp.sin(dec_angles)
    lane = jnp.arange(key_piece)
    swap = (lane[:, None] == (lane[None, :] ^ 1)).astype(jnp.bfloat16)
    query_partner = jnp.dot(query_part, swap, preferred_element_type=jnp.float32)
    key_partner = jnp.dot(key_part, swap, preferred_element_type=jnp.float32)
    query_turned = (
        query_part.astype(jnp.float32) * dec_cosine + query_partner * dec_sine
    ).astype(jnp.bfloat16)
    key_turned = (
        (key_part.astype(jnp.float32) * dec_cosine + key_partner * dec_sine)
        * key_width ** (-0.5)
    ).astype(jnp.bfloat16)
    packed = jnp.concatenate([query_turned, key_turned, value_dec], -1)
    packed = packed.reshape(step_total, slots, prompts_here, -1).transpose(1, 0, 2, 3)
    arrived = lax.all_to_all(packed, "heads", 0, 0, tiled=True)
    query_rot = (
        arrived[..., :key_piece]
        .transpose(1, 2, 0, 3)
        .reshape(step_total, prompts_here, heads_here, key_width)
    )
    key_rot = (
        arrived[..., key_piece : 2 * key_piece]
        .transpose(1, 2, 0, 3)
        .reshape(step_total, prompts_here, heads_here, key_width)
    )
    value_own = (
        arrived[..., 2 * key_piece :]
        .reshape(slots, step_total, prompts_here, heads_here, value_slice)
        .transpose(1, 2, 3, 0, 4)
        .reshape(step_total, prompts_here, heads_here, value_width)
    )
    from_state = jnp.einsum(
        "tbhk,bhkv->tbhv", query_rot, state_new, preferred_element_type=jnp.float32
    )
    step_gap = (steps[:, None] - steps[None, :]).astype(jnp.float32)
    step_decay = jnp.where(
        step_gap[None] >= 0,
        jnp.exp(-local_rates[:, None, None] * jnp.maximum(step_gap, 0.0)[None]),
        0.0,
    )
    step_scores = jnp.einsum(
        "tbhk,ubhk->bhtu", query_rot, key_rot, preferred_element_type=jnp.float32
    )
    from_steps = jnp.einsum(
        "bhtu,ubhv->tbhv",
        step_scores * step_decay[None],
        value_own.astype(jnp.float32),
        precision=lax.Precision.HIGHEST,
    )
    state_decay = jnp.exp(-local_rates[None, :] * (steps[:, None] + 1).astype(jnp.float32))
    readout = state_decay[:, None, :, None] * from_state + from_steps
    read_mean = jnp.mean(readout, -1, keepdims=True)
    read_square = jnp.mean(readout * readout, -1, keepdims=True)
    normed = norm_with(readout, read_mean, read_square)
    normed = normed.reshape(step_total, prompts_here, heads_here, slots, value_slice)
    normed = normed.transpose(3, 0, 1, 2, 4)
    normed = lax.all_to_all(normed.astype(jnp.bfloat16), "heads", 0, 0, tiled=True)
    normed = normed.transpose(1, 0, 2, 3, 4).reshape(
        step_total, total_prompts, heads_here, value_slice
    ).astype(jnp.float32)
    gates_steps = gate_values.reshape(step_total, total_prompts, heads_here, value_slice)
    activated = (
        (jax.nn.silu(gates_steps) * normed)
        .astype(jnp.bfloat16)
        .reshape(-1, heads_here * value_slice)
    )
    partial_out = jnp.dot(
        activated,
        w_out.reshape(heads_here * value_slice, model_width),
        preferred_element_type=jnp.float32,
    )
    partial_out = partial_out.reshape(step_total, total_prompts, model_width)
    query_span, key_span, value_span, prior_state, partial_out = lax.optimization_barrier(
        (query_span, key_span, value_span, prior_state, partial_out)
    )
    prefill_out = prefill_output(
        query_span, key_span, value_span, prior_state, local_rates, tables, live_count
    )
    out_slots = head_slots * lax.axis_size("tp")
    column_block = model_width // out_slots
    pieces = partial_out.reshape(step_total, total_prompts, out_slots, column_block)
    pieces = lax.all_to_all(pieces.astype(jnp.bfloat16), ("heads", "tp"), 2, 2, tiled=True)
    decode_out = jnp.sum(pieces.astype(jnp.float32), 2).astype(jnp.bfloat16)
    return (prefill_out, decode_out)


def solution(mesh):
    placed = (
        P(("groups", "heads"), None, "tp", None),
        P(("groups", "heads"), None, "tp", None),
        P(("groups", "heads"), None, "tp", None),
        P(("groups", "heads"), "tp", None, None),
        P(),
        P("groups"),
        P(None, "groups", None),
        P(None, "tp", "heads", None),
        P(None, "tp", "heads", None),
        P(None, "tp", None, "heads", None),
        P(None, "tp", None, "heads", None),
        P("tp", None, "heads", None, None),
    )
    return jax.shard_map(
        per_device,
        mesh=mesh,
        in_specs=placed,
        out_specs=(P(("groups", "heads"), None, "tp", None), P(None, "groups", ("heads", "tp"))),
        check_vma=False,
    )
```

```python
import jax
import jax.numpy as jnp
from jax import lax
from jax.experimental import pallas as pl
from jax.experimental.pallas import tpu as pltpu
from jax.sharding import PartitionSpec as P

EPSILON = 1e-05


def rotate(values, positions):
    halfway = values.shape[-1] // 2
    frequency = 10000.0 ** (-jnp.arange(halfway).astype(jnp.float32) / halfway)
    angles = positions[..., None] * frequency
    cosine = jnp.cos(angles)
    sine_part = jnp.sin(angles)
    paired = values.reshape(values.shape[:-1] + (halfway, 2))
    even_part = paired[..., 0]
    odd_part = paired[..., 1]
    turned = jnp.stack(
        [even_part * cosine - odd_part * sine_part, odd_part * cosine + even_part * sine_part], -1
    )
    return turned.reshape(values.shape)


def norm_with(output, mean_value, mean_square):
    return (output - mean_value) * lax.rsqrt(mean_square - mean_value * mean_value + EPSILON)


def turn_lanes(raw, swap, cosine, sine_part):
    partner = jnp.dot(raw, swap, preferred_element_type=jnp.float32)
    return raw.astype(jnp.float32) * cosine + partner * sine_part


def output_kernel(
    rates_ref, live_ref, q_ref, k_ref, v_ref, prior_ref, cos_ref, sin_ref, swap_ref, out_ref
):
    swap = swap_ref[...]
    cosine = cos_ref[...]
    sine_part = sin_ref[...]
    span_len = q_ref.shape[0]
    live = live_ref[pl.program_id(0)]
    row = lax.broadcasted_iota(jnp.int32, (span_len, span_len), 0)
    column = lax.broadcasted_iota(jnp.int32, (span_len, span_len), 1)
    distance = jnp.maximum(row - column, 0).astype(jnp.float32)
    keep = (row >= column) & (column < live)
    row_index = lax.broadcasted_iota(jnp.int32, (span_len, 1), 0)
    valid = row_index < live
    q_all = q_ref[...]
    k_all = k_ref[...]
    v_all = v_ref[...]
    for head in range(q_ref.shape[1]):
        rate = rates_ref[head]
        q_raw = q_all[:, head, :]
        k_raw = k_all[:, head, :]
        queries = turn_lanes(q_raw, swap, cosine, sine_part).astype(jnp.bfloat16)
        keys = (turn_lanes(k_raw, swap, cosine, sine_part) * (k_raw.shape[-1] ** (-0.5))).astype(
            jnp.bfloat16
        )
        scores = lax.dot_general(
            queries, keys, (((1,), (1,)), ((), ())), preferred_element_type=jnp.float32
        )
        table = jnp.where(keep, jnp.exp(-rate * distance), 0.0)
        weights = (scores * table).astype(jnp.bfloat16)
        inner = jnp.dot(weights, v_all[:, head, :], preferred_element_type=jnp.float32)
        carried = jnp.dot(queries, prior_ref[head], preferred_element_type=jnp.float32)
        lead = jnp.exp(-rate * (row_index + 1).astype(jnp.float32))
        mixed = inner + lead * carried
        mean_value = jnp.mean(mixed, -1, keepdims=True)
        mean_square = jnp.mean(mixed * mixed, -1, keepdims=True)
        normed = norm_with(mixed, mean_value, mean_square)
        out_ref[:, head, :] = jnp.where(valid, normed, 0.0).astype(out_ref.dtype)


def prefill_tables(key_width, span_len, local_rates, span_start, live_count):
    halfway = key_width // 2
    offsets = jnp.arange(span_len)
    positions = (span_start[:, None] + offsets[None, :]).astype(jnp.float32)
    frequency = 10000.0 ** (-jnp.arange(halfway).astype(jnp.float32) / halfway)
    angles = positions[..., None] * frequency
    cosine = jnp.repeat(jnp.cos(angles), 2, axis=-1)
    sine_part = jnp.sin(angles)
    sine_part = jnp.stack([-sine_part, sine_part], -1).reshape(cosine.shape)
    lane = jnp.arange(key_width)
    swap = (lane[:, None] == (lane[None, :] ^ 1)).astype(jnp.bfloat16)
    valid_rows = offsets[None, :] < live_count[:, None]
    lead_decay = jnp.exp(-local_rates[:, None] * (offsets[None, :] + 1).astype(jnp.float32))
    remaining = (live_count[:, None] - 1 - offsets[None, :]).astype(jnp.float32)
    key_weight = jnp.where(
        valid_rows[:, None, :],
        jnp.exp(-local_rates[None, :, None] * jnp.maximum(remaining, 0.0)[:, None, :]),
        0.0,
    )
    kept_share = jnp.exp(-local_rates[None, :] * live_count[:, None].astype(jnp.float32))
    shape_rows = key_weight.shape
    rows = jnp.stack(
        [
            jnp.broadcast_to(lead_decay[None], shape_rows),
            jnp.broadcast_to(valid_rows[:, None, :].astype(jnp.float32), shape_rows),
            key_weight,
            jnp.broadcast_to(kept_share[:, :, None], shape_rows),
        ]
        + [jnp.zeros(shape_rows, jnp.float32)] * 4,
        -1,
    )
    return cosine, sine_part, swap, rows, valid_rows


def prefill_output(
    query_span, key_span, value_span, prior_state, local_rates, tables, live_count,
    first, count, earlier,
):
    prompts_here, span_len, heads_here, key_width = query_span.shape
    value_width = value_span.shape[3]
    cosine, sine_part, swap, rows, valid_rows = tables
    whole = pl.BlockSpec(memory_space=pltpu.SMEM)
    in_specs = [
        whole,
        whole,
        pl.BlockSpec((None, span_len, heads_here, key_width), lambda i: (first + i, 0, 0, 0)),
        pl.BlockSpec((None, span_len, heads_here, key_width), lambda i: (first + i, 0, 0, 0)),
        pl.BlockSpec((None, span_len, heads_here, value_width), lambda i: (first + i, 0, 0, 0)),
        pl.BlockSpec((None, heads_here, key_width, value_width), lambda i: (first + i, 0, 0, 0)),
        pl.BlockSpec((None, span_len, key_width), lambda i: (first + i, 0, 0)),
        pl.BlockSpec((None, span_len, key_width), lambda i: (first + i, 0, 0)),
        pl.BlockSpec((key_width, key_width), lambda i: (0, 0)),
    ]
    operands = [
        local_rates, live_count[first : first + count].astype(jnp.int32), query_span, key_span,
        value_span, prior_state, cosine, sine_part, swap,
    ]
    kernel = output_kernel
    aliases = {}
    if earlier is not None:
        in_specs.append(pl.BlockSpec(memory_space=pl.ANY))
        operands.append(earlier)
        aliases = {len(operands) - 1: 0}

        def kernel(*refs):
            output_kernel(*refs[:9], refs[10])

    return pl.pallas_call(
        kernel,
        grid=(count,),
        in_specs=in_specs,
        out_specs=pl.BlockSpec(
            (None, span_len, heads_here, value_width), lambda i: (first + i, 0, 0, 0)
        ),
        out_shape=jax.ShapeDtypeStruct(value_span.shape, jnp.bfloat16),
        input_output_aliases=aliases,
    )(*operands)


def per_device(
    query_span,
    key_span,
    value_span,
    prior_state,
    decay_rates,
    prompt_lengths,
    decode_inputs,
    w_query,
    w_key,
    w_value,
    w_gate,
    w_out,
):
    prompts_here, span_len, heads_here, key_width = query_span.shape
    value_width = value_span.shape[3]
    model_width = decode_inputs.shape[2]
    step_total = decode_inputs.shape[0]
    head_slots = lax.axis_size("heads")
    total_prompts = prompts_here * head_slots
    key_piece = w_query.shape[3]
    value_slice = w_value.shape[4]
    tp_index = lax.axis_index("tp")
    slot_index = lax.axis_index("heads")
    local_rates = lax.dynamic_slice_in_dim(decay_rates, tp_index * heads_here, heads_here)
    local_lengths = lax.dynamic_slice_in_dim(
        prompt_lengths, slot_index * prompts_here, prompts_here
    )
    span_start = span_len * ((local_lengths - 1) // span_len)
    live_count = local_lengths - span_start
    tables = prefill_tables(key_width, span_len, local_rates, span_start, live_count)
    offsets = jnp.arange(span_len)
    positions = (span_start[:, None] + offsets[None, :]).astype(jnp.float32)
    cosine, sine_part, swap = tables[:3]
    key_partner = jnp.einsum("bihk,kl->bihl", key_span, swap, preferred_element_type=jnp.float32)
    keys = (
        (key_span.astype(jnp.float32) * cosine[:, :, None, :] + key_partner * sine_part[:, :, None, :])
        * key_width ** (-0.5)
    ).astype(jnp.bfloat16)
    valid_rows = offsets[None, :] < live_count[:, None]
    remaining = (live_count[:, None] - 1 - offsets[None, :]).astype(jnp.float32)
    key_weight = jnp.where(
        valid_rows[:, :, None],
        jnp.exp(-local_rates[None, None, :] * jnp.maximum(remaining, 0.0)[:, :, None]),
        0.0,
    )
    weighted = (keys.astype(jnp.float32) * key_weight[..., None]).astype(jnp.bfloat16)
    update = jnp.einsum("bjhk,bjhv->bhkv", weighted, value_span, preferred_element_type=jnp.float32)
    kept_share = jnp.exp(-local_rates[None, :] * live_count[:, None].astype(jnp.float32))
    state_new = (kept_share[:, :, None, None] * prior_state.astype(jnp.float32) + update).astype(
        jnp.bfloat16
    )
    slots = head_slots
    flat_inputs = decode_inputs.reshape(step_total * total_prompts, model_width)
    query_part = jnp.dot(
        flat_inputs, w_query.reshape(model_width, key_piece), preferred_element_type=jnp.float32
    ).astype(jnp.bfloat16)
    key_part = jnp.dot(
        flat_inputs, w_key.reshape(model_width, key_piece), preferred_element_type=jnp.float32
    ).astype(jnp.bfloat16)
    value_dec = jnp.dot(
        flat_inputs,
        w_value.reshape(model_width, heads_here * value_slice),
        preferred_element_type=jnp.float32,
    ).astype(jnp.bfloat16)
    gate_values = lax.optimization_barrier(
        jnp.dot(
            flat_inputs,
            w_gate.reshape(model_width, heads_here * value_slice),
            preferred_element_type=jnp.float32,
        )
    )
    steps = jnp.arange(step_total)
    halfway = key_width // 2
    head_column = (slot_index * key_piece + jnp.arange(key_piece)) % key_width
    column_frequency = 10000.0 ** (-(head_column // 2).astype(jnp.float32) / halfway)
    dec_positions = (
        (prompt_lengths[None, :] + steps[:, None]).astype(jnp.float32).reshape(-1, 1)
    )
    dec_angles = dec_positions * column_frequency[None, :]
    dec_cosine = jnp.cos(dec_angles)
    dec_sine = jnp.where(head_column % 2 == 0, -1.0, 1.0)[None, :] * jnp.sin(dec_angles)
    lane = jnp.arange(key_piece)
    swap = (lane[:, None] == (lane[None, :] ^ 1)).astype(jnp.bfloat16)
    query_partner = jnp.dot(query_part, swap, preferred_element_type=jnp.float32)
    key_partner = jnp.dot(key_part, swap, preferred_element_type=jnp.float32)
    query_turned = (
        query_part.astype(jnp.float32) * dec_cosine + query_partner * dec_sine
    ).astype(jnp.bfloat16)
    key_turned = (
        (key_part.astype(jnp.float32) * dec_cosine + key_partner * dec_sine)
        * key_width ** (-0.5)
    ).astype(jnp.bfloat16)
    packed = jnp.concatenate([query_turned, key_turned, value_dec], -1)
    packed = packed.reshape(step_total, slots, prompts_here, -1).transpose(1, 0, 2, 3)
    arrived = lax.all_to_all(packed, "heads", 0, 0, tiled=True)
    query_rot = (
        arrived[..., :key_piece]
        .transpose(1, 2, 0, 3)
        .reshape(step_total, prompts_here, heads_here, key_width)
    )
    key_rot = (
        arrived[..., key_piece : 2 * key_piece]
        .transpose(1, 2, 0, 3)
        .reshape(step_total, prompts_here, heads_here, key_width)
    )
    value_own = (
        arrived[..., 2 * key_piece :]
        .reshape(slots, step_total, prompts_here, heads_here, value_slice)
        .transpose(1, 2, 3, 0, 4)
        .reshape(step_total, prompts_here, heads_here, value_width)
    )
    from_state = jnp.einsum(
        "tbhk,bhkv->tbhv", query_rot, state_new, preferred_element_type=jnp.float32
    )
    step_gap = (steps[:, None] - steps[None, :]).astype(jnp.float32)
    step_decay = jnp.where(
        step_gap[None] >= 0,
        jnp.exp(-local_rates[:, None, None] * jnp.maximum(step_gap, 0.0)[None]),
        0.0,
    )
    step_scores = jnp.einsum(
        "tbhk,ubhk->bhtu", query_rot, key_rot, preferred_element_type=jnp.float32
    )
    from_steps = jnp.einsum(
        "bhtu,ubhv->tbhv",
        step_scores * step_decay[None],
        value_own.astype(jnp.float32),
        precision=lax.Precision.HIGHEST,
    )
    state_decay = jnp.exp(-local_rates[None, :] * (steps[:, None] + 1).astype(jnp.float32))
    readout = state_decay[:, None, :, None] * from_state + from_steps
    read_mean = jnp.mean(readout, -1, keepdims=True)
    read_square = jnp.mean(readout * readout, -1, keepdims=True)
    normed = norm_with(readout, read_mean, read_square)
    normed = normed.reshape(step_total, prompts_here, heads_here, slots, value_slice)
    normed = normed.transpose(3, 0, 1, 2, 4)
    first_half = prompts_here // 2
    q_early, k_early, v_early, prior_early, normed = lax.optimization_barrier(
        (query_span, key_span, value_span, prior_state, normed)
    )
    prefill_early = prefill_output(
        q_early, k_early, v_early, prior_early, local_rates, tables, live_count,
        0, first_half, None,
    )
    normed = lax.all_to_all(normed.astype(jnp.bfloat16), "heads", 0, 0, tiled=True)
    normed, prefill_early = lax.optimization_barrier((normed, prefill_early))
    normed = normed.transpose(1, 0, 2, 3, 4).reshape(
        step_total, total_prompts, heads_here, value_slice
    ).astype(jnp.float32)
    gates_steps = gate_values.reshape(step_total, total_prompts, heads_here, value_slice)
    activated = (
        (jax.nn.silu(gates_steps) * normed)
        .astype(jnp.bfloat16)
        .reshape(-1, heads_here * value_slice)
    )
    partial_out = jnp.dot(
        activated,
        w_out.reshape(heads_here * value_slice, model_width),
        preferred_element_type=jnp.float32,
    )
    partial_out = partial_out.reshape(step_total, total_prompts, model_width)
    query_span, key_span, value_span, prior_state, partial_out = lax.optimization_barrier(
        (query_span, key_span, value_span, prior_state, partial_out)
    )
    prefill_out = prefill_output(
        query_span, key_span, value_span, prior_state, local_rates, tables, live_count,
        first_half, prompts_here - first_half, prefill_early,
    )
    out_slots = head_slots * lax.axis_size("tp")
    column_block = model_width // out_slots
    pieces = partial_out.reshape(step_total, total_prompts, out_slots, column_block)
    pieces = lax.all_to_all(pieces.astype(jnp.bfloat16), ("heads", "tp"), 2, 2, tiled=True)
    decode_out = jnp.sum(pieces.astype(jnp.float32), 2).astype(jnp.bfloat16)
    return (prefill_out, decode_out)


def solution(mesh):
    placed = (
        P(("groups", "heads"), None, "tp", None),
        P(("groups", "heads"), None, "tp", None),
        P(("groups", "heads"), None, "tp", None),
        P(("groups", "heads"), "tp", None, None),
        P(),
        P("groups"),
        P(None, "groups", None),
        P(None, "tp", "heads", None),
        P(None, "tp", "heads", None),
        P(None, "tp", None, "heads", None),
        P(None, "tp", None, "heads", None),
        P("tp", None, "heads", None, None),
    )
    return jax.shard_map(
        per_device,
        mesh=mesh,
        in_specs=placed,
        out_specs=(P(("groups", "heads"), None, "tp", None), P(None, "groups", ("heads", "tp"))),
        check_vma=False,
    )
```

```python
import jax
import jax.numpy as jnp
from jax import lax
from jax.experimental import pallas as pl
from jax.experimental.pallas import tpu as pltpu
from jax.sharding import PartitionSpec as P

EPSILON = 1e-05


def rotate(values, positions):
    halfway = values.shape[-1] // 2
    frequency = 10000.0 ** (-jnp.arange(halfway).astype(jnp.float32) / halfway)
    angles = positions[..., None] * frequency
    cosine = jnp.cos(angles)
    sine_part = jnp.sin(angles)
    paired = values.reshape(values.shape[:-1] + (halfway, 2))
    even_part = paired[..., 0]
    odd_part = paired[..., 1]
    turned = jnp.stack(
        [even_part * cosine - odd_part * sine_part, odd_part * cosine + even_part * sine_part], -1
    )
    return turned.reshape(values.shape)


def norm_with(output, mean_value, mean_square):
    return (output - mean_value) * lax.rsqrt(mean_square - mean_value * mean_value + EPSILON)


def turn_lanes(raw, swap, cosine, sine_part):
    partner = jnp.dot(raw, swap, preferred_element_type=jnp.float32)
    return raw.astype(jnp.float32) * cosine + partner * sine_part


def output_kernel(
    rates_ref, live_ref, q_ref, k_ref, v_ref, prior_ref, cos_ref, sin_ref, swap_ref, out_ref
):
    swap = swap_ref[...]
    cosine = cos_ref[...]
    sine_part = sin_ref[...]
    span_len = q_ref.shape[0]
    live = live_ref[pl.program_id(0)]
    row = lax.broadcasted_iota(jnp.int32, (span_len, span_len), 0)
    column = lax.broadcasted_iota(jnp.int32, (span_len, span_len), 1)
    distance = jnp.maximum(row - column, 0).astype(jnp.float32)
    keep = (row >= column) & (column < live)
    row_index = lax.broadcasted_iota(jnp.int32, (span_len, 1), 0)
    valid = row_index < live
    q_all = q_ref[...]
    k_all = k_ref[...]
    v_all = v_ref[...]
    for head in range(q_ref.shape[1]):
        rate = rates_ref[head]
        q_raw = q_all[:, head, :]
        k_raw = k_all[:, head, :]
        both = jnp.concatenate([q_raw, k_raw], 0)
        partner = jnp.dot(both, swap, preferred_element_type=jnp.float32)
        queries = (
            q_raw.astype(jnp.float32) * cosine + partner[:span_len] * sine_part
        ).astype(jnp.bfloat16)
        keys = (
            (k_raw.astype(jnp.float32) * cosine + partner[span_len:] * sine_part)
            * (k_raw.shape[-1] ** (-0.5))
        ).astype(jnp.bfloat16)
        scores = lax.dot_general(
            queries, keys, (((1,), (1,)), ((), ())), preferred_element_type=jnp.float32
        )
        table = jnp.where(keep, jnp.exp(-rate * distance), 0.0)
        weights = (scores * table).astype(jnp.bfloat16)
        inner = jnp.dot(weights, v_all[:, head, :], preferred_element_type=jnp.float32)
        carried = jnp.dot(queries, prior_ref[head], preferred_element_type=jnp.float32)
        lead = jnp.exp(-rate * (row_index + 1).astype(jnp.float32))
        mixed = inner + lead * carried
        mean_value = jnp.mean(mixed, -1, keepdims=True)
        mean_square = jnp.mean(mixed * mixed, -1, keepdims=True)
        normed = norm_with(mixed, mean_value, mean_square)
        out_ref[:, head, :] = jnp.where(valid, normed, 0.0).astype(out_ref.dtype)


def prefill_tables(key_width, span_len, local_rates, span_start, live_count):
    halfway = key_width // 2
    offsets = jnp.arange(span_len)
    positions = (span_start[:, None] + offsets[None, :]).astype(jnp.float32)
    frequency = 10000.0 ** (-jnp.arange(halfway).astype(jnp.float32) / halfway)
    angles = positions[..., None] * frequency
    cosine = jnp.repeat(jnp.cos(angles), 2, axis=-1)
    sine_part = jnp.sin(angles)
    sine_part = jnp.stack([-sine_part, sine_part], -1).reshape(cosine.shape)
    lane = jnp.arange(key_width)
    swap = (lane[:, None] == (lane[None, :] ^ 1)).astype(jnp.bfloat16)
    valid_rows = offsets[None, :] < live_count[:, None]
    lead_decay = jnp.exp(-local_rates[:, None] * (offsets[None, :] + 1).astype(jnp.float32))
    remaining = (live_count[:, None] - 1 - offsets[None, :]).astype(jnp.float32)
    key_weight = jnp.where(
        valid_rows[:, None, :],
        jnp.exp(-local_rates[None, :, None] * jnp.maximum(remaining, 0.0)[:, None, :]),
        0.0,
    )
    kept_share = jnp.exp(-local_rates[None, :] * live_count[:, None].astype(jnp.float32))
    shape_rows = key_weight.shape
    rows = jnp.stack(
        [
            jnp.broadcast_to(lead_decay[None], shape_rows),
            jnp.broadcast_to(valid_rows[:, None, :].astype(jnp.float32), shape_rows),
            key_weight,
            jnp.broadcast_to(kept_share[:, :, None], shape_rows),
        ]
        + [jnp.zeros(shape_rows, jnp.float32)] * 4,
        -1,
    )
    return cosine, sine_part, swap, rows, valid_rows


def prefill_output(query_span, key_span, value_span, prior_state, local_rates, tables, live_count):
    prompts_here, span_len, heads_here, key_width = query_span.shape
    value_width = value_span.shape[3]
    cosine, sine_part, swap, rows, valid_rows = tables
    whole = pl.BlockSpec(memory_space=pltpu.SMEM)
    return pl.pallas_call(
        output_kernel,
        grid=(prompts_here,),
        in_specs=[
            whole,
            whole,
            pl.BlockSpec((None, span_len, heads_here, key_width), lambda b: (b, 0, 0, 0)),
            pl.BlockSpec((None, span_len, heads_here, key_width), lambda b: (b, 0, 0, 0)),
            pl.BlockSpec((None, span_len, heads_here, value_width), lambda b: (b, 0, 0, 0)),
            pl.BlockSpec((None, heads_here, key_width, value_width), lambda b: (b, 0, 0, 0)),
            pl.BlockSpec((None, span_len, key_width), lambda b: (b, 0, 0)),
            pl.BlockSpec((None, span_len, key_width), lambda b: (b, 0, 0)),
            pl.BlockSpec((key_width, key_width), lambda b: (0, 0)),
        ],
        out_specs=pl.BlockSpec(
            (None, span_len, heads_here, value_width), lambda b: (b, 0, 0, 0)
        ),
        out_shape=jax.ShapeDtypeStruct(value_span.shape, jnp.bfloat16),
    )(
        local_rates, live_count.astype(jnp.int32), query_span, key_span, value_span,
        prior_state, cosine, sine_part, swap,
    )


def per_device(
    query_span,
    key_span,
    value_span,
    prior_state,
    decay_rates,
    prompt_lengths,
    decode_inputs,
    w_query,
    w_key,
    w_value,
    w_gate,
    w_out,
):
    prompts_here, span_len, heads_here, key_width = query_span.shape
    value_width = value_span.shape[3]
    model_width = decode_inputs.shape[2]
    step_total = decode_inputs.shape[0]
    head_slots = lax.axis_size("heads")
    total_prompts = prompts_here * head_slots
    key_piece = w_query.shape[3]
    value_slice = w_value.shape[4]
    tp_index = lax.axis_index("tp")
    slot_index = lax.axis_index("heads")
    local_rates = lax.dynamic_slice_in_dim(decay_rates, tp_index * heads_here, heads_here)
    local_lengths = lax.dynamic_slice_in_dim(
        prompt_lengths, slot_index * prompts_here, prompts_here
    )
    span_start = span_len * ((local_lengths - 1) // span_len)
    live_count = local_lengths - span_start
    tables = prefill_tables(key_width, span_len, local_rates, span_start, live_count)
    offsets = jnp.arange(span_len)
    positions = (span_start[:, None] + offsets[None, :]).astype(jnp.float32)
    cosine, sine_part, swap = tables[:3]
    key_partner = jnp.einsum("bihk,kl->bihl", key_span, swap, preferred_element_type=jnp.float32)
    keys = (
        (key_span.astype(jnp.float32) * cosine[:, :, None, :] + key_partner * sine_part[:, :, None, :])
        * key_width ** (-0.5)
    ).astype(jnp.bfloat16)
    valid_rows = offsets[None, :] < live_count[:, None]
    remaining = (live_count[:, None] - 1 - offsets[None, :]).astype(jnp.float32)
    key_weight = jnp.where(
        valid_rows[:, :, None],
        jnp.exp(-local_rates[None, None, :] * jnp.maximum(remaining, 0.0)[:, :, None]),
        0.0,
    )
    weighted = (keys.astype(jnp.float32) * key_weight[..., None]).astype(jnp.bfloat16)
    update = jnp.einsum("bjhk,bjhv->bhkv", weighted, value_span, preferred_element_type=jnp.float32)
    kept_share = jnp.exp(-local_rates[None, :] * live_count[:, None].astype(jnp.float32))
    state_new = (kept_share[:, :, None, None] * prior_state.astype(jnp.float32) + update).astype(
        jnp.bfloat16
    )
    slots = head_slots
    flat_inputs = decode_inputs.reshape(step_total * total_prompts, model_width)
    query_part = jnp.dot(
        flat_inputs, w_query.reshape(model_width, key_piece), preferred_element_type=jnp.float32
    ).astype(jnp.bfloat16)
    key_part = jnp.dot(
        flat_inputs, w_key.reshape(model_width, key_piece), preferred_element_type=jnp.float32
    ).astype(jnp.bfloat16)
    value_dec = jnp.dot(
        flat_inputs,
        w_value.reshape(model_width, heads_here * value_slice),
        preferred_element_type=jnp.float32,
    ).astype(jnp.bfloat16)
    gate_values = lax.optimization_barrier(
        jnp.dot(
            flat_inputs,
            w_gate.reshape(model_width, heads_here * value_slice),
            preferred_element_type=jnp.float32,
        )
    )
    steps = jnp.arange(step_total)
    halfway = key_width // 2
    head_column = (slot_index * key_piece + jnp.arange(key_piece)) % key_width
    column_frequency = 10000.0 ** (-(head_column // 2).astype(jnp.float32) / halfway)
    dec_positions = (
        (prompt_lengths[None, :] + steps[:, None]).astype(jnp.float32).reshape(-1, 1)
    )
    dec_angles = dec_positions * column_frequency[None, :]
    dec_cosine = jnp.cos(dec_angles)
    dec_sine = jnp.where(head_column % 2 == 0, -1.0, 1.0)[None, :] * jnp.sin(dec_angles)
    lane = jnp.arange(key_piece)
    swap = (lane[:, None] == (lane[None, :] ^ 1)).astype(jnp.bfloat16)
    query_partner = jnp.dot(query_part, swap, preferred_element_type=jnp.float32)
    key_partner = jnp.dot(key_part, swap, preferred_element_type=jnp.float32)
    query_turned = (
        query_part.astype(jnp.float32) * dec_cosine + query_partner * dec_sine
    ).astype(jnp.bfloat16)
    key_turned = (
        (key_part.astype(jnp.float32) * dec_cosine + key_partner * dec_sine)
        * key_width ** (-0.5)
    ).astype(jnp.bfloat16)
    packed = jnp.concatenate([query_turned, key_turned, value_dec], -1)
    packed = packed.reshape(step_total, slots, prompts_here, -1).transpose(1, 0, 2, 3)
    arrived = lax.all_to_all(packed, "heads", 0, 0, tiled=True)
    query_rot = (
        arrived[..., :key_piece]
        .transpose(1, 2, 0, 3)
        .reshape(step_total, prompts_here, heads_here, key_width)
    )
    key_rot = (
        arrived[..., key_piece : 2 * key_piece]
        .transpose(1, 2, 0, 3)
        .reshape(step_total, prompts_here, heads_here, key_width)
    )
    value_own = (
        arrived[..., 2 * key_piece :]
        .reshape(slots, step_total, prompts_here, heads_here, value_slice)
        .transpose(1, 2, 3, 0, 4)
        .reshape(step_total, prompts_here, heads_here, value_width)
    )
    from_state = jnp.einsum(
        "tbhk,bhkv->tbhv", query_rot, state_new, preferred_element_type=jnp.float32
    )
    step_gap = (steps[:, None] - steps[None, :]).astype(jnp.float32)
    step_decay = jnp.where(
        step_gap[None] >= 0,
        jnp.exp(-local_rates[:, None, None] * jnp.maximum(step_gap, 0.0)[None]),
        0.0,
    )
    step_scores = jnp.einsum(
        "tbhk,ubhk->bhtu", query_rot, key_rot, preferred_element_type=jnp.float32
    )
    from_steps = jnp.einsum(
        "bhtu,ubhv->tbhv",
        step_scores * step_decay[None],
        value_own.astype(jnp.float32),
        precision=lax.Precision.HIGHEST,
    )
    state_decay = jnp.exp(-local_rates[None, :] * (steps[:, None] + 1).astype(jnp.float32))
    readout = state_decay[:, None, :, None] * from_state + from_steps
    read_mean = jnp.mean(readout, -1, keepdims=True)
    read_square = jnp.mean(readout * readout, -1, keepdims=True)
    normed = norm_with(readout, read_mean, read_square)
    normed = normed.reshape(step_total, prompts_here, heads_here, slots, value_slice)
    normed = normed.transpose(3, 0, 1, 2, 4)
    normed = lax.all_to_all(normed.astype(jnp.bfloat16), "heads", 0, 0, tiled=True)
    normed = normed.transpose(1, 0, 2, 3, 4).reshape(
        step_total, total_prompts, heads_here, value_slice
    ).astype(jnp.float32)
    gates_steps = gate_values.reshape(step_total, total_prompts, heads_here, value_slice)
    activated = (
        (jax.nn.silu(gates_steps) * normed)
        .astype(jnp.bfloat16)
        .reshape(-1, heads_here * value_slice)
    )
    partial_out = jnp.dot(
        activated,
        w_out.reshape(heads_here * value_slice, model_width),
        preferred_element_type=jnp.float32,
    )
    partial_out = partial_out.reshape(step_total, total_prompts, model_width)
    query_span, key_span, value_span, prior_state, partial_out = lax.optimization_barrier(
        (query_span, key_span, value_span, prior_state, partial_out)
    )
    prefill_out = prefill_output(
        query_span, key_span, value_span, prior_state, local_rates, tables, live_count
    )
    out_slots = head_slots * lax.axis_size("tp")
    column_block = model_width // out_slots
    pieces = partial_out.reshape(step_total, total_prompts, out_slots, column_block)
    pieces = lax.all_to_all(pieces.astype(jnp.bfloat16), ("heads", "tp"), 2, 2, tiled=True)
    decode_out = jnp.sum(pieces.astype(jnp.float32), 2).astype(jnp.bfloat16)
    return (prefill_out, decode_out)


def solution(mesh):
    placed = (
        P(("groups", "heads"), None, "tp", None),
        P(("groups", "heads"), None, "tp", None),
        P(("groups", "heads"), None, "tp", None),
        P(("groups", "heads"), "tp", None, None),
        P(),
        P("groups"),
        P(None, "groups", None),
        P(None, "tp", "heads", None),
        P(None, "tp", "heads", None),
        P(None, "tp", None, "heads", None),
        P(None, "tp", None, "heads", None),
        P("tp", None, "heads", None, None),
    )
    return jax.shard_map(
        per_device,
        mesh=mesh,
        in_specs=placed,
        out_specs=(P(("groups", "heads"), None, "tp", None), P(None, "groups", ("heads", "tp"))),
        check_vma=False,
    )
```

```python
import jax
import jax.numpy as jnp
from jax import lax
from jax.experimental import pallas as pl
from jax.experimental.pallas import tpu as pltpu
from jax.sharding import PartitionSpec as P

EPSILON = 1e-05


def rotate(values, positions):
    halfway = values.shape[-1] // 2
    frequency = 10000.0 ** (-jnp.arange(halfway).astype(jnp.float32) / halfway)
    angles = positions[..., None] * frequency
    cosine = jnp.cos(angles)
    sine_part = jnp.sin(angles)
    paired = values.reshape(values.shape[:-1] + (halfway, 2))
    even_part = paired[..., 0]
    odd_part = paired[..., 1]
    turned = jnp.stack(
        [even_part * cosine - odd_part * sine_part, odd_part * cosine + even_part * sine_part], -1
    )
    return turned.reshape(values.shape)


def norm_with(output, mean_value, mean_square):
    return (output - mean_value) * lax.rsqrt(mean_square - mean_value * mean_value + EPSILON)


def turn_lanes(raw, swap, cosine, sine_part):
    partner = jnp.dot(raw, swap, preferred_element_type=jnp.float32)
    return raw.astype(jnp.float32) * cosine + partner * sine_part


def output_kernel(
    rates_ref, live_ref, q_ref, k_ref, v_ref, prior_ref, cos_ref, sin_ref, swap_ref, out_ref
):
    swap = swap_ref[...]
    cosine = cos_ref[...]
    sine_part = sin_ref[...]
    span_len = q_ref.shape[0]
    live = live_ref[pl.program_id(0)]
    row = lax.broadcasted_iota(jnp.int32, (span_len, span_len), 0)
    column = lax.broadcasted_iota(jnp.int32, (span_len, span_len), 1)
    distance = jnp.maximum(row - column, 0).astype(jnp.float32)
    keep = (row >= column) & (column < live)
    row_index = lax.broadcasted_iota(jnp.int32, (span_len, 1), 0)
    valid = row_index < live
    q_all = q_ref[...]
    k_all = k_ref[...]
    v_all = v_ref[...]
    for head in range(q_ref.shape[1]):
        rate = rates_ref[head]
        q_raw = q_all[:, head, :]
        k_raw = k_all[:, head, :]
        queries = turn_lanes(q_raw, swap, cosine, sine_part).astype(jnp.bfloat16)
        keys = (turn_lanes(k_raw, swap, cosine, sine_part) * (k_raw.shape[-1] ** (-0.5))).astype(
            jnp.bfloat16
        )
        scores = lax.dot_general(
            queries, keys, (((1,), (1,)), ((), ())), preferred_element_type=jnp.float32
        )
        table = jnp.where(keep, jnp.exp(-rate * distance), 0.0)
        weights = (scores * table).astype(jnp.bfloat16)
        inner = jnp.dot(weights, v_all[:, head, :], preferred_element_type=jnp.float32)
        carried = jnp.dot(queries, prior_ref[head], preferred_element_type=jnp.float32)
        lead = jnp.exp(-rate * (row_index + 1).astype(jnp.float32))
        mixed = inner + lead * carried
        mean_value = jnp.mean(mixed, -1, keepdims=True)
        mean_square = jnp.mean(mixed * mixed, -1, keepdims=True)
        normed = norm_with(mixed, mean_value, mean_square)
        out_ref[:, head, :] = jnp.where(valid, normed, 0.0).astype(out_ref.dtype)


def prefill_tables(key_width, span_len, local_rates, span_start, live_count):
    halfway = key_width // 2
    offsets = jnp.arange(span_len)
    positions = (span_start[:, None] + offsets[None, :]).astype(jnp.float32)
    frequency = 10000.0 ** (-jnp.arange(halfway).astype(jnp.float32) / halfway)
    angles = positions[..., None] * frequency
    cosine = jnp.repeat(jnp.cos(angles), 2, axis=-1)
    sine_part = jnp.sin(angles)
    sine_part = jnp.stack([-sine_part, sine_part], -1).reshape(cosine.shape)
    lane = jnp.arange(key_width)
    swap = (lane[:, None] == (lane[None, :] ^ 1)).astype(jnp.bfloat16)
    valid_rows = offsets[None, :] < live_count[:, None]
    lead_decay = jnp.exp(-local_rates[:, None] * (offsets[None, :] + 1).astype(jnp.float32))
    remaining = (live_count[:, None] - 1 - offsets[None, :]).astype(jnp.float32)
    key_weight = jnp.where(
        valid_rows[:, None, :],
        jnp.exp(-local_rates[None, :, None] * jnp.maximum(remaining, 0.0)[:, None, :]),
        0.0,
    )
    kept_share = jnp.exp(-local_rates[None, :] * live_count[:, None].astype(jnp.float32))
    shape_rows = key_weight.shape
    rows = jnp.stack(
        [
            jnp.broadcast_to(lead_decay[None], shape_rows),
            jnp.broadcast_to(valid_rows[:, None, :].astype(jnp.float32), shape_rows),
            key_weight,
            jnp.broadcast_to(kept_share[:, :, None], shape_rows),
        ]
        + [jnp.zeros(shape_rows, jnp.float32)] * 4,
        -1,
    )
    return cosine, sine_part, swap, rows, valid_rows


def prefill_output(query_span, key_span, value_span, prior_state, local_rates, tables, live_count):
    prompts_here, span_len, heads_here, key_width = query_span.shape
    value_width = value_span.shape[3]
    cosine, sine_part, swap, rows, valid_rows = tables
    whole = pl.BlockSpec(memory_space=pltpu.SMEM)
    return pl.pallas_call(
        output_kernel,
        grid=(prompts_here,),
        in_specs=[
            whole,
            whole,
            pl.BlockSpec((None, span_len, heads_here, key_width), lambda b: (b, 0, 0, 0)),
            pl.BlockSpec((None, span_len, heads_here, key_width), lambda b: (b, 0, 0, 0)),
            pl.BlockSpec((None, span_len, heads_here, value_width), lambda b: (b, 0, 0, 0)),
            pl.BlockSpec((None, heads_here, key_width, value_width), lambda b: (b, 0, 0, 0)),
            pl.BlockSpec((None, span_len, key_width), lambda b: (b, 0, 0)),
            pl.BlockSpec((None, span_len, key_width), lambda b: (b, 0, 0)),
            pl.BlockSpec((key_width, key_width), lambda b: (0, 0)),
        ],
        out_specs=pl.BlockSpec(
            (None, span_len, heads_here, value_width), lambda b: (b, 0, 0, 0)
        ),
        out_shape=jax.ShapeDtypeStruct(value_span.shape, jnp.bfloat16),
    )(
        local_rates, live_count.astype(jnp.int32), query_span, key_span, value_span,
        prior_state, cosine, sine_part, swap,
    )


def per_device(
    query_span,
    key_span,
    value_span,
    prior_state,
    decay_rates,
    prompt_lengths,
    decode_inputs,
    w_query,
    w_key,
    w_value,
    w_gate,
    w_out,
):
    prompts_here, span_len, heads_here, key_width = query_span.shape
    value_width = value_span.shape[3]
    model_width = decode_inputs.shape[2]
    step_total = decode_inputs.shape[0]
    head_slots = lax.axis_size("heads")
    total_prompts = prompts_here * head_slots
    key_piece = w_query.shape[3]
    value_slice = w_value.shape[4]
    tp_index = lax.axis_index("tp")
    slot_index = lax.axis_index("heads")
    local_rates = lax.dynamic_slice_in_dim(decay_rates, tp_index * heads_here, heads_here)
    local_lengths = lax.dynamic_slice_in_dim(
        prompt_lengths, slot_index * prompts_here, prompts_here
    )
    span_start = span_len * ((local_lengths - 1) // span_len)
    live_count = local_lengths - span_start
    tables = prefill_tables(key_width, span_len, local_rates, span_start, live_count)
    offsets = jnp.arange(span_len)
    positions = (span_start[:, None] + offsets[None, :]).astype(jnp.float32)
    cosine, sine_part, swap = tables[:3]
    key_partner = jnp.einsum("bihk,kl->bihl", key_span, swap, preferred_element_type=jnp.float32)
    keys = (
        (key_span.astype(jnp.float32) * cosine[:, :, None, :] + key_partner * sine_part[:, :, None, :])
        * key_width ** (-0.5)
    ).astype(jnp.bfloat16)
    valid_rows = offsets[None, :] < live_count[:, None]
    remaining = (live_count[:, None] - 1 - offsets[None, :]).astype(jnp.float32)
    key_weight = jnp.where(
        valid_rows[:, :, None],
        jnp.exp(-local_rates[None, None, :] * jnp.maximum(remaining, 0.0)[:, :, None]),
        0.0,
    )
    weighted = (keys.astype(jnp.float32) * key_weight[..., None]).astype(jnp.bfloat16)
    update = jnp.einsum("bjhk,bjhv->bhkv", weighted, value_span, preferred_element_type=jnp.float32)
    kept_share = jnp.exp(-local_rates[None, :] * live_count[:, None].astype(jnp.float32))
    state_new = (kept_share[:, :, None, None] * prior_state.astype(jnp.float32) + update).astype(
        jnp.bfloat16
    )
    slots = head_slots
    flat_inputs = decode_inputs.reshape(step_total * total_prompts, model_width)
    query_part = lax.dot_general(
        w_query.reshape(model_width, key_piece), flat_inputs, (((0,), (1,)), ((), ())),
        preferred_element_type=jnp.float32,
    ).T.astype(jnp.bfloat16)
    key_part = lax.dot_general(
        w_key.reshape(model_width, key_piece), flat_inputs, (((0,), (1,)), ((), ())),
        preferred_element_type=jnp.float32,
    ).T.astype(jnp.bfloat16)
    value_dec = jnp.dot(
        flat_inputs,
        w_value.reshape(model_width, heads_here * value_slice),
        preferred_element_type=jnp.float32,
    ).astype(jnp.bfloat16)
    gate_values = lax.optimization_barrier(
        jnp.dot(
            flat_inputs,
            w_gate.reshape(model_width, heads_here * value_slice),
            preferred_element_type=jnp.float32,
        )
    )
    steps = jnp.arange(step_total)
    halfway = key_width // 2
    head_column = (slot_index * key_piece + jnp.arange(key_piece)) % key_width
    column_frequency = 10000.0 ** (-(head_column // 2).astype(jnp.float32) / halfway)
    dec_positions = (
        (prompt_lengths[None, :] + steps[:, None]).astype(jnp.float32).reshape(-1, 1)
    )
    dec_angles = dec_positions * column_frequency[None, :]
    dec_cosine = jnp.cos(dec_angles)
    dec_sine = jnp.where(head_column % 2 == 0, -1.0, 1.0)[None, :] * jnp.sin(dec_angles)
    lane = jnp.arange(key_piece)
    swap = (lane[:, None] == (lane[None, :] ^ 1)).astype(jnp.bfloat16)
    query_partner = jnp.dot(query_part, swap, preferred_element_type=jnp.float32)
    key_partner = jnp.dot(key_part, swap, preferred_element_type=jnp.float32)
    query_turned = (
        query_part.astype(jnp.float32) * dec_cosine + query_partner * dec_sine
    ).astype(jnp.bfloat16)
    key_turned = (
        (key_part.astype(jnp.float32) * dec_cosine + key_partner * dec_sine)
        * key_width ** (-0.5)
    ).astype(jnp.bfloat16)
    packed = jnp.concatenate([query_turned, key_turned, value_dec], -1)
    packed = packed.reshape(step_total, slots, prompts_here, -1).transpose(1, 0, 2, 3)
    arrived = lax.all_to_all(packed, "heads", 0, 0, tiled=True)
    query_rot = (
        arrived[..., :key_piece]
        .transpose(1, 2, 0, 3)
        .reshape(step_total, prompts_here, heads_here, key_width)
    )
    key_rot = (
        arrived[..., key_piece : 2 * key_piece]
        .transpose(1, 2, 0, 3)
        .reshape(step_total, prompts_here, heads_here, key_width)
    )
    value_own = (
        arrived[..., 2 * key_piece :]
        .reshape(slots, step_total, prompts_here, heads_here, value_slice)
        .transpose(1, 2, 3, 0, 4)
        .reshape(step_total, prompts_here, heads_here, value_width)
    )
    from_state = jnp.einsum(
        "tbhk,bhkv->tbhv", query_rot, state_new, preferred_element_type=jnp.float32
    )
    step_gap = (steps[:, None] - steps[None, :]).astype(jnp.float32)
    step_decay = jnp.where(
        step_gap[None] >= 0,
        jnp.exp(-local_rates[:, None, None] * jnp.maximum(step_gap, 0.0)[None]),
        0.0,
    )
    step_scores = jnp.einsum(
        "tbhk,ubhk->bhtu", query_rot, key_rot, preferred_element_type=jnp.float32
    )
    from_steps = jnp.einsum(
        "bhtu,ubhv->tbhv",
        step_scores * step_decay[None],
        value_own.astype(jnp.float32),
        precision=lax.Precision.HIGHEST,
    )
    state_decay = jnp.exp(-local_rates[None, :] * (steps[:, None] + 1).astype(jnp.float32))
    readout = state_decay[:, None, :, None] * from_state + from_steps
    read_mean = jnp.mean(readout, -1, keepdims=True)
    read_square = jnp.mean(readout * readout, -1, keepdims=True)
    normed = norm_with(readout, read_mean, read_square)
    normed = normed.reshape(step_total, prompts_here, heads_here, slots, value_slice)
    normed = normed.transpose(3, 0, 1, 2, 4)
    normed = lax.all_to_all(normed.astype(jnp.bfloat16), "heads", 0, 0, tiled=True)
    normed = normed.transpose(1, 0, 2, 3, 4).reshape(
        step_total, total_prompts, heads_here, value_slice
    ).astype(jnp.float32)
    gates_steps = gate_values.reshape(step_total, total_prompts, heads_here, value_slice)
    activated = (
        (jax.nn.silu(gates_steps) * normed)
        .astype(jnp.bfloat16)
        .reshape(-1, heads_here * value_slice)
    )
    partial_out = jnp.dot(
        activated,
        w_out.reshape(heads_here * value_slice, model_width),
        preferred_element_type=jnp.float32,
    )
    partial_out = partial_out.reshape(step_total, total_prompts, model_width)
    query_span, key_span, value_span, prior_state, partial_out = lax.optimization_barrier(
        (query_span, key_span, value_span, prior_state, partial_out)
    )
    prefill_out = prefill_output(
        query_span, key_span, value_span, prior_state, local_rates, tables, live_count
    )
    out_slots = head_slots * lax.axis_size("tp")
    column_block = model_width // out_slots
    pieces = partial_out.reshape(step_total, total_prompts, out_slots, column_block)
    pieces = lax.all_to_all(pieces.astype(jnp.bfloat16), ("heads", "tp"), 2, 2, tiled=True)
    decode_out = jnp.sum(pieces.astype(jnp.float32), 2).astype(jnp.bfloat16)
    return (prefill_out, decode_out)


def solution(mesh):
    placed = (
        P(("groups", "heads"), None, "tp", None),
        P(("groups", "heads"), None, "tp", None),
        P(("groups", "heads"), None, "tp", None),
        P(("groups", "heads"), "tp", None, None),
        P(),
        P("groups"),
        P(None, "groups", None),
        P(None, "tp", "heads", None),
        P(None, "tp", "heads", None),
        P(None, "tp", None, "heads", None),
        P(None, "tp", None, "heads", None),
        P("tp", None, "heads", None, None),
    )
    return jax.shard_map(
        per_device,
        mesh=mesh,
        in_specs=placed,
        out_specs=(P(("groups", "heads"), None, "tp", None), P(None, "groups", ("heads", "tp"))),
        check_vma=False,
    )
```

```python
import jax
import numpy as np
import jax.numpy as jnp
from jax import lax
from jax.experimental import pallas as pl
from jax.experimental.pallas import tpu as pltpu
from jax.sharding import PartitionSpec as P

EPSILON = 1e-05


def rotate(values, positions):
    halfway = values.shape[-1] // 2
    frequency = 10000.0 ** (-jnp.arange(halfway).astype(jnp.float32) / halfway)
    angles = positions[..., None] * frequency
    cosine = jnp.cos(angles)
    sine_part = jnp.sin(angles)
    paired = values.reshape(values.shape[:-1] + (halfway, 2))
    even_part = paired[..., 0]
    odd_part = paired[..., 1]
    turned = jnp.stack(
        [even_part * cosine - odd_part * sine_part, odd_part * cosine + even_part * sine_part], -1
    )
    return turned.reshape(values.shape)


def norm_with(output, mean_value, mean_square):
    return (output - mean_value) * lax.rsqrt(mean_square - mean_value * mean_value + EPSILON)


def turn_lanes(raw, swap, cosine, sine_part):
    partner = jnp.dot(raw, swap, preferred_element_type=jnp.float32)
    return raw.astype(jnp.float32) * cosine + partner * sine_part


def output_kernel(
    rates_ref, live_ref, q_ref, k_ref, v_ref, prior_ref, cos_ref, sin_ref, swap_ref, out_ref
):
    swap = swap_ref[...]
    cosine = cos_ref[...]
    sine_part = sin_ref[...]
    span_len = q_ref.shape[0]
    live = live_ref[pl.program_id(0)]
    row = lax.broadcasted_iota(jnp.int32, (span_len, span_len), 0)
    column = lax.broadcasted_iota(jnp.int32, (span_len, span_len), 1)
    distance = jnp.maximum(row - column, 0).astype(jnp.float32)
    keep = (row >= column) & (column < live)
    row_index = lax.broadcasted_iota(jnp.int32, (span_len, 1), 0)
    valid = row_index < live
    q_all = q_ref[...]
    k_all = k_ref[...]
    v_all = v_ref[...]
    for head in range(q_ref.shape[1]):
        rate = rates_ref[head]
        q_raw = q_all[:, head, :]
        k_raw = k_all[:, head, :]
        queries = turn_lanes(q_raw, swap, cosine, sine_part).astype(jnp.bfloat16)
        keys = (turn_lanes(k_raw, swap, cosine, sine_part) * (k_raw.shape[-1] ** (-0.5))).astype(
            jnp.bfloat16
        )
        scores = lax.dot_general(
            queries, keys, (((1,), (1,)), ((), ())), preferred_element_type=jnp.float32
        )
        table = jnp.where(keep, jnp.exp(-rate * distance), 0.0)
        weights = (scores * table).astype(jnp.bfloat16)
        inner = jnp.dot(weights, v_all[:, head, :], preferred_element_type=jnp.float32)
        carried = jnp.dot(queries, prior_ref[head], preferred_element_type=jnp.float32)
        lead = jnp.exp(-rate * (row_index + 1).astype(jnp.float32))
        mixed = inner + lead * carried
        mean_value = jnp.mean(mixed, -1, keepdims=True)
        mean_square = jnp.mean(mixed * mixed, -1, keepdims=True)
        normed = norm_with(mixed, mean_value, mean_square)
        out_ref[:, head, :] = jnp.where(valid, normed, 0.0).astype(out_ref.dtype)


def prefill_tables(key_width, span_len, local_rates, span_start, live_count):
    halfway = key_width // 2
    offsets = jnp.arange(span_len)
    positions = (span_start[:, None] + offsets[None, :]).astype(jnp.float32)
    frequency = 10000.0 ** (-jnp.arange(halfway).astype(jnp.float32) / halfway)
    angles = positions[..., None] * frequency
    cosine = jnp.repeat(jnp.cos(angles), 2, axis=-1)
    sine_part = jnp.sin(angles)
    sine_part = jnp.stack([-sine_part, sine_part], -1).reshape(cosine.shape)
    pairs = np.arange(key_width)
    swap = jnp.asarray((pairs[:, None] == (pairs[None, :] ^ 1)).astype(np.float32), jnp.bfloat16)
    valid_rows = offsets[None, :] < live_count[:, None]
    lead_decay = jnp.exp(-local_rates[:, None] * (offsets[None, :] + 1).astype(jnp.float32))
    remaining = (live_count[:, None] - 1 - offsets[None, :]).astype(jnp.float32)
    key_weight = jnp.where(
        valid_rows[:, None, :],
        jnp.exp(-local_rates[None, :, None] * jnp.maximum(remaining, 0.0)[:, None, :]),
        0.0,
    )
    kept_share = jnp.exp(-local_rates[None, :] * live_count[:, None].astype(jnp.float32))
    shape_rows = key_weight.shape
    rows = jnp.stack(
        [
            jnp.broadcast_to(lead_decay[None], shape_rows),
            jnp.broadcast_to(valid_rows[:, None, :].astype(jnp.float32), shape_rows),
            key_weight,
            jnp.broadcast_to(kept_share[:, :, None], shape_rows),
        ]
        + [jnp.zeros(shape_rows, jnp.float32)] * 4,
        -1,
    )
    return cosine, sine_part, swap, rows, valid_rows


def prefill_output(query_span, key_span, value_span, prior_state, local_rates, tables, live_count):
    prompts_here, span_len, heads_here, key_width = query_span.shape
    value_width = value_span.shape[3]
    cosine, sine_part, swap, rows, valid_rows = tables
    whole = pl.BlockSpec(memory_space=pltpu.SMEM)
    return pl.pallas_call(
        output_kernel,
        grid=(prompts_here,),
        in_specs=[
            whole,
            whole,
            pl.BlockSpec((None, span_len, heads_here, key_width), lambda b: (b, 0, 0, 0)),
            pl.BlockSpec((None, span_len, heads_here, key_width), lambda b: (b, 0, 0, 0)),
            pl.BlockSpec((None, span_len, heads_here, value_width), lambda b: (b, 0, 0, 0)),
            pl.BlockSpec((None, heads_here, key_width, value_width), lambda b: (b, 0, 0, 0)),
            pl.BlockSpec((None, span_len, key_width), lambda b: (b, 0, 0)),
            pl.BlockSpec((None, span_len, key_width), lambda b: (b, 0, 0)),
            pl.BlockSpec((key_width, key_width), lambda b: (0, 0)),
        ],
        out_specs=pl.BlockSpec(
            (None, span_len, heads_here, value_width), lambda b: (b, 0, 0, 0)
        ),
        out_shape=jax.ShapeDtypeStruct(value_span.shape, jnp.bfloat16),
    )(
        local_rates, live_count.astype(jnp.int32), query_span, key_span, value_span,
        prior_state, cosine, sine_part, swap,
    )


def per_device(
    query_span,
    key_span,
    value_span,
    prior_state,
    decay_rates,
    prompt_lengths,
    decode_inputs,
    w_query,
    w_key,
    w_value,
    w_gate,
    w_out,
):
    prompts_here, span_len, heads_here, key_width = query_span.shape
    value_width = value_span.shape[3]
    model_width = decode_inputs.shape[2]
    step_total = decode_inputs.shape[0]
    head_slots = lax.axis_size("heads")
    total_prompts = prompts_here * head_slots
    key_piece = w_query.shape[3]
    value_slice = w_value.shape[4]
    tp_index = lax.axis_index("tp")
    slot_index = lax.axis_index("heads")
    local_rates = lax.dynamic_slice_in_dim(decay_rates, tp_index * heads_here, heads_here)
    local_lengths = lax.dynamic_slice_in_dim(
        prompt_lengths, slot_index * prompts_here, prompts_here
    )
    span_start = span_len * ((local_lengths - 1) // span_len)
    live_count = local_lengths - span_start
    tables = prefill_tables(key_width, span_len, local_rates, span_start, live_count)
    offsets = jnp.arange(span_len)
    positions = (span_start[:, None] + offsets[None, :]).astype(jnp.float32)
    cosine, sine_part, swap = tables[:3]
    key_partner = jnp.einsum("bihk,kl->bihl", key_span, swap, preferred_element_type=jnp.float32)
    keys = (
        (key_span.astype(jnp.float32) * cosine[:, :, None, :] + key_partner * sine_part[:, :, None, :])
        * key_width ** (-0.5)
    ).astype(jnp.bfloat16)
    valid_rows = offsets[None, :] < live_count[:, None]
    remaining = (live_count[:, None] - 1 - offsets[None, :]).astype(jnp.float32)
    key_weight = jnp.where(
        valid_rows[:, :, None],
        jnp.exp(-local_rates[None, None, :] * jnp.maximum(remaining, 0.0)[:, :, None]),
        0.0,
    )
    weighted = (keys.astype(jnp.float32) * key_weight[..., None]).astype(jnp.bfloat16)
    update = jnp.einsum("bjhk,bjhv->bhkv", weighted, value_span, preferred_element_type=jnp.float32)
    kept_share = jnp.exp(-local_rates[None, :] * live_count[:, None].astype(jnp.float32))
    state_new = (kept_share[:, :, None, None] * prior_state.astype(jnp.float32) + update).astype(
        jnp.bfloat16
    )
    slots = head_slots
    flat_inputs = decode_inputs.reshape(step_total * total_prompts, model_width)
    query_part = jnp.dot(
        flat_inputs, w_query.reshape(model_width, key_piece), preferred_element_type=jnp.float32
    ).astype(jnp.bfloat16)
    key_part = jnp.dot(
        flat_inputs, w_key.reshape(model_width, key_piece), preferred_element_type=jnp.float32
    ).astype(jnp.bfloat16)
    value_dec = jnp.dot(
        flat_inputs,
        w_value.reshape(model_width, heads_here * value_slice),
        preferred_element_type=jnp.float32,
    ).astype(jnp.bfloat16)
    gate_values = lax.optimization_barrier(
        jnp.dot(
            flat_inputs,
            w_gate.reshape(model_width, heads_here * value_slice),
            preferred_element_type=jnp.float32,
        )
    )
    steps = jnp.arange(step_total)
    halfway = key_width // 2
    head_column = (slot_index * key_piece + jnp.arange(key_piece)) % key_width
    column_frequency = 10000.0 ** (-(head_column // 2).astype(jnp.float32) / halfway)
    dec_positions = (
        (prompt_lengths[None, :] + steps[:, None]).astype(jnp.float32).reshape(-1, 1)
    )
    dec_angles = dec_positions * column_frequency[None, :]
    dec_cosine = jnp.cos(dec_angles)
    dec_sine = jnp.where(head_column % 2 == 0, -1.0, 1.0)[None, :] * jnp.sin(dec_angles)
    lane = jnp.arange(key_piece)
    swap = (lane[:, None] == (lane[None, :] ^ 1)).astype(jnp.bfloat16)
    query_partner = jnp.dot(query_part, swap, preferred_element_type=jnp.float32)
    key_partner = jnp.dot(key_part, swap, preferred_element_type=jnp.float32)
    query_turned = (
        query_part.astype(jnp.float32) * dec_cosine + query_partner * dec_sine
    ).astype(jnp.bfloat16)
    key_turned = (
        (key_part.astype(jnp.float32) * dec_cosine + key_partner * dec_sine)
        * key_width ** (-0.5)
    ).astype(jnp.bfloat16)
    packed = jnp.concatenate([query_turned, key_turned, value_dec], -1)
    packed = packed.reshape(step_total, slots, prompts_here, -1).transpose(1, 0, 2, 3)
    arrived = lax.all_to_all(packed, "heads", 0, 0, tiled=True)
    query_rot = (
        arrived[..., :key_piece]
        .transpose(1, 2, 0, 3)
        .reshape(step_total, prompts_here, heads_here, key_width)
    )
    key_rot = (
        arrived[..., key_piece : 2 * key_piece]
        .transpose(1, 2, 0, 3)
        .reshape(step_total, prompts_here, heads_here, key_width)
    )
    value_own = (
        arrived[..., 2 * key_piece :]
        .reshape(slots, step_total, prompts_here, heads_here, value_slice)
        .transpose(1, 2, 3, 0, 4)
        .reshape(step_total, prompts_here, heads_here, value_width)
    )
    from_state = jnp.einsum(
        "tbhk,bhkv->tbhv", query_rot, state_new, preferred_element_type=jnp.float32
    )
    step_gap = (steps[:, None] - steps[None, :]).astype(jnp.float32)
    step_decay = jnp.where(
        step_gap[None] >= 0,
        jnp.exp(-local_rates[:, None, None] * jnp.maximum(step_gap, 0.0)[None]),
        0.0,
    )
    step_scores = jnp.einsum(
        "tbhk,ubhk->bhtu", query_rot, key_rot, preferred_element_type=jnp.float32
    )
    from_steps = jnp.einsum(
        "bhtu,ubhv->tbhv",
        step_scores * step_decay[None],
        value_own.astype(jnp.float32),
        precision=lax.Precision.HIGHEST,
    )
    state_decay = jnp.exp(-local_rates[None, :] * (steps[:, None] + 1).astype(jnp.float32))
    readout = state_decay[:, None, :, None] * from_state + from_steps
    read_mean = jnp.mean(readout, -1, keepdims=True)
    read_square = jnp.mean(readout * readout, -1, keepdims=True)
    normed = norm_with(readout, read_mean, read_square)
    normed = normed.reshape(step_total, prompts_here, heads_here, slots, value_slice)
    normed = normed.transpose(3, 0, 1, 2, 4)
    normed = lax.all_to_all(normed.astype(jnp.bfloat16), "heads", 0, 0, tiled=True)
    normed = normed.transpose(1, 0, 2, 3, 4).reshape(
        step_total, total_prompts, heads_here, value_slice
    ).astype(jnp.float32)
    gates_steps = gate_values.reshape(step_total, total_prompts, heads_here, value_slice)
    activated = (
        (jax.nn.silu(gates_steps) * normed)
        .astype(jnp.bfloat16)
        .reshape(-1, heads_here * value_slice)
    )
    partial_out = jnp.dot(
        activated,
        w_out.reshape(heads_here * value_slice, model_width),
        preferred_element_type=jnp.float32,
    )
    partial_out = partial_out.reshape(step_total, total_prompts, model_width)
    query_span, key_span, value_span, prior_state, partial_out = lax.optimization_barrier(
        (query_span, key_span, value_span, prior_state, partial_out)
    )
    prefill_out = prefill_output(
        query_span, key_span, value_span, prior_state, local_rates, tables, live_count
    )
    out_slots = head_slots * lax.axis_size("tp")
    column_block = model_width // out_slots
    pieces = partial_out.reshape(step_total, total_prompts, out_slots, column_block)
    pieces = lax.all_to_all(pieces.astype(jnp.bfloat16), ("heads", "tp"), 2, 2, tiled=True)
    decode_out = jnp.sum(pieces.astype(jnp.float32), 2).astype(jnp.bfloat16)
    return (prefill_out, decode_out)


def solution(mesh):
    placed = (
        P(("groups", "heads"), None, "tp", None),
        P(("groups", "heads"), None, "tp", None),
        P(("groups", "heads"), None, "tp", None),
        P(("groups", "heads"), "tp", None, None),
        P(),
        P("groups"),
        P(None, "groups", None),
        P(None, "tp", "heads", None),
        P(None, "tp", "heads", None),
        P(None, "tp", None, "heads", None),
        P(None, "tp", None, "heads", None),
        P("tp", None, "heads", None, None),
    )
    return jax.shard_map(
        per_device,
        mesh=mesh,
        in_specs=placed,
        out_specs=(P(("groups", "heads"), None, "tp", None), P(None, "groups", ("heads", "tp"))),
        check_vma=False,
    )
```

```python
import jax
import numpy as np
import jax.numpy as jnp
from jax import lax
from jax.experimental import pallas as pl
from jax.experimental.pallas import tpu as pltpu
from jax.sharding import PartitionSpec as P

EPSILON = 1e-05


def rotate(values, positions):
    halfway = values.shape[-1] // 2
    frequency = 10000.0 ** (-jnp.arange(halfway).astype(jnp.float32) / halfway)
    angles = positions[..., None] * frequency
    cosine = jnp.cos(angles)
    sine_part = jnp.sin(angles)
    paired = values.reshape(values.shape[:-1] + (halfway, 2))
    even_part = paired[..., 0]
    odd_part = paired[..., 1]
    turned = jnp.stack(
        [even_part * cosine - odd_part * sine_part, odd_part * cosine + even_part * sine_part], -1
    )
    return turned.reshape(values.shape)


def norm_with(output, mean_value, mean_square):
    return (output - mean_value) * lax.rsqrt(mean_square - mean_value * mean_value + EPSILON)


def turn_lanes(raw, swap, cosine, sine_part):
    partner = jnp.dot(raw, swap, preferred_element_type=jnp.float32)
    return raw.astype(jnp.float32) * cosine + partner * sine_part


def output_kernel(
    rates_ref, live_ref, q_ref, k_ref, v_ref, prior_ref, cos_ref, sin_ref, swap_ref, out_ref
):
    swap = swap_ref[...]
    cosine = cos_ref[...]
    sine_part = sin_ref[...]
    span_len = q_ref.shape[0]
    live = live_ref[pl.program_id(0)]
    row = lax.broadcasted_iota(jnp.int32, (span_len, span_len), 0)
    column = lax.broadcasted_iota(jnp.int32, (span_len, span_len), 1)
    distance = jnp.maximum(row - column, 0).astype(jnp.float32)
    keep = (row >= column) & (column < live)
    row_index = lax.broadcasted_iota(jnp.int32, (span_len, 1), 0)
    valid = row_index < live
    q_all = q_ref[...]
    k_all = k_ref[...]
    v_all = v_ref[...]
    for head in range(q_ref.shape[1]):
        rate = rates_ref[head]
        q_raw = q_all[:, head, :]
        k_raw = k_all[:, head, :]
        queries = turn_lanes(q_raw, swap, cosine, sine_part).astype(jnp.bfloat16)
        keys = (turn_lanes(k_raw, swap, cosine, sine_part) * (k_raw.shape[-1] ** (-0.5))).astype(
            jnp.bfloat16
        )
        scores = lax.dot_general(
            queries, keys, (((1,), (1,)), ((), ())), preferred_element_type=jnp.float32
        )
        table = jnp.where(keep, jnp.exp(-rate * distance), 0.0)
        weights = (scores * table).astype(jnp.bfloat16)
        inner = jnp.dot(weights, v_all[:, head, :], preferred_element_type=jnp.float32)
        carried = jnp.dot(queries, prior_ref[head], preferred_element_type=jnp.float32)
        lead = jnp.exp(-rate * (row_index + 1).astype(jnp.float32))
        mixed = inner + lead * carried
        mean_value = jnp.mean(mixed, -1, keepdims=True)
        mean_square = jnp.mean(mixed * mixed, -1, keepdims=True)
        normed = norm_with(mixed, mean_value, mean_square)
        out_ref[:, head, :] = jnp.where(valid, normed, 0.0).astype(out_ref.dtype)


def prefill_tables(key_width, span_len, local_rates, span_start, live_count):
    halfway = key_width // 2
    offsets = jnp.arange(span_len)
    positions = (span_start[:, None] + offsets[None, :]).astype(jnp.float32)
    lane = np.arange(key_width)
    frequency = 10000.0 ** (-jnp.asarray(lane // 2).astype(jnp.float32) / halfway)
    angles = positions[..., None] * frequency
    cosine = jnp.cos(angles)
    sine_part = jnp.asarray(np.where(lane % 2 == 0, -1.0, 1.0), jnp.float32) * jnp.sin(angles)
    pairs = np.arange(key_width)
    swap = jnp.asarray((pairs[:, None] == (pairs[None, :] ^ 1)).astype(np.float32), jnp.bfloat16)
    valid_rows = offsets[None, :] < live_count[:, None]
    lead_decay = jnp.exp(-local_rates[:, None] * (offsets[None, :] + 1).astype(jnp.float32))
    remaining = (live_count[:, None] - 1 - offsets[None, :]).astype(jnp.float32)
    key_weight = jnp.where(
        valid_rows[:, None, :],
        jnp.exp(-local_rates[None, :, None] * jnp.maximum(remaining, 0.0)[:, None, :]),
        0.0,
    )
    kept_share = jnp.exp(-local_rates[None, :] * live_count[:, None].astype(jnp.float32))
    shape_rows = key_weight.shape
    rows = jnp.stack(
        [
            jnp.broadcast_to(lead_decay[None], shape_rows),
            jnp.broadcast_to(valid_rows[:, None, :].astype(jnp.float32), shape_rows),
            key_weight,
            jnp.broadcast_to(kept_share[:, :, None], shape_rows),
        ]
        + [jnp.zeros(shape_rows, jnp.float32)] * 4,
        -1,
    )
    return cosine, sine_part, swap, rows, valid_rows


def prefill_output(query_span, key_span, value_span, prior_state, local_rates, tables, live_count):
    prompts_here, span_len, heads_here, key_width = query_span.shape
    value_width = value_span.shape[3]
    cosine, sine_part, swap, rows, valid_rows = tables
    whole = pl.BlockSpec(memory_space=pltpu.SMEM)
    return pl.pallas_call(
        output_kernel,
        grid=(prompts_here,),
        in_specs=[
            whole,
            whole,
            pl.BlockSpec((None, span_len, heads_here, key_width), lambda b: (b, 0, 0, 0)),
            pl.BlockSpec((None, span_len, heads_here, key_width), lambda b: (b, 0, 0, 0)),
            pl.BlockSpec((None, span_len, heads_here, value_width), lambda b: (b, 0, 0, 0)),
            pl.BlockSpec((None, heads_here, key_width, value_width), lambda b: (b, 0, 0, 0)),
            pl.BlockSpec((None, span_len, key_width), lambda b: (b, 0, 0)),
            pl.BlockSpec((None, span_len, key_width), lambda b: (b, 0, 0)),
            pl.BlockSpec((key_width, key_width), lambda b: (0, 0)),
        ],
        out_specs=pl.BlockSpec(
            (None, span_len, heads_here, value_width), lambda b: (b, 0, 0, 0)
        ),
        out_shape=jax.ShapeDtypeStruct(value_span.shape, jnp.bfloat16),
    )(
        local_rates, live_count.astype(jnp.int32), query_span, key_span, value_span,
        prior_state, cosine, sine_part, swap,
    )


def per_device(
    query_span,
    key_span,
    value_span,
    prior_state,
    decay_rates,
    prompt_lengths,
    decode_inputs,
    w_query,
    w_key,
    w_value,
    w_gate,
    w_out,
):
    prompts_here, span_len, heads_here, key_width = query_span.shape
    value_width = value_span.shape[3]
    model_width = decode_inputs.shape[2]
    step_total = decode_inputs.shape[0]
    head_slots = lax.axis_size("heads")
    total_prompts = prompts_here * head_slots
    key_piece = w_query.shape[3]
    value_slice = w_value.shape[4]
    tp_index = lax.axis_index("tp")
    slot_index = lax.axis_index("heads")
    local_rates = lax.dynamic_slice_in_dim(decay_rates, tp_index * heads_here, heads_here)
    local_lengths = lax.dynamic_slice_in_dim(
        prompt_lengths, slot_index * prompts_here, prompts_here
    )
    span_start = span_len * ((local_lengths - 1) // span_len)
    live_count = local_lengths - span_start
    tables = prefill_tables(key_width, span_len, local_rates, span_start, live_count)
    offsets = jnp.arange(span_len)
    positions = (span_start[:, None] + offsets[None, :]).astype(jnp.float32)
    cosine, sine_part, swap = tables[:3]
    key_partner = jnp.einsum("bihk,kl->bihl", key_span, swap, preferred_element_type=jnp.float32)
    keys = (
        (key_span.astype(jnp.float32) * cosine[:, :, None, :] + key_partner * sine_part[:, :, None, :])
        * key_width ** (-0.5)
    ).astype(jnp.bfloat16)
    valid_rows = offsets[None, :] < live_count[:, None]
    remaining = (live_count[:, None] - 1 - offsets[None, :]).astype(jnp.float32)
    key_weight = jnp.where(
        valid_rows[:, :, None],
        jnp.exp(-local_rates[None, None, :] * jnp.maximum(remaining, 0.0)[:, :, None]),
        0.0,
    )
    weighted = (keys.astype(jnp.float32) * key_weight[..., None]).astype(jnp.bfloat16)
    update = jnp.einsum("bjhk,bjhv->bhkv", weighted, value_span, preferred_element_type=jnp.float32)
    kept_share = jnp.exp(-local_rates[None, :] * live_count[:, None].astype(jnp.float32))
    state_new = (kept_share[:, :, None, None] * prior_state.astype(jnp.float32) + update).astype(
        jnp.bfloat16
    )
    slots = head_slots
    flat_inputs = decode_inputs.reshape(step_total * total_prompts, model_width)
    query_part = jnp.dot(
        flat_inputs, w_query.reshape(model_width, key_piece), preferred_element_type=jnp.float32
    ).astype(jnp.bfloat16)
    key_part = jnp.dot(
        flat_inputs, w_key.reshape(model_width, key_piece), preferred_element_type=jnp.float32
    ).astype(jnp.bfloat16)
    value_dec = jnp.dot(
        flat_inputs,
        w_value.reshape(model_width, heads_here * value_slice),
        preferred_element_type=jnp.float32,
    ).astype(jnp.bfloat16)
    gate_values = lax.optimization_barrier(
        jnp.dot(
            flat_inputs,
            w_gate.reshape(model_width, heads_here * value_slice),
            preferred_element_type=jnp.float32,
        )
    )
    steps = jnp.arange(step_total)
    halfway = key_width // 2
    head_column = (slot_index * key_piece + jnp.arange(key_piece)) % key_width
    column_frequency = 10000.0 ** (-(head_column // 2).astype(jnp.float32) / halfway)
    dec_positions = (
        (prompt_lengths[None, :] + steps[:, None]).astype(jnp.float32).reshape(-1, 1)
    )
    dec_angles = dec_positions * column_frequency[None, :]
    dec_cosine = jnp.cos(dec_angles)
    dec_sine = jnp.where(head_column % 2 == 0, -1.0, 1.0)[None, :] * jnp.sin(dec_angles)
    lane = jnp.arange(key_piece)
    swap = (lane[:, None] == (lane[None, :] ^ 1)).astype(jnp.bfloat16)
    query_partner = jnp.dot(query_part, swap, preferred_element_type=jnp.float32)
    key_partner = jnp.dot(key_part, swap, preferred_element_type=jnp.float32)
    query_turned = (
        query_part.astype(jnp.float32) * dec_cosine + query_partner * dec_sine
    ).astype(jnp.bfloat16)
    key_turned = (
        (key_part.astype(jnp.float32) * dec_cosine + key_partner * dec_sine)
        * key_width ** (-0.5)
    ).astype(jnp.bfloat16)
    packed = jnp.concatenate([query_turned, key_turned, value_dec], -1)
    packed = packed.reshape(step_total, slots, prompts_here, -1).transpose(1, 0, 2, 3)
    arrived = lax.all_to_all(packed, "heads", 0, 0, tiled=True)
    query_rot = (
        arrived[..., :key_piece]
        .transpose(1, 2, 0, 3)
        .reshape(step_total, prompts_here, heads_here, key_width)
    )
    key_rot = (
        arrived[..., key_piece : 2 * key_piece]
        .transpose(1, 2, 0, 3)
        .reshape(step_total, prompts_here, heads_here, key_width)
    )
    value_own = (
        arrived[..., 2 * key_piece :]
        .reshape(slots, step_total, prompts_here, heads_here, value_slice)
        .transpose(1, 2, 3, 0, 4)
        .reshape(step_total, prompts_here, heads_here, value_width)
    )
    from_state = jnp.einsum(
        "tbhk,bhkv->tbhv", query_rot, state_new, preferred_element_type=jnp.float32
    )
    step_gap = (steps[:, None] - steps[None, :]).astype(jnp.float32)
    step_decay = jnp.where(
        step_gap[None] >= 0,
        jnp.exp(-local_rates[:, None, None] * jnp.maximum(step_gap, 0.0)[None]),
        0.0,
    )
    step_scores = jnp.einsum(
        "tbhk,ubhk->bhtu", query_rot, key_rot, preferred_element_type=jnp.float32
    )
    from_steps = jnp.einsum(
        "bhtu,ubhv->tbhv",
        step_scores * step_decay[None],
        value_own.astype(jnp.float32),
        precision=lax.Precision.HIGHEST,
    )
    state_decay = jnp.exp(-local_rates[None, :] * (steps[:, None] + 1).astype(jnp.float32))
    readout = state_decay[:, None, :, None] * from_state + from_steps
    read_mean = jnp.mean(readout, -1, keepdims=True)
    read_square = jnp.mean(readout * readout, -1, keepdims=True)
    normed = norm_with(readout, read_mean, read_square)
    normed = normed.reshape(step_total, prompts_here, heads_here, slots, value_slice)
    normed = normed.transpose(3, 0, 1, 2, 4)
    normed = lax.all_to_all(normed.astype(jnp.bfloat16), "heads", 0, 0, tiled=True)
    normed = normed.transpose(1, 0, 2, 3, 4).reshape(
        step_total, total_prompts, heads_here, value_slice
    ).astype(jnp.float32)
    gates_steps = gate_values.reshape(step_total, total_prompts, heads_here, value_slice)
    activated = (
        (jax.nn.silu(gates_steps) * normed)
        .astype(jnp.bfloat16)
        .reshape(-1, heads_here * value_slice)
    )
    partial_out = jnp.dot(
        activated,
        w_out.reshape(heads_here * value_slice, model_width),
        preferred_element_type=jnp.float32,
    )
    partial_out = partial_out.reshape(step_total, total_prompts, model_width)
    query_span, key_span, value_span, prior_state, partial_out = lax.optimization_barrier(
        (query_span, key_span, value_span, prior_state, partial_out)
    )
    prefill_out = prefill_output(
        query_span, key_span, value_span, prior_state, local_rates, tables, live_count
    )
    out_slots = head_slots * lax.axis_size("tp")
    column_block = model_width // out_slots
    pieces = partial_out.reshape(step_total, total_prompts, out_slots, column_block)
    pieces = lax.all_to_all(pieces.astype(jnp.bfloat16), ("heads", "tp"), 2, 2, tiled=True)
    decode_out = jnp.sum(pieces.astype(jnp.float32), 2).astype(jnp.bfloat16)
    return (prefill_out, decode_out)


def solution(mesh):
    placed = (
        P(("groups", "heads"), None, "tp", None),
        P(("groups", "heads"), None, "tp", None),
        P(("groups", "heads"), None, "tp", None),
        P(("groups", "heads"), "tp", None, None),
        P(),
        P("groups"),
        P(None, "groups", None),
        P(None, "tp", "heads", None),
        P(None, "tp", "heads", None),
        P(None, "tp", None, "heads", None),
        P(None, "tp", None, "heads", None),
        P("tp", None, "heads", None, None),
    )
    return jax.shard_map(
        per_device,
        mesh=mesh,
        in_specs=placed,
        out_specs=(P(("groups", "heads"), None, "tp", None), P(None, "groups", ("heads", "tp"))),
        check_vma=False,
    )
```
